128 devices in a mesh: req: 32 (over z, y, core), seq: 4 (over x).
Axes of the slice: x: 4, y: 4, z: 4, core: 2. Of those that a mesh axis runs over, the one named last changes fastest.
Arguments:
- hidden: bfloat16 [32, 4, 512, 2048], P('req', 'seq'), may hold values from -6 to 6
- w_in: bfloat16 [2048, 4384], P('req', 'seq'), may hold values from -0.125 to 0.125
- conv_weight: float32 [4, 2304], replicated, may hold values from -3 to 3
- conv_bias: float32 [2304], replicated, may hold values from -0.5 to 0.5
- dt_bias: float32 [32], replicated, may hold values from -5 to -2
- a_log: float32 [32], replicated, may hold values from -12 to 2
- d_skip: float32 [32], replicated, may hold values from 0.5 to 1.5
- norm_weight: float32 [2048], replicated, may hold values from 0.5 to 1.5
- lengths: int32 [32], replicated, may hold values from 4 to 512, as said below
- prompt_group: int32 [32], replicated, may hold values from 0 to 31, each once
Outputs:
- gated_out: bfloat16 [32, 4, 512, 2048], P('req', 'seq')
- final_states: float32 [32, 32, 64, 128], P(None, 'req', 'seq')
The draws below stay inside these ranges and needn't reach their ends.
Inputs may be any that keep to these rules, and one draw needn't show every extreme that they name: Every prompt has 4 * lengths[p] tokens; some prompt has exactly 512 a device. Group prompt_group[p] holds prompt p; each group holds one prompt.
All inputs are finite; a program needn't handle non-finite values.
Results may differ from the reference program's by a relative error of at most 0.0059.
Values may be sent and summed in bfloat16 or wider, within the bound.
No kernel may reach another device: no remote copies, remote signals or barrier semaphores. Data moves between devices by JAX's collectives and lax.ppermute only.
A program may use at most 128 MiB of HBM per device.

```python
import jax
import jax.numpy as jnp
from jax import lax

D = 2048
HEADS = 32
HDIM = 64
NSTATE = 128
KCONV = 4
QCAP = 512
STEP_ROWS = 256
DI = 2048
CONVDIM = 2304
E = 4384
GROUPS = 32
PROMPTS = 32
N_SEQ = 4


def draw_lengths(key, part):
    base_key = jax.random.fold_in(key, 11)
    values = jax.random.randint(jax.random.fold_in(base_key, 1), (PROMPTS,), KCONV, QCAP + 1)
    where_top = jax.random.randint(jax.random.fold_in(base_key, 2), (), 0, PROMPTS)
    return jnp.where(jnp.arange(PROMPTS) == where_top, QCAP, values).astype(jnp.int32)


def levels(own_key, shape, split, least, high):
    gain = 1.0
    for dim, shards_of in split:
        draws = jax.random.uniform(jax.random.fold_in(jax.random.fold_in(own_key, 6), dim), (shards_of,), jnp.float32, least / len(split), high / len(split))
        gain = gain * jnp.repeat(jnp.exp(draws), shape[dim] // shards_of).reshape((-1,) + (1,) * (len(shape) - 1 - dim))
    return gain


def gaussian(key, dims, scale, limit, split=(), kind=jnp.bfloat16):
    array = jax.random.normal(key, dims, jnp.float32) * scale
    if len(split) > 0:
        array = levels(key, dims, split, -0.22, 0.18) * array
    return jnp.clip(array, min=-limit, max=limit).astype(kind)


def setup_inputs(seed: int = 0) -> dict:
    keys = jax.random.split(jax.random.key(seed), 11)
    return {
        "hidden": gaussian(keys[0], (GROUPS, N_SEQ, QCAP, D), 1.0, 6.0, ((0, 32), (1, 4))),
        "w_in": gaussian(keys[1], (D, E), D ** -0.5, 0.125, ((0, 32), (1, 4))),
        "conv_weight": gaussian(keys[2], (KCONV, CONVDIM), KCONV ** -0.5, 3.0, (), jnp.float32),
        "conv_bias": jnp.clip(jax.random.uniform(keys[3], (CONVDIM,), jnp.float32, -0.5, 0.5), -0.5, 0.5),
        "dt_bias": jnp.clip(jax.random.uniform(keys[4], (HEADS,), jnp.float32, -5.0, -2.0), -5.0, -2.0),
        "a_log": jnp.clip(jax.random.uniform(keys[5], (HEADS,), jnp.float32, -12.0, 2.0), -12.0, 2.0),
        "d_skip": jnp.clip(jax.random.uniform(keys[6], (HEADS,), jnp.float32, 0.5, 1.5), 0.5, 1.5),
        "norm_weight": jnp.clip(1.0 + 0.1 * jax.random.normal(keys[7], (DI,), jnp.float32), 0.5, 1.5),
        "lengths": draw_lengths(jax.random.fold_in(keys[10], 71), 0),
        "prompt_group": jax.random.permutation(keys[9], PROMPTS).astype(jnp.int32),
    }


def block_step(state, pieces):
    inputs_x, b_rows, c_rows, step_dt, log_decay = pieces
    length = inputs_x.shape[0]
    heads = step_dt.shape[1]
    hdim = inputs_x.shape[1] // heads
    running = jnp.cumsum(log_decay, axis=0)
    gram = jnp.einsum('tn,un->tu', c_rows.astype(jnp.float32), b_rows.astype(jnp.float32))
    later = jnp.arange(length)[:, None] >= jnp.arange(length)[None, :]
    spread = running.T[:, :, None] - running.T[:, None, :]
    decay = jnp.where(later[None], jnp.exp(jnp.where(later[None], spread, 0.0)), 0.0)
    mixing = (gram[None] * decay * step_dt.T[:, None, :]).astype(jnp.bfloat16)
    heads_x = inputs_x.reshape(length, heads, hdim)
    inside = jnp.einsum('htu,uhp->thp', mixing.astype(jnp.float32), heads_x.astype(jnp.float32))
    carried = jnp.exp(running)[:, :, None] * jnp.einsum('tn,hpn->thp', c_rows.astype(jnp.float32), state, precision=lax.Precision.HIGHEST)
    final_log = running[-1]
    weighting = jnp.exp(final_log[None, :] - running) * step_dt
    weighted = (heads_x.astype(jnp.float32) * weighting[:, :, None]).astype(jnp.bfloat16).reshape(length, heads * hdim)
    contrib = jnp.einsum('ud,un->dn', weighted.astype(jnp.float32), b_rows.astype(jnp.float32)).reshape(heads, hdim, -1)
    new_state = jnp.exp(final_log)[:, None, None] * state + contrib
    return (new_state, (inside + carried).reshape(length, heads * hdim))

def one_group(hidden_group, qlen, w_in, conv_weight, conv_bias, dt_bias, a_log, d_skip, norm_weight):
    total = N_SEQ * QCAP
    tok_rows = hidden_group.reshape(total, D)
    projected = jnp.dot(tok_rows, w_in, preferred_element_type=jnp.float32).astype(jnp.bfloat16)
    gate_z = projected[:, :DI]
    conv_in = projected[:, DI:DI + CONVDIM]
    dt_raw = projected[:, DI + CONVDIM:]
    slot = jnp.arange(total, dtype=jnp.int32)
    segment = slot // QCAP
    column = slot % QCAP
    filled = column < qlen
    position = segment * qlen + column
    accum = jnp.zeros((total, CONVDIM), jnp.float32) + conv_bias[None, :]
    for tap_index in range(KCONV):
        source = position - (KCONV - 1) + tap_index
        usable = (source >= 0) & filled
        safe = jnp.maximum(source, 0)
        row_index = (safe // qlen * QCAP + safe % qlen).astype(jnp.int32)
        row_index = jnp.clip(row_index, 0, total - 1).astype(jnp.int32)
        taken = jnp.take(conv_in, row_index, axis=0).astype(jnp.float32)
        accum = accum + conv_weight[tap_index][None, :] * jnp.where(usable[:, None], taken, 0.0)
    conv_act = jax.nn.silu(accum).astype(jnp.bfloat16)
    inputs_x = conv_act[:, :DI]
    b_rows = conv_act[:, DI:DI + NSTATE]
    c_rows = conv_act[:, DI + NSTATE:]
    step_dt = jnp.where(filled[:, None], jax.nn.softplus(dt_raw.astype(jnp.float32) + dt_bias[None, :]), 0.0)
    log_decay = step_dt * (-jnp.exp(a_log))[None, :]
    count = total // STEP_ROWS
    pieces = (inputs_x.reshape(count, STEP_ROWS, DI), b_rows.reshape(count, STEP_ROWS, NSTATE), c_rows.reshape(count, STEP_ROWS, NSTATE), step_dt.reshape(count, STEP_ROWS, HEADS), log_decay.reshape(count, STEP_ROWS, HEADS))
    start_state = jnp.zeros((HEADS, HDIM, NSTATE), jnp.float32)
    end_state, outputs = lax.scan(block_step, start_state, pieces)
    heads_y = outputs.reshape(total, HEADS, HDIM) + d_skip[None, :, None] * inputs_x.astype(jnp.float32).reshape(total, HEADS, HDIM)
    gated = heads_y.reshape(total, DI) * jax.nn.silu(gate_z.astype(jnp.float32))
    scale = lax.rsqrt(lax.optimization_barrier(jnp.mean(gated * gated, axis=1, keepdims=True)) + 1e-05)
    normed = jnp.where(filled[:, None], gated * scale * norm_weight[None, :], 0.0)
    return (normed.astype(jnp.bfloat16).reshape(N_SEQ, QCAP, DI), end_state)

def reference(hidden, w_in, conv_weight, conv_bias, dt_bias, a_log, d_skip, norm_weight, lengths, prompt_group):
    group_ids = jnp.arange(GROUPS, dtype=jnp.int32)
    qlens = lax.optimization_barrier(jnp.sum(jnp.where(prompt_group[None, :] == group_ids[:, None], lengths[None, :], 0), axis=1)).astype(jnp.int32)

    def apply(inputs):
        return one_group(inputs[0], inputs[1], w_in, conv_weight, conv_bias, dt_bias, a_log, d_skip, norm_weight)
    gated_out, group_states = lax.map(apply, (hidden, qlens))
    final_states = jnp.take(group_states, prompt_group.astype(jnp.int32), axis=0)
    return (gated_out, final_states)
```

```python
import jax
import jax.numpy as jnp
from jax import lax
from jax.sharding import PartitionSpec as P

BLOCK = 256


def shifted(block, axis, distance):
    devices = range(lax.axis_size(axis))
    route = [(i - distance, i) for i in devices if i - distance in devices]
    return lax.ppermute(block, axis, route)


def block_step(state, pieces):
    inputs_x, b_rows, c_rows, step_dt, log_decay = pieces
    length = inputs_x.shape[0]
    heads = step_dt.shape[1]
    hdim = inputs_x.shape[1] // heads
    running = jnp.cumsum(log_decay, axis=0)
    gram = jnp.einsum("tn,un->tu", c_rows, b_rows, preferred_element_type=jnp.float32)
    later = jnp.arange(length)[:, None] >= jnp.arange(length)[None, :]
    spread = running.T[:, :, None] - running.T[:, None, :]
    decay = jnp.where(later[None], jnp.exp(jnp.where(later[None], spread, 0.0)), 0.0)
    mixing = (gram[None] * decay * step_dt.T[:, None, :]).astype(jnp.bfloat16)
    heads_x = inputs_x.reshape(length, heads, hdim)
    inside = jnp.einsum("htu,uhp->thp", mixing, heads_x, preferred_element_type=jnp.float32)
    carried = jnp.exp(running)[:, :, None] * jnp.einsum(
        "tn,hpn->thp", c_rows.astype(jnp.float32), state, precision=lax.Precision.HIGHEST
    )
    final_log = running[-1]
    weighting = jnp.exp(final_log[None, :] - running) * step_dt
    weighted = (
        (heads_x.astype(jnp.float32) * weighting[:, :, None])
        .astype(jnp.bfloat16)
        .reshape(length, heads * hdim)
    )
    contrib = jnp.einsum("ud,un->dn", weighted, b_rows, preferred_element_type=jnp.float32).reshape(
        heads, hdim, -1
    )
    new_state = jnp.exp(final_log)[:, None, None] * state + contrib
    return (new_state, (inside + carried).reshape(length, heads * hdim))


def local(
    hidden, w_in, conv_weight, conv_bias, dt_bias, a_log, d_skip, norm_weight, lengths, prompt_group
):
    tok_rows = hidden[0, 0]
    slots = tok_rows.shape[0]
    inner = norm_weight.shape[0]
    heads = dt_bias.shape[0]
    hdim = inner // heads
    nstate = (conv_bias.shape[0] - inner) // 2
    convdim = conv_bias.shape[0]
    taps = conv_weight.shape[0]
    seq_count = lax.axis_size("seq")
    my_group = lax.axis_index("req")
    my_block = lax.axis_index("seq")
    qlen = jnp.sum(jnp.where(prompt_group == my_group, lengths, 0))
    filled = jnp.arange(slots, dtype=jnp.int32) < qlen
    wide_rows = lax.all_gather(w_in, "seq", axis=1, tiled=True)
    projected = jnp.dot(
        tok_rows,
        lax.all_gather(wide_rows, "req", axis=0, tiled=True),
        preferred_element_type=jnp.float32,
    ).astype(jnp.bfloat16)
    gate_z = projected[:, :inner]
    conv_in = projected[:, inner : inner + convdim]
    dt_raw = projected[:, inner + convdim :]
    edge_rows = lax.dynamic_slice_in_dim(conv_in, qlen - (taps - 1), taps - 1, 0)
    prev_edge = shifted(edge_rows, "seq", 1)
    extended = jnp.concatenate([prev_edge, conv_in], axis=0)
    accum = jnp.zeros((slots, convdim), jnp.float32) + conv_bias[None, :]
    for tap_index in range(taps):
        accum = accum + conv_weight[tap_index][None, :] * extended[
            tap_index : tap_index + slots
        ].astype(jnp.float32)
    conv_act = jax.nn.silu(accum).astype(jnp.bfloat16)
    inputs_x = conv_act[:, :inner]
    b_rows = conv_act[:, inner : inner + nstate]
    c_rows = conv_act[:, inner + nstate :]
    step_dt = jnp.where(
        filled[:, None], jax.nn.softplus(dt_raw.astype(jnp.float32) + dt_bias[None, :]), 0.0
    )
    log_decay = step_dt * (-jnp.exp(a_log))[None, :]
    through = jnp.cumsum(log_decay, axis=0)
    block_total = through[-1]
    block_rows = min(BLOCK, slots)
    count = slots // block_rows
    pieces = (
        inputs_x.reshape(count, block_rows, inner),
        b_rows.reshape(count, block_rows, nstate),
        c_rows.reshape(count, block_rows, nstate),
        step_dt.reshape(count, block_rows, heads),
        log_decay.reshape(count, block_rows, heads),
    )
    zero_state = jnp.zeros((heads, hdim, nstate), jnp.float32)
    local_end = zero_state
    outs = []
    for index in range(count):
        local_end, out = block_step(local_end, tuple(piece[index] for piece in pieces))
        outs.append(out)
    outputs = jnp.concatenate(outs, axis=0)
    decays_all = lax.all_gather(block_total[None, :], "seq", axis=0, tiled=True)
    after_mine = jnp.sum(
        jnp.where(jnp.arange(seq_count)[:, None] > my_block, decays_all, 0.0), axis=0
    )
    entering = zero_state
    for turn in range(seq_count - 1):
        entering = shifted(jnp.exp(block_total)[:, None, None] * entering + local_end, "seq", 1)
    incoming = jnp.exp(through)[:, :, None] * jnp.einsum(
        "tn,hpn->thp", c_rows.astype(jnp.float32), entering, precision=lax.Precision.HIGHEST
    )
    heads_y = (
        outputs.reshape(slots, heads, hdim)
        + incoming
        + d_skip[None, :, None] * inputs_x.astype(jnp.float32).reshape(slots, heads, hdim)
    )
    gated = heads_y.reshape(slots, inner) * jax.nn.silu(gate_z.astype(jnp.float32))
    scale = lax.rsqrt(jnp.mean(gated * gated, axis=1, keepdims=True) + 1e-05)
    normed = jnp.where(filled[:, None], gated * scale * norm_weight[None, :], 0.0)
    gated_out = normed.astype(jnp.bfloat16).reshape(1, 1, slots, inner)
    decayed_end = jnp.exp(after_mine)[:, None, None] * local_end
    share = lax.psum_scatter(decayed_end, "seq", scatter_dimension=1, tiled=True)
    moved = lax.all_to_all(share[None], "req", split_axis=1, concat_axis=0, tiled=True)
    final_states = jnp.take(moved, prompt_group, axis=0)
    return (gated_out, final_states)


def solution(mesh):
    in_specs = (
        P("req", "seq", None, None),
        P("req", "seq"),
        P(),
        P(),
        P(),
        P(),
        P(),
        P(),
        P(),
        P(),
    )
    out_specs = (P("req", "seq", None, None), P(None, "req", "seq", None))
    return jax.shard_map(local, mesh=mesh, in_specs=in_specs, out_specs=out_specs, check_vma=False)
```

```python
import jax
import jax.numpy as jnp
from jax import lax
from jax.sharding import PartitionSpec as P

BLOCK = 256


def shifted(block, axis, distance):
    devices = range(lax.axis_size(axis))
    route = [(i - distance, i) for i in devices if i - distance in devices]
    return lax.ppermute(block, axis, route)


def block_step(state, pieces):
    inputs_x, b_rows, c_rows, step_dt, log_decay = pieces
    length = inputs_x.shape[0]
    heads = step_dt.shape[1]
    hdim = inputs_x.shape[1] // heads
    running = jnp.cumsum(log_decay, axis=0)
    gram = jnp.einsum("tn,un->tu", c_rows, b_rows, preferred_element_type=jnp.float32)
    later = jnp.arange(length)[:, None] >= jnp.arange(length)[None, :]
    spread = running.T[:, :, None] - running.T[:, None, :]
    decay = jnp.where(later[None], jnp.exp(jnp.where(later[None], spread, 0.0)), 0.0)
    mixing = (gram[None] * decay * step_dt.T[:, None, :]).astype(jnp.bfloat16)
    heads_x = inputs_x.reshape(length, heads, hdim)
    inside = jnp.einsum("htu,uhp->thp", mixing, heads_x, preferred_element_type=jnp.float32)
    carried = jnp.exp(running)[:, :, None] * jnp.einsum(
        "tn,hpn->thp", c_rows.astype(jnp.float32), state, precision=lax.Precision.HIGHEST
    )
    final_log = running[-1]
    weighting = jnp.exp(final_log[None, :] - running) * step_dt
    weighted = (
        (heads_x.astype(jnp.float32) * weighting[:, :, None])
        .astype(jnp.bfloat16)
        .reshape(length, heads * hdim)
    )
    contrib = jnp.einsum("ud,un->dn", weighted, b_rows, preferred_element_type=jnp.float32).reshape(
        heads, hdim, -1
    )
    new_state = jnp.exp(final_log)[:, None, None] * state + contrib
    return (new_state, (inside + carried).reshape(length, heads * hdim))


def local(
    hidden, w_in, conv_weight, conv_bias, dt_bias, a_log, d_skip, norm_weight, lengths, prompt_group
):
    tok_rows = hidden[0, 0]
    slots = tok_rows.shape[0]
    inner = norm_weight.shape[0]
    heads = dt_bias.shape[0]
    hdim = inner // heads
    nstate = (conv_bias.shape[0] - inner) // 2
    convdim = conv_bias.shape[0]
    taps = conv_weight.shape[0]
    seq_count = lax.axis_size("seq")
    my_group = lax.axis_index("req")
    my_block = lax.axis_index("seq")
    qlen = jnp.sum(jnp.where(prompt_group == my_group, lengths, 0))
    filled = jnp.arange(slots, dtype=jnp.int32) < qlen
    wide_rows = lax.all_gather(w_in, "seq", axis=1, tiled=True)
    projected = jnp.dot(
        tok_rows,
        lax.all_gather(wide_rows, "req", axis=0, tiled=True),
        preferred_element_type=jnp.float32,
    ).astype(jnp.bfloat16)
    gate_z = projected[:, :inner]
    conv_in = projected[:, inner : inner + convdim]
    dt_raw = projected[:, inner + convdim :]
    edge_rows = lax.dynamic_slice_in_dim(conv_in, qlen - (taps - 1), taps - 1, 0)
    prev_edge = shifted(edge_rows, "seq", 1)
    extended = jnp.concatenate([prev_edge, conv_in], axis=0)
    accum = jnp.zeros((slots, convdim), jnp.float32) + conv_bias[None, :]
    for tap_index in range(taps):
        accum = accum + conv_weight[tap_index][None, :] * extended[
            tap_index : tap_index + slots
        ].astype(jnp.float32)
    conv_act = jax.nn.silu(accum).astype(jnp.bfloat16)
    inputs_x = conv_act[:, :inner]
    b_rows = conv_act[:, inner : inner + nstate]
    c_rows = conv_act[:, inner + nstate :]
    step_dt = jnp.where(
        filled[:, None], jax.nn.softplus(dt_raw.astype(jnp.float32) + dt_bias[None, :]), 0.0
    )
    log_decay = step_dt * (-jnp.exp(a_log))[None, :]
    through = jnp.cumsum(log_decay, axis=0)
    block_total = through[-1]
    block_rows = min(BLOCK, slots)
    count = slots // block_rows
    pieces = (
        inputs_x.reshape(count, block_rows, inner),
        b_rows.reshape(count, block_rows, nstate),
        c_rows.reshape(count, block_rows, nstate),
        step_dt.reshape(count, block_rows, heads),
        log_decay.reshape(count, block_rows, heads),
    )
    zero_state = jnp.zeros((heads, hdim, nstate), jnp.float32)
    local_end = zero_state
    outs = []
    for index in range(count):
        local_end, out = block_step(local_end, tuple(piece[index] for piece in pieces))
        outs.append(out)
    outputs = jnp.concatenate(outs, axis=0)
    packed = jnp.concatenate(
        [local_end.reshape(heads, hdim * nstate), jnp.broadcast_to(block_total[:, None], (heads, 128))],
        axis=1,
    )
    gathered = lax.all_gather(packed, "seq", axis=0, tiled=False)
    ends = gathered[:, :, : hdim * nstate].reshape(seq_count, heads, hdim, nstate)
    totals = gathered[:, :, hdim * nstate]
    entering = zero_state
    for turn in range(seq_count - 1):
        stepped = jnp.exp(totals[turn])[:, None, None] * entering + ends[turn]
        entering = jnp.where(turn < my_block, stepped, entering)
    incoming = jnp.exp(through)[:, :, None] * jnp.einsum(
        "tn,hpn->thp", c_rows.astype(jnp.float32), entering, precision=lax.Precision.HIGHEST
    )
    heads_y = (
        outputs.reshape(slots, heads, hdim)
        + incoming
        + d_skip[None, :, None] * inputs_x.astype(jnp.float32).reshape(slots, heads, hdim)
    )
    gated = heads_y.reshape(slots, inner) * jax.nn.silu(gate_z.astype(jnp.float32))
    scale = lax.rsqrt(jnp.mean(gated * gated, axis=1, keepdims=True) + 1e-05)
    normed = jnp.where(filled[:, None], gated * scale * norm_weight[None, :], 0.0)
    gated_out = normed.astype(jnp.bfloat16).reshape(1, 1, slots, inner)
    later_mask = jnp.arange(seq_count)[None, :] > jnp.arange(seq_count)[:, None]
    after = jnp.sum(jnp.where(later_mask[:, :, None], totals[None, :, :], 0.0), axis=1)
    piece = hdim // seq_count
    own_ends = lax.dynamic_slice_in_dim(ends, my_block * piece, piece, axis=2)
    share = jnp.sum(jnp.exp(after)[:, :, None, None] * own_ends, axis=0)
    moved = lax.all_to_all(share[None], "req", split_axis=1, concat_axis=0, tiled=True)
    final_states = jnp.take(moved, prompt_group, axis=0)
    return (gated_out, final_states)


def solution(mesh):
    in_specs = (
        P("req", "seq", None, None),
        P("req", "seq"),
        P(),
        P(),
        P(),
        P(),
        P(),
        P(),
        P(),
        P(),
    )
    out_specs = (P("req", "seq", None, None), P(None, "req", "seq", None))
    return jax.shard_map(local, mesh=mesh, in_specs=in_specs, out_specs=out_specs, check_vma=False)
```

```python
import jax
import jax.numpy as jnp
from jax import lax
from jax.sharding import Mesh, PartitionSpec as P

BLOCK = 256


def shifted(block, axis, distance):
    devices = range(lax.axis_size(axis))
    route = [(i - distance, i) for i in devices if i - distance in devices]
    return lax.ppermute(block, axis, route)


def block_step(state, pieces):
    inputs_x, b_rows, c_rows, step_dt, log_decay = pieces
    length = inputs_x.shape[0]
    heads = step_dt.shape[1]
    hdim = inputs_x.shape[1] // heads
    running = jnp.cumsum(log_decay, axis=0)
    gram = jnp.einsum("tn,un->tu", c_rows, b_rows, preferred_element_type=jnp.float32)
    later = jnp.arange(length)[:, None] >= jnp.arange(length)[None, :]
    spread = running.T[:, :, None] - running.T[:, None, :]
    decay = jnp.where(later[None], jnp.exp(jnp.where(later[None], spread, 0.0)), 0.0)
    mixing = (gram[None] * decay * step_dt.T[:, None, :]).astype(jnp.bfloat16)
    heads_x = inputs_x.reshape(length, heads, hdim)
    inside = jnp.einsum("htu,uhp->thp", mixing, heads_x, preferred_element_type=jnp.float32)
    carried = jnp.exp(running)[:, :, None] * jnp.einsum(
        "tn,hpn->thp", c_rows.astype(jnp.float32), state, precision=lax.Precision.HIGHEST
    )
    final_log = running[-1]
    weighting = jnp.exp(final_log[None, :] - running) * step_dt
    weighted = (
        (heads_x.astype(jnp.float32) * weighting[:, :, None])
        .astype(jnp.bfloat16)
        .reshape(length, heads * hdim)
    )
    contrib = jnp.einsum("ud,un->dn", weighted, b_rows, preferred_element_type=jnp.float32).reshape(
        heads, hdim, -1
    )
    new_state = jnp.exp(final_log)[:, None, None] * state + contrib
    return (new_state, (inside + carried).reshape(length, heads * hdim))


def local(
    hidden, w_in, conv_weight, conv_bias, dt_bias, a_log, d_skip, norm_weight, lengths, prompt_group
):
    tok_rows = hidden[0, 0]
    slots = tok_rows.shape[0]
    inner = norm_weight.shape[0]
    heads = dt_bias.shape[0]
    hdim = inner // heads
    nstate = (conv_bias.shape[0] - inner) // 2
    convdim = conv_bias.shape[0]
    taps = conv_weight.shape[0]
    seq_count = lax.axis_size("seq")
    pair = lax.axis_index("core")
    my_group = lax.axis_index("rq") * 2 + pair
    my_block = lax.axis_index("seq")
    qlen = jnp.sum(jnp.where(prompt_group == my_group, lengths, 0))
    filled = jnp.arange(slots, dtype=jnp.int32) < qlen
    half = w_in.shape[1] // 2
    pair_rows = lax.all_gather(w_in, "core", axis=0, tiled=True)
    my_cols = lax.dynamic_slice_in_dim(pair_rows, pair * half, half, axis=1)
    weights = lax.all_gather(my_cols, ("seq", "rq"), axis=0, tiled=False)
    weights = weights.reshape(seq_count, -1, half)
    swap = [(0, 1), (1, 0)]
    partner_rows = lax.ppermute(tok_rows, "core", swap)
    for_partner = jnp.einsum(
        "tk,skn->tsn", partner_rows, weights, preferred_element_type=jnp.float32
    ).astype(jnp.bfloat16)
    from_partner = lax.ppermute(for_partner, "core", swap)
    for_me = jnp.einsum(
        "tk,skn->tsn", tok_rows, weights, preferred_element_type=jnp.float32
    ).astype(jnp.bfloat16)
    first = jnp.where(pair == 0, for_me, from_partner)
    second = jnp.where(pair == 0, from_partner, for_me)
    projected = jnp.stack([first, second], axis=2).reshape(slots, -1)
    gate_z = projected[:, :inner]
    conv_in = projected[:, inner : inner + convdim]
    dt_raw = projected[:, inner + convdim :]
    edge_rows = lax.dynamic_slice_in_dim(conv_in, qlen - (taps - 1), taps - 1, 0)
    prev_edge = shifted(edge_rows, "seq", 1)
    extended = jnp.concatenate([prev_edge, conv_in], axis=0)
    accum = jnp.zeros((slots, convdim), jnp.float32) + conv_bias[None, :]
    for tap_index in range(taps):
        accum = accum + conv_weight[tap_index][None, :] * extended[
            tap_index : tap_index + slots
        ].astype(jnp.float32)
    conv_act = jax.nn.silu(accum).astype(jnp.bfloat16)
    inputs_x = conv_act[:, :inner]
    b_rows = conv_act[:, inner : inner + nstate]
    c_rows = conv_act[:, inner + nstate :]
    step_dt = jnp.where(
        filled[:, None], jax.nn.softplus(dt_raw.astype(jnp.float32) + dt_bias[None, :]), 0.0
    )
    log_decay = step_dt * (-jnp.exp(a_log))[None, :]
    through = jnp.cumsum(log_decay, axis=0)
    block_total = through[-1]
    block_rows = min(BLOCK, slots)
    count = slots // block_rows
    pieces = (
        inputs_x.reshape(count, block_rows, inner),
        b_rows.reshape(count, block_rows, nstate),
        c_rows.reshape(count, block_rows, nstate),
        step_dt.reshape(count, block_rows, heads),
        log_decay.reshape(count, block_rows, heads),
    )
    zero_state = jnp.zeros((heads, hdim, nstate), jnp.float32)
    local_end = zero_state
    outs = []
    for index in range(count):
        local_end, out = block_step(local_end, tuple(piece[index] for piece in pieces))
        outs.append(out)
    outputs = jnp.concatenate(outs, axis=0)
    packed = jnp.concatenate(
        [local_end.reshape(heads, hdim * nstate), jnp.broadcast_to(block_total[:, None], (heads, 128))],
        axis=1,
    )
    gathered = lax.all_gather(packed, "seq", axis=0, tiled=False)
    ends = gathered[:, :, : hdim * nstate].reshape(seq_count, heads, hdim, nstate)
    totals = gathered[:, :, hdim * nstate]
    entering = zero_state
    for turn in range(seq_count - 1):
        stepped = jnp.exp(totals[turn])[:, None, None] * entering + ends[turn]
        entering = jnp.where(turn < my_block, stepped, entering)
    incoming = jnp.exp(through)[:, :, None] * jnp.einsum(
        "tn,hpn->thp", c_rows.astype(jnp.float32), entering, precision=lax.Precision.HIGHEST
    )
    heads_y = (
        outputs.reshape(slots, heads, hdim)
        + incoming
        + d_skip[None, :, None] * inputs_x.astype(jnp.float32).reshape(slots, heads, hdim)
    )
    gated = heads_y.reshape(slots, inner) * jax.nn.silu(gate_z.astype(jnp.float32))
    scale = lax.rsqrt(jnp.mean(gated * gated, axis=1, keepdims=True) + 1e-05)
    normed = jnp.where(filled[:, None], gated * scale * norm_weight[None, :], 0.0)
    gated_out = normed.astype(jnp.bfloat16).reshape(1, 1, slots, inner)
    later_mask = jnp.arange(seq_count)[None, :] > jnp.arange(seq_count)[:, None]
    after = jnp.sum(jnp.where(later_mask[:, :, None], totals[None, :, :], 0.0), axis=1)
    piece = hdim // seq_count
    own_ends = lax.dynamic_slice_in_dim(ends, my_block * piece, piece, axis=2)
    share = jnp.sum(jnp.exp(after)[:, :, None, None] * own_ends, axis=0)
    moved = lax.all_to_all(share[None], ("rq", "core"), split_axis=1, concat_axis=0, tiled=True)
    final_states = jnp.take(moved, prompt_group, axis=0)
    return (gated_out, final_states)


def solution(mesh):
    groups, blocks = mesh.devices.shape
    split = Mesh(mesh.devices.reshape(groups // 2, 2, blocks), ("rq", "core", "seq"))
    req = ("rq", "core")
    in_specs = (
        P(req, "seq", None, None),
        P(req, "seq"),
        P(),
        P(),
        P(),
        P(),
        P(),
        P(),
        P(),
        P(),
    )
    out_specs = (P(req, "seq", None, None), P(None, req, "seq", None))
    return jax.shard_map(local, mesh=split, in_specs=in_specs, out_specs=out_specs, check_vma=False)
```

```python
import jax
import jax.numpy as jnp
from jax import lax
from jax.sharding import PartitionSpec as P

BLOCK = 256


def shifted(block, axis, distance):
    devices = range(lax.axis_size(axis))
    route = [(i - distance, i) for i in devices if i - distance in devices]
    return lax.ppermute(block, axis, route)


def block_step(state, pieces):
    inputs_x, b_rows, c_rows, step_dt, log_decay = pieces
    length = inputs_x.shape[0]
    heads = step_dt.shape[1]
    hdim = inputs_x.shape[1] // heads
    running = jnp.cumsum(log_decay, axis=0)
    gram = jnp.einsum("tn,un->tu", c_rows, b_rows, preferred_element_type=jnp.float32)
    later = jnp.arange(length)[:, None] >= jnp.arange(length)[None, :]
    spread = running.T[:, :, None] - running.T[:, None, :]
    decay = jnp.where(later[None], jnp.exp(jnp.where(later[None], spread, 0.0)), 0.0)
    mixing = (gram[None] * decay * step_dt.T[:, None, :]).astype(jnp.bfloat16)
    heads_x = inputs_x.reshape(length, heads, hdim)
    inside = jnp.einsum("htu,uhp->thp", mixing, heads_x, preferred_element_type=jnp.float32)
    carried = jnp.exp(running)[:, :, None] * jnp.einsum(
        "tn,hpn->thp", c_rows.astype(jnp.float32), state, precision=lax.Precision.HIGHEST
    )
    final_log = running[-1]
    weighting = jnp.exp(final_log[None, :] - running) * step_dt
    weighted = (
        (heads_x.astype(jnp.float32) * weighting[:, :, None])
        .astype(jnp.bfloat16)
        .reshape(length, heads * hdim)
    )
    contrib = jnp.einsum("ud,un->dn", weighted, b_rows, preferred_element_type=jnp.float32).reshape(
        heads, hdim, -1
    )
    new_state = jnp.exp(final_log)[:, None, None] * state + contrib
    return (new_state, (inside + carried).reshape(length, heads * hdim))


def local(
    hidden, w_in, conv_weight, conv_bias, dt_bias, a_log, d_skip, norm_weight, lengths, prompt_group
):
    tok_rows = hidden[0, 0]
    slots = tok_rows.shape[0]
    inner = norm_weight.shape[0]
    heads = dt_bias.shape[0]
    hdim = inner // heads
    nstate = (conv_bias.shape[0] - inner) // 2
    convdim = conv_bias.shape[0]
    taps = conv_weight.shape[0]
    seq_count = lax.axis_size("seq")
    my_group = lax.axis_index("req")
    my_block = lax.axis_index("seq")
    qlen = jnp.sum(jnp.where(prompt_group == my_group, lengths, 0))
    filled = jnp.arange(slots, dtype=jnp.int32) < qlen
    wide_rows = lax.all_gather(w_in, "seq", axis=1, tiled=True)
    ssm_weights = lax.all_gather(wide_rows[:, inner:], "req", axis=0, tiled=True)
    ssm_weights, gate_rows = lax.optimization_barrier((ssm_weights, wide_rows[:, :inner]))
    gate_weights = lax.all_gather(gate_rows, "req", axis=0, tiled=True)
    ssm_part = jnp.dot(tok_rows, ssm_weights, preferred_element_type=jnp.float32).astype(jnp.bfloat16)
    conv_in = ssm_part[:, :convdim]
    dt_raw = ssm_part[:, convdim:]
    edge_rows = lax.dynamic_slice_in_dim(conv_in, qlen - (taps - 1), taps - 1, 0)
    prev_edge = shifted(edge_rows, "seq", 1)
    extended = jnp.concatenate([prev_edge, conv_in], axis=0)
    accum = jnp.zeros((slots, convdim), jnp.float32) + conv_bias[None, :]
    for tap_index in range(taps):
        accum = accum + conv_weight[tap_index][None, :] * extended[
            tap_index : tap_index + slots
        ].astype(jnp.float32)
    conv_act = jax.nn.silu(accum).astype(jnp.bfloat16)
    inputs_x = conv_act[:, :inner]
    b_rows = conv_act[:, inner : inner + nstate]
    c_rows = conv_act[:, inner + nstate :]
    step_dt = jnp.where(
        filled[:, None], jax.nn.softplus(dt_raw.astype(jnp.float32) + dt_bias[None, :]), 0.0
    )
    log_decay = step_dt * (-jnp.exp(a_log))[None, :]
    through = jnp.cumsum(log_decay, axis=0)
    block_total = through[-1]
    block_rows = min(BLOCK, slots)
    count = slots // block_rows
    pieces = (
        inputs_x.reshape(count, block_rows, inner),
        b_rows.reshape(count, block_rows, nstate),
        c_rows.reshape(count, block_rows, nstate),
        step_dt.reshape(count, block_rows, heads),
        log_decay.reshape(count, block_rows, heads),
    )
    zero_state = jnp.zeros((heads, hdim, nstate), jnp.float32)
    local_end = zero_state
    outs = []
    for index in range(count):
        local_end, out = block_step(local_end, tuple(piece[index] for piece in pieces))
        outs.append(out)
    outputs = jnp.concatenate(outs, axis=0)
    packed = jnp.concatenate(
        [local_end.reshape(heads, hdim * nstate), jnp.broadcast_to(block_total[:, None], (heads, 128))],
        axis=1,
    )
    packed, gate_weights = lax.optimization_barrier((packed, gate_weights))
    gathered = lax.all_gather(packed, "seq", axis=0, tiled=False)
    gate_z = jnp.dot(tok_rows, gate_weights, preferred_element_type=jnp.float32).astype(jnp.bfloat16)
    ends = gathered[:, :, : hdim * nstate].reshape(seq_count, heads, hdim, nstate)
    totals = gathered[:, :, hdim * nstate]
    entering = zero_state
    for turn in range(seq_count - 1):
        stepped = jnp.exp(totals[turn])[:, None, None] * entering + ends[turn]
        entering = jnp.where(turn < my_block, stepped, entering)
    incoming = jnp.exp(through)[:, :, None] * jnp.einsum(
        "tn,hpn->thp", c_rows.astype(jnp.float32), entering, precision=lax.Precision.HIGHEST
    )
    heads_y = (
        outputs.reshape(slots, heads, hdim)
        + incoming
        + d_skip[None, :, None] * inputs_x.astype(jnp.float32).reshape(slots, heads, hdim)
    )
    gated = heads_y.reshape(slots, inner) * jax.nn.silu(gate_z.astype(jnp.float32))
    scale = lax.rsqrt(jnp.mean(gated * gated, axis=1, keepdims=True) + 1e-05)
    normed = jnp.where(filled[:, None], gated * scale * norm_weight[None, :], 0.0)
    gated_out = normed.astype(jnp.bfloat16).reshape(1, 1, slots, inner)
    later_mask = jnp.arange(seq_count)[None, :] > jnp.arange(seq_count)[:, None]
    after = jnp.sum(jnp.where(later_mask[:, :, None], totals[None, :, :], 0.0), axis=1)
    piece = hdim // seq_count
    own_ends = lax.dynamic_slice_in_dim(ends, my_block * piece, piece, axis=2)
    share = jnp.sum(jnp.exp(after)[:, :, None, None] * own_ends, axis=0)
    moved = lax.all_to_all(share[None], "req", split_axis=1, concat_axis=0, tiled=True)
    final_states = jnp.take(moved, prompt_group, axis=0)
    return (gated_out, final_states)


def solution(mesh):
    in_specs = (
        P("req", "seq", None, None),
        P("req", "seq"),
        P(),
        P(),
        P(),
        P(),
        P(),
        P(),
        P(),
        P(),
    )
    out_specs = (P("req", "seq", None, None), P(None, "req", "seq", None))
    return jax.shard_map(local, mesh=mesh, in_specs=in_specs, out_specs=out_specs, check_vma=False)
```

```python
import jax
import jax.numpy as jnp
from jax import lax
from jax.sharding import PartitionSpec as P

BLOCK = 256


def shifted(block, axis, distance):
    devices = range(lax.axis_size(axis))
    route = [(i - distance, i) for i in devices if i - distance in devices]
    return lax.ppermute(block, axis, route)


def block_step(state, pieces):
    inputs_x, b_rows, c_rows, step_dt, log_decay = pieces
    length = inputs_x.shape[0]
    heads = step_dt.shape[1]
    hdim = inputs_x.shape[1] // heads
    running = jnp.cumsum(log_decay, axis=0)
    gram = jnp.einsum("tn,un->tu", c_rows, b_rows, preferred_element_type=jnp.float32)
    later = jnp.arange(length)[:, None] >= jnp.arange(length)[None, :]
    spread = running.T[:, :, None] - running.T[:, None, :]
    decay = jnp.where(later[None], jnp.exp(jnp.where(later[None], spread, 0.0)), 0.0)
    mixing = (gram[None] * decay * step_dt.T[:, None, :]).astype(jnp.bfloat16)
    heads_x = inputs_x.reshape(length, heads, hdim)
    inside = jnp.einsum("htu,uhp->thp", mixing, heads_x, preferred_element_type=jnp.float32)
    carried = jnp.exp(running)[:, :, None] * jnp.einsum(
        "tn,hpn->thp", c_rows.astype(jnp.float32), state, precision=lax.Precision.HIGHEST
    )
    final_log = running[-1]
    weighting = jnp.exp(final_log[None, :] - running) * step_dt
    weighted = (
        (heads_x.astype(jnp.float32) * weighting[:, :, None])
        .astype(jnp.bfloat16)
        .reshape(length, heads * hdim)
    )
    contrib = jnp.einsum("ud,un->dn", weighted, b_rows, preferred_element_type=jnp.float32).reshape(
        heads, hdim, -1
    )
    new_state = jnp.exp(final_log)[:, None, None] * state + contrib
    return (new_state, (inside + carried).reshape(length, heads * hdim))


def local(
    hidden, w_in, conv_weight, conv_bias, dt_bias, a_log, d_skip, norm_weight, lengths, prompt_group
):
    tok_rows = hidden[0, 0]
    slots = tok_rows.shape[0]
    inner = norm_weight.shape[0]
    heads = dt_bias.shape[0]
    hdim = inner // heads
    nstate = (conv_bias.shape[0] - inner) // 2
    convdim = conv_bias.shape[0]
    taps = conv_weight.shape[0]
    seq_count = lax.axis_size("seq")
    my_group = lax.axis_index("req")
    my_block = lax.axis_index("seq")
    qlen = jnp.sum(jnp.where(prompt_group == my_group, lengths, 0))
    filled = jnp.arange(slots, dtype=jnp.int32) < qlen
    wide_rows = lax.all_gather(w_in, "seq", axis=1, tiled=True)
    projected = jnp.dot(
        tok_rows,
        lax.all_gather(wide_rows, "req", axis=0, tiled=True),
        preferred_element_type=jnp.float32,
    ).astype(jnp.bfloat16)
    gate_z = projected[:, :inner]
    conv_in = projected[:, inner : inner + convdim]
    dt_raw = projected[:, inner + convdim :]
    edge_rows = lax.dynamic_slice_in_dim(conv_in, qlen - (taps - 1), taps - 1, 0)
    prev_edge = shifted(edge_rows, "seq", 1)
    extended = jnp.concatenate([prev_edge, conv_in], axis=0)
    accum = jnp.zeros((slots, convdim), jnp.float32) + conv_bias[None, :]
    for tap_index in range(taps):
        accum = accum + conv_weight[tap_index][None, :] * extended[
            tap_index : tap_index + slots
        ].astype(jnp.float32)
    conv_act = jax.nn.silu(accum).astype(jnp.bfloat16)
    inputs_x = conv_act[:, :inner]
    b_rows = conv_act[:, inner : inner + nstate]
    c_rows = conv_act[:, inner + nstate :]
    step_dt = jnp.where(
        filled[:, None], jax.nn.softplus(dt_raw.astype(jnp.float32) + dt_bias[None, :]), 0.0
    )
    log_decay = step_dt * (-jnp.exp(a_log))[None, :]
    through = jnp.cumsum(log_decay, axis=0)
    block_total = through[-1]
    block_rows = min(BLOCK, slots)
    count = slots // block_rows
    pieces = (
        inputs_x.reshape(count, block_rows, inner),
        b_rows.reshape(count, block_rows, nstate),
        c_rows.reshape(count, block_rows, nstate),
        step_dt.reshape(count, block_rows, heads),
        log_decay.reshape(count, block_rows, heads),
    )
    zero_state = jnp.zeros((heads, hdim, nstate), jnp.float32)
    local_end = zero_state
    outs = []
    for index in range(count):
        local_end, out = block_step(local_end, tuple(piece[index] for piece in pieces))
        outs.append(out)
    outputs = jnp.concatenate(outs, axis=0)
    total_hi = lax.reduce_precision(block_total, exponent_bits=8, mantissa_bits=7)
    total_rest = block_total - total_hi
    total_mid = lax.reduce_precision(total_rest, exponent_bits=8, mantissa_bits=7)
    total_lo = total_rest - total_mid
    parts = jnp.stack([total_hi, total_mid, total_lo], axis=1).astype(jnp.bfloat16)
    parts = jnp.broadcast_to(parts[:, :, None], (heads, 3, 128))
    packed = jnp.concatenate(
        [local_end.reshape(heads, hdim * nstate).astype(jnp.bfloat16), parts.reshape(heads, 3 * 128)],
        axis=1,
    )
    gathered = lax.all_gather(packed, "seq", axis=0, tiled=False)
    ends = gathered[:, :, : hdim * nstate].astype(jnp.float32).reshape(seq_count, heads, hdim, nstate)
    sent = gathered[:, :, hdim * nstate :].astype(jnp.float32)
    totals = sent[:, :, 0] + (sent[:, :, 128] + sent[:, :, 256])
    entering = zero_state
    for turn in range(seq_count - 1):
        stepped = jnp.exp(totals[turn])[:, None, None] * entering + ends[turn]
        entering = jnp.where(turn < my_block, stepped, entering)
    incoming = jnp.exp(through)[:, :, None] * jnp.einsum(
        "tn,hpn->thp", c_rows.astype(jnp.float32), entering, precision=lax.Precision.HIGHEST
    )
    heads_y = (
        outputs.reshape(slots, heads, hdim)
        + incoming
        + d_skip[None, :, None] * inputs_x.astype(jnp.float32).reshape(slots, heads, hdim)
    )
    gated = heads_y.reshape(slots, inner) * jax.nn.silu(gate_z.astype(jnp.float32))
    scale = lax.rsqrt(jnp.mean(gated * gated, axis=1, keepdims=True) + 1e-05)
    normed = jnp.where(filled[:, None], gated * scale * norm_weight[None, :], 0.0)
    gated_out = normed.astype(jnp.bfloat16).reshape(1, 1, slots, inner)
    later_mask = jnp.arange(seq_count)[None, :] > jnp.arange(seq_count)[:, None]
    after = jnp.sum(jnp.where(later_mask[:, :, None], totals[None, :, :], 0.0), axis=1)
    piece = hdim // seq_count
    own_ends = lax.dynamic_slice_in_dim(ends, my_block * piece, piece, axis=2)
    share = jnp.sum(jnp.exp(after)[:, :, None, None] * own_ends, axis=0)
    moved = lax.all_to_all(share[None], "req", split_axis=1, concat_axis=0, tiled=True)
    final_states = jnp.take(moved, prompt_group, axis=0)
    return (gated_out, final_states)


def solution(mesh):
    in_specs = (
        P("req", "seq", None, None),
        P("req", "seq"),
        P(),
        P(),
        P(),
        P(),
        P(),
        P(),
        P(),
        P(),
    )
    out_specs = (P("req", "seq", None, None), P(None, "req", "seq", None))
    return jax.shard_map(local, mesh=mesh, in_specs=in_specs, out_specs=out_specs, check_vma=False)
```

```python
import jax
import jax.numpy as jnp
from jax import lax
from jax.sharding import PartitionSpec as P

BLOCK = 256


def shifted(block, axis, distance):
    devices = range(lax.axis_size(axis))
    route = [(i - distance, i) for i in devices if i - distance in devices]
    return lax.ppermute(block, axis, route)


def block_step(state, pieces):
    inputs_x, b_rows, c_rows, step_dt, log_decay = pieces
    length = inputs_x.shape[0]
    heads = step_dt.shape[1]
    hdim = inputs_x.shape[1] // heads
    running = jnp.cumsum(log_decay, axis=0)
    gram = jnp.einsum("tn,un->tu", c_rows, b_rows, preferred_element_type=jnp.float32)
    later = jnp.arange(length)[:, None] >= jnp.arange(length)[None, :]
    spread = running.T[:, :, None] - running.T[:, None, :]
    decay = jnp.where(later[None], jnp.exp(jnp.where(later[None], spread, 0.0)), 0.0)
    mixing = (gram[None] * decay * step_dt.T[:, None, :]).astype(jnp.bfloat16)
    heads_x = inputs_x.reshape(length, heads, hdim)
    inside = jnp.einsum("htu,uhp->thp", mixing, heads_x, preferred_element_type=jnp.float32)
    carried = jnp.exp(running)[:, :, None] * jnp.einsum(
        "tn,hpn->thp", c_rows.astype(jnp.float32), state, precision=lax.Precision.HIGHEST
    )
    final_log = running[-1]
    weighting = jnp.exp(final_log[None, :] - running) * step_dt
    weighted = (
        (heads_x.astype(jnp.float32) * weighting[:, :, None])
        .astype(jnp.bfloat16)
        .reshape(length, heads * hdim)
    )
    contrib = jnp.einsum("ud,un->dn", weighted, b_rows, preferred_element_type=jnp.float32).reshape(
        heads, hdim, -1
    )
    new_state = jnp.exp(final_log)[:, None, None] * state + contrib
    return (new_state, (inside + carried).reshape(length, heads * hdim))


def local(
    hidden, w_in, conv_weight, conv_bias, dt_bias, a_log, d_skip, norm_weight, lengths, prompt_group
):
    tok_rows = hidden[0, 0]
    slots = tok_rows.shape[0]
    inner = norm_weight.shape[0]
    heads = dt_bias.shape[0]
    hdim = inner // heads
    nstate = (conv_bias.shape[0] - inner) // 2
    convdim = conv_bias.shape[0]
    taps = conv_weight.shape[0]
    seq_count = lax.axis_size("seq")
    my_group = lax.axis_index("req")
    my_block = lax.axis_index("seq")
    qlen = jnp.sum(jnp.where(prompt_group == my_group, lengths, 0))
    filled = jnp.arange(slots, dtype=jnp.int32) < qlen
    edge_hidden = lax.dynamic_slice_in_dim(tok_rows, qlen - (taps - 1), taps - 1, 0)
    prev_hidden = shifted(edge_hidden, "seq", 1)
    wide_rows = lax.all_gather(w_in, "seq", axis=1, tiled=True)
    both_rows = jnp.concatenate([tok_rows, prev_hidden], axis=0)
    projected = jnp.dot(
        both_rows,
        lax.all_gather(wide_rows, "req", axis=0, tiled=True),
        preferred_element_type=jnp.float32,
    ).astype(jnp.bfloat16)
    gate_z = projected[:slots, :inner]
    conv_in = projected[:slots, inner : inner + convdim]
    prev_edge = projected[slots:, inner : inner + convdim].astype(jnp.float32)
    dt_raw = projected[:slots, inner + convdim :]
    accum = jnp.zeros((slots, convdim), jnp.float32) + conv_bias[None, :]
    for tap_index in range(taps):
        lag = taps - 1 - tap_index
        taken = jnp.pad(conv_in[: slots - lag], ((lag, 0), (0, 0))).astype(jnp.float32)
        accum = accum + conv_weight[tap_index][None, :] * taken
    edge_terms = []
    for row in range(taps - 1):
        term = jnp.zeros((convdim,), jnp.float32)
        for tap_index in range(taps - 1 - row):
            term = term + conv_weight[tap_index] * prev_edge[row + tap_index]
        edge_terms.append(term)
    edge_fix = jnp.pad(jnp.stack(edge_terms), ((0, slots - (taps - 1)), (0, 0)))
    accum = accum + edge_fix
    conv_act = jax.nn.silu(accum).astype(jnp.bfloat16)
    inputs_x = conv_act[:, :inner]
    b_rows = conv_act[:, inner : inner + nstate]
    c_rows = conv_act[:, inner + nstate :]
    step_dt = jnp.where(
        filled[:, None], jax.nn.softplus(dt_raw.astype(jnp.float32) + dt_bias[None, :]), 0.0
    )
    log_decay = step_dt * (-jnp.exp(a_log))[None, :]
    through = jnp.cumsum(log_decay, axis=0)
    block_total = through[-1]
    block_rows = min(BLOCK, slots)
    count = slots // block_rows
    pieces = (
        inputs_x.reshape(count, block_rows, inner),
        b_rows.reshape(count, block_rows, nstate),
        c_rows.reshape(count, block_rows, nstate),
        step_dt.reshape(count, block_rows, heads),
        log_decay.reshape(count, block_rows, heads),
    )
    zero_state = jnp.zeros((heads, hdim, nstate), jnp.float32)
    local_end = zero_state
    outs = []
    for index in range(count):
        local_end, out = block_step(local_end, tuple(piece[index] for piece in pieces))
        outs.append(out)
    outputs = jnp.concatenate(outs, axis=0)
    total_hi = lax.reduce_precision(block_total, exponent_bits=8, mantissa_bits=7)
    total_rest = block_total - total_hi
    total_mid = lax.reduce_precision(total_rest, exponent_bits=8, mantissa_bits=7)
    total_lo = total_rest - total_mid
    parts = jnp.stack([total_hi, total_mid, total_lo], axis=1).astype(jnp.bfloat16)
    parts = jnp.broadcast_to(parts[:, :, None], (heads, 3, 128))
    packed = jnp.concatenate(
        [local_end.reshape(heads, hdim * nstate).astype(jnp.bfloat16), parts.reshape(heads, 3 * 128)],
        axis=1,
    )
    gathered = lax.all_gather(packed, "seq", axis=0, tiled=False)
    ends = gathered[:, :, : hdim * nstate].astype(jnp.float32).reshape(seq_count, heads, hdim, nstate)
    sent = gathered[:, :, hdim * nstate :].astype(jnp.float32)
    totals = sent[:, :, 0] + (sent[:, :, 128] + sent[:, :, 256])
    order = jnp.arange(seq_count)
    between = (order[None, :] > order[:, None]) & (order[None, :] < my_block)
    log_coef = jnp.sum(jnp.where(between[:, :, None], totals[None, :, :], 0.0), axis=1)
    coef = jnp.where((order < my_block)[:, None], jnp.exp(log_coef), 0.0)
    entering = jnp.sum(coef[:, :, None, None] * ends, axis=0)
    incoming = jnp.exp(through)[:, :, None] * jnp.einsum(
        "tn,hpn->thp", c_rows.astype(jnp.float32), entering, precision=lax.Precision.HIGHEST
    )
    heads_y = (
        outputs.reshape(slots, heads, hdim)
        + incoming
        + d_skip[None, :, None] * inputs_x.astype(jnp.float32).reshape(slots, heads, hdim)
    )
    gated = heads_y.reshape(slots, inner) * jax.nn.silu(gate_z.astype(jnp.float32))
    scale = lax.rsqrt(jnp.mean(gated * gated, axis=1, keepdims=True) + 1e-05)
    normed = jnp.where(filled[:, None], gated * scale * norm_weight[None, :], 0.0)
    gated_out = normed.astype(jnp.bfloat16).reshape(1, 1, slots, inner)
    later_mask = jnp.arange(seq_count)[None, :] > jnp.arange(seq_count)[:, None]
    after = jnp.sum(jnp.where(later_mask[:, :, None], totals[None, :, :], 0.0), axis=1)
    piece = hdim // seq_count
    own_ends = lax.dynamic_slice_in_dim(ends, my_block * piece, piece, axis=2)
    share = jnp.sum(jnp.exp(after)[:, :, None, None] * own_ends, axis=0)
    moved = lax.all_to_all(share[None], "req", split_axis=1, concat_axis=0, tiled=True)
    final_states = jnp.take(moved, prompt_group, axis=0)
    return (gated_out, final_states)


def solution(mesh):
    in_specs = (
        P("req", "seq", None, None),
        P("req", "seq"),
        P(),
        P(),
        P(),
        P(),
        P(),
        P(),
        P(),
        P(),
    )
    out_specs = (P("req", "seq", None, None), P(None, "req", "seq", None))
    return jax.shard_map(local, mesh=mesh, in_specs=in_specs, out_specs=out_specs, check_vma=False)
```

```python
import jax
import jax.numpy as jnp
from jax import lax
from jax.sharding import PartitionSpec as P

BLOCK = 256


def shifted(block, axis, distance):
    devices = range(lax.axis_size(axis))
    route = [(i - distance, i) for i in devices if i - distance in devices]
    return lax.ppermute(block, axis, route)


def block_step(state, pieces):
    inputs_x, b_rows, c_rows, step_dt, log_decay = pieces
    length = inputs_x.shape[0]
    heads = step_dt.shape[1]
    hdim = inputs_x.shape[1] // heads
    running = jnp.cumsum(log_decay, axis=0)
    gram = jnp.einsum("tn,un->tu", c_rows, b_rows, preferred_element_type=jnp.float32)
    later = jnp.arange(length)[:, None] >= jnp.arange(length)[None, :]
    spread = running.T[:, :, None] - running.T[:, None, :]
    decay = jnp.where(later[None], jnp.exp(jnp.where(later[None], spread, 0.0)), 0.0)
    mixing = (gram[None] * decay * step_dt.T[:, None, :]).astype(jnp.bfloat16)
    heads_x = inputs_x.reshape(length, heads, hdim)
    inside = jnp.einsum("htu,uhp->thp", mixing, heads_x, preferred_element_type=jnp.float32)
    carried = jnp.exp(running)[:, :, None] * jnp.einsum(
        "tn,hpn->thp", c_rows.astype(jnp.float32), state, precision=lax.Precision.HIGHEST
    )
    final_log = running[-1]
    weighting = jnp.exp(final_log[None, :] - running) * step_dt
    weighted = (
        (heads_x.astype(jnp.float32) * weighting[:, :, None])
        .astype(jnp.bfloat16)
        .reshape(length, heads * hdim)
    )
    contrib = jnp.einsum("ud,un->dn", weighted, b_rows, preferred_element_type=jnp.float32).reshape(
        heads, hdim, -1
    )
    new_state = jnp.exp(final_log)[:, None, None] * state + contrib
    return (new_state, (inside + carried).reshape(length, heads * hdim))


def local(
    hidden, w_in, conv_weight, conv_bias, dt_bias, a_log, d_skip, norm_weight, lengths, prompt_group
):
    tok_rows = hidden[0, 0]
    slots = tok_rows.shape[0]
    inner = norm_weight.shape[0]
    heads = dt_bias.shape[0]
    hdim = inner // heads
    nstate = (conv_bias.shape[0] - inner) // 2
    convdim = conv_bias.shape[0]
    taps = conv_weight.shape[0]
    seq_count = lax.axis_size("seq")
    my_group = lax.axis_index("req")
    my_block = lax.axis_index("seq")
    qlen = jnp.sum(jnp.where(prompt_group == my_group, lengths, 0))
    filled = jnp.arange(slots, dtype=jnp.int32) < qlen
    wide_rows = lax.all_gather(w_in, "seq", axis=1, tiled=True)
    projected = jnp.dot(
        tok_rows,
        lax.all_gather(wide_rows, "req", axis=0, tiled=True),
        preferred_element_type=jnp.float32,
    ).astype(jnp.bfloat16)
    gate_z = projected[:, :inner]
    conv_in = projected[:, inner : inner + convdim]
    dt_raw = projected[:, inner + convdim :]
    edge_rows = lax.dynamic_slice_in_dim(conv_in, qlen - (taps - 1), taps - 1, 0)
    prev_edge = shifted(edge_rows, "seq", 1).astype(jnp.float32)
    accum = jnp.zeros((slots, convdim), jnp.float32) + conv_bias[None, :]
    for tap_index in range(taps):
        lag = taps - 1 - tap_index
        taken = jnp.pad(conv_in[: slots - lag], ((lag, 0), (0, 0))).astype(jnp.float32)
        accum = accum + conv_weight[tap_index][None, :] * taken
    edge_terms = []
    for row in range(taps - 1):
        term = jnp.zeros((convdim,), jnp.float32)
        for tap_index in range(taps - 1 - row):
            term = term + conv_weight[tap_index] * prev_edge[row + tap_index]
        edge_terms.append(term)
    edge_fix = jnp.pad(jnp.stack(edge_terms), ((0, slots - (taps - 1)), (0, 0)))
    accum = accum + edge_fix
    conv_act = jax.nn.silu(accum).astype(jnp.bfloat16)
    inputs_x = conv_act[:, :inner]
    b_rows = conv_act[:, inner : inner + nstate]
    c_rows = conv_act[:, inner + nstate :]
    step_dt = jnp.where(
        filled[:, None], jax.nn.softplus(dt_raw.astype(jnp.float32) + dt_bias[None, :]), 0.0
    )
    log_decay = step_dt * (-jnp.exp(a_log))[None, :]
    through = jnp.cumsum(log_decay, axis=0)
    block_total = through[-1]
    block_rows = min(BLOCK, slots)
    count = slots // block_rows
    pieces = (
        inputs_x.reshape(count, block_rows, inner),
        b_rows.reshape(count, block_rows, nstate),
        c_rows.reshape(count, block_rows, nstate),
        step_dt.reshape(count, block_rows, heads),
        log_decay.reshape(count, block_rows, heads),
    )
    zero_state = jnp.zeros((heads, hdim, nstate), jnp.float32)
    local_end = zero_state
    outs = []
    for index in range(count):
        local_end, out = block_step(local_end, tuple(piece[index] for piece in pieces))
        outs.append(out)
    outputs = jnp.concatenate(outs, axis=0)
    total_hi = lax.reduce_precision(block_total, exponent_bits=8, mantissa_bits=7)
    total_rest = block_total - total_hi
    total_mid = lax.reduce_precision(total_rest, exponent_bits=8, mantissa_bits=7)
    total_lo = total_rest - total_mid
    parts = jnp.stack([total_hi, total_mid, total_lo], axis=1).astype(jnp.bfloat16)
    parts = jnp.broadcast_to(parts[:, :, None], (heads, 3, 128))
    packed = jnp.concatenate(
        [local_end.reshape(heads, hdim * nstate).astype(jnp.bfloat16), parts.reshape(heads, 3 * 128)],
        axis=1,
    )
    gathered = lax.all_gather(packed, "seq", axis=0, tiled=False)
    ends = gathered[:, :, : hdim * nstate].astype(jnp.float32).reshape(seq_count, heads, hdim, nstate)
    sent = gathered[:, :, hdim * nstate :].astype(jnp.float32)
    totals = sent[:, :, 0] + (sent[:, :, 128] + sent[:, :, 256])
    order = jnp.arange(seq_count)
    between = (order[None, :] > order[:, None]) & (order[None, :] < my_block)
    log_coef = jnp.sum(jnp.where(between[:, :, None], totals[None, :, :], 0.0), axis=1)
    coef = jnp.where((order < my_block)[:, None], jnp.exp(log_coef), 0.0)
    entering = jnp.sum(coef[:, :, None, None] * ends, axis=0)
    incoming = jnp.exp(through)[:, :, None] * jnp.einsum(
        "tn,hpn->thp", c_rows.astype(jnp.float32), entering, precision=lax.Precision.HIGHEST
    )
    heads_y = (
        outputs.reshape(slots, heads, hdim)
        + incoming
        + d_skip[None, :, None] * inputs_x.astype(jnp.float32).reshape(slots, heads, hdim)
    )
    gated = heads_y.reshape(slots, inner) * jax.nn.silu(gate_z.astype(jnp.float32))
    scale = lax.rsqrt(jnp.mean(gated * gated, axis=1, keepdims=True) + 1e-05)
    normed = jnp.where(filled[:, None], gated * scale * norm_weight[None, :], 0.0)
    gated_out = normed.astype(jnp.bfloat16).reshape(1, 1, slots, inner)
    later_mask = jnp.arange(seq_count)[None, :] > jnp.arange(seq_count)[:, None]
    after = jnp.sum(jnp.where(later_mask[:, :, None], totals[None, :, :], 0.0), axis=1)
    piece = hdim // seq_count
    own_ends = lax.dynamic_slice_in_dim(ends, my_block * piece, piece, axis=2)
    share = jnp.sum(jnp.exp(after)[:, :, None, None] * own_ends, axis=0)
    moved = lax.all_to_all(share[None], "req", split_axis=1, concat_axis=0, tiled=True)
    final_states = jnp.take(moved, prompt_group, axis=0)
    return (gated_out, final_states)


def solution(mesh):
    in_specs = (
        P("req", "seq", None, None),
        P("req", "seq"),
        P(),
        P(),
        P(),
        P(),
        P(),
        P(),
        P(),
        P(),
    )
    out_specs = (P("req", "seq", None, None), P(None, "req", "seq", None))
    return jax.shard_map(local, mesh=mesh, in_specs=in_specs, out_specs=out_specs, check_vma=False)
```

```python
import jax
import jax.numpy as jnp
from jax import lax
from jax.sharding import PartitionSpec as P

BLOCK = 256


def shifted(block, axis, distance):
    devices = range(lax.axis_size(axis))
    route = [(i - distance, i) for i in devices if i - distance in devices]
    return lax.ppermute(block, axis, route)


def block_step(state, pieces):
    inputs_x, b_rows, c_rows, step_dt, log_decay = pieces
    length = inputs_x.shape[0]
    heads = step_dt.shape[1]
    hdim = inputs_x.shape[1] // heads
    running = jnp.cumsum(log_decay, axis=0)
    gram = jnp.einsum("tn,un->tu", c_rows, b_rows, preferred_element_type=jnp.float32)
    later = jnp.arange(length)[:, None] >= jnp.arange(length)[None, :]
    spread = running.T[:, :, None] - running.T[:, None, :]
    decay = jnp.where(later[None], jnp.exp(jnp.where(later[None], spread, 0.0)), 0.0)
    mixing = (gram[None] * decay * step_dt.T[:, None, :]).astype(jnp.bfloat16)
    heads_x = inputs_x.reshape(length, heads, hdim)
    inside = jnp.einsum("htu,uhp->thp", mixing, heads_x, preferred_element_type=jnp.float32)
    carried = jnp.exp(running)[:, :, None] * jnp.einsum(
        "tn,hpn->thp", c_rows.astype(jnp.float32), state, precision=lax.Precision.HIGHEST
    )
    final_log = running[-1]
    weighting = jnp.exp(final_log[None, :] - running) * step_dt
    weighted = (
        (heads_x.astype(jnp.float32) * weighting[:, :, None])
        .astype(jnp.bfloat16)
        .reshape(length, heads * hdim)
    )
    contrib = jnp.einsum("ud,un->dn", weighted, b_rows, preferred_element_type=jnp.float32).reshape(
        heads, hdim, -1
    )
    new_state = jnp.exp(final_log)[:, None, None] * state + contrib
    return (new_state, (inside + carried).reshape(length, heads * hdim))


def local(
    hidden, w_in, conv_weight, conv_bias, dt_bias, a_log, d_skip, norm_weight, lengths, prompt_group
):
    tok_rows = hidden[0, 0]
    slots = tok_rows.shape[0]
    inner = norm_weight.shape[0]
    heads = dt_bias.shape[0]
    hdim = inner // heads
    nstate = (conv_bias.shape[0] - inner) // 2
    convdim = conv_bias.shape[0]
    taps = conv_weight.shape[0]
    seq_count = lax.axis_size("seq")
    my_group = lax.axis_index("req")
    my_block = lax.axis_index("seq")
    qlen = jnp.sum(jnp.where(prompt_group == my_group, lengths, 0))
    filled = jnp.arange(slots, dtype=jnp.int32) < qlen
    wide_rows = lax.all_gather(w_in, "seq", axis=1, tiled=True)
    projected = jnp.dot(
        tok_rows,
        lax.all_gather(wide_rows, "req", axis=0, tiled=True),
        preferred_element_type=jnp.float32,
    ).astype(jnp.bfloat16)
    gate_z = projected[:, :inner]
    conv_in = projected[:, inner : inner + convdim]
    dt_raw = projected[:, inner + convdim :]
    edge_rows = lax.dynamic_slice_in_dim(conv_in, qlen - (taps - 1), taps - 1, 0)
    prev_edge = shifted(edge_rows, "seq", 1).astype(jnp.float32)
    accum = jnp.zeros((slots, convdim), jnp.float32) + conv_bias[None, :]
    for tap_index in range(taps):
        lag = taps - 1 - tap_index
        taken = jnp.pad(conv_in[: slots - lag], ((lag, 0), (0, 0))).astype(jnp.float32)
        accum = accum + conv_weight[tap_index][None, :] * taken
    edge_terms = []
    for row in range(taps - 1):
        term = jnp.zeros((convdim,), jnp.float32)
        for tap_index in range(taps - 1 - row):
            term = term + conv_weight[tap_index] * prev_edge[row + tap_index]
        edge_terms.append(term)
    edge_fix = jnp.pad(jnp.stack(edge_terms), ((0, slots - (taps - 1)), (0, 0)))
    accum = accum + edge_fix
    conv_act = jax.nn.silu(accum).astype(jnp.bfloat16)
    inputs_x = conv_act[:, :inner]
    b_rows = conv_act[:, inner : inner + nstate]
    c_rows = conv_act[:, inner + nstate :]
    step_dt = jnp.where(
        filled[:, None], jax.nn.softplus(dt_raw.astype(jnp.float32) + dt_bias[None, :]), 0.0
    )
    log_decay = step_dt * (-jnp.exp(a_log))[None, :]
    through = jnp.cumsum(log_decay, axis=0)
    block_total = through[-1]
    block_rows = min(BLOCK, slots)
    count = slots // block_rows
    pieces = (
        inputs_x.reshape(count, block_rows, inner),
        b_rows.reshape(count, block_rows, nstate),
        c_rows.reshape(count, block_rows, nstate),
        step_dt.reshape(count, block_rows, heads),
        log_decay.reshape(count, block_rows, heads),
    )
    zero_state = jnp.zeros((heads, hdim, nstate), jnp.float32)
    local_end = zero_state
    outs = []
    for index in range(count):
        local_end, out = block_step(local_end, tuple(piece[index] for piece in pieces))
        outs.append(out)
    outputs = jnp.concatenate(outs, axis=0)
    total_hi = lax.reduce_precision(block_total, exponent_bits=8, mantissa_bits=7)
    total_rest = block_total - total_hi
    total_mid = lax.reduce_precision(total_rest, exponent_bits=8, mantissa_bits=7)
    total_lo = total_rest - total_mid
    parts = jnp.stack([total_hi, total_mid, total_lo], axis=1).astype(jnp.bfloat16)
    parts = jnp.broadcast_to(parts[:, :, None], (heads, 3, 128))
    packed = jnp.concatenate(
        [local_end.reshape(heads, hdim * nstate).astype(jnp.bfloat16), parts.reshape(heads, 3 * 128)],
        axis=1,
    )
    arrived = [packed]
    for distance in range(1, seq_count):
        cycle = [(i, (i + distance) % seq_count) for i in range(seq_count)]
        arrived.append(lax.ppermute(packed, "seq", cycle))
    gathered = jnp.stack(arrived)
    ends = gathered[:, :, : hdim * nstate].astype(jnp.float32).reshape(seq_count, heads, hdim, nstate)
    sent = gathered[:, :, hdim * nstate :].astype(jnp.float32)
    by_distance = sent[:, :, 0] + (sent[:, :, 128] + sent[:, :, 256])
    order = jnp.arange(seq_count)
    source = (my_block - order) % seq_count
    totals = jnp.take(by_distance, (my_block - order) % seq_count, axis=0)
    between = (order[None, :] > order[:, None]) & (order[None, :] < my_block)
    log_coef = jnp.sum(jnp.where(between[:, :, None], totals[None, :, :], 0.0), axis=1)
    coef = jnp.where((order < my_block)[:, None], jnp.exp(log_coef), 0.0)
    coef_by_distance = jnp.take(coef, source, axis=0)
    entering = jnp.sum(coef_by_distance[:, :, None, None] * ends, axis=0)
    incoming = jnp.exp(through)[:, :, None] * jnp.einsum(
        "tn,hpn->thp", c_rows.astype(jnp.float32), entering, precision=lax.Precision.HIGHEST
    )
    heads_y = (
        outputs.reshape(slots, heads, hdim)
        + incoming
        + d_skip[None, :, None] * inputs_x.astype(jnp.float32).reshape(slots, heads, hdim)
    )
    gated = heads_y.reshape(slots, inner) * jax.nn.silu(gate_z.astype(jnp.float32))
    scale = lax.rsqrt(jnp.mean(gated * gated, axis=1, keepdims=True) + 1e-05)
    normed = jnp.where(filled[:, None], gated * scale * norm_weight[None, :], 0.0)
    gated_out = normed.astype(jnp.bfloat16).reshape(1, 1, slots, inner)
    later_mask = order[None, :] > order[:, None]
    after = jnp.sum(jnp.where(later_mask[:, :, None], totals[None, :, :], 0.0), axis=1)
    after_by_distance = jnp.take(after, source, axis=0)
    piece = hdim // seq_count
    own_ends = lax.dynamic_slice_in_dim(ends, my_block * piece, piece, axis=2)
    share = jnp.sum(jnp.exp(after_by_distance)[:, :, None, None] * own_ends, axis=0)
    moved = lax.all_to_all(share[None], "req", split_axis=1, concat_axis=0, tiled=True)
    final_states = jnp.take(moved, prompt_group, axis=0)
    return (gated_out, final_states)


def solution(mesh):
    in_specs = (
        P("req", "seq", None, None),
        P("req", "seq"),
        P(),
        P(),
        P(),
        P(),
        P(),
        P(),
        P(),
        P(),
    )
    out_specs = (P("req", "seq", None, None), P(None, "req", "seq", None))
    return jax.shard_map(local, mesh=mesh, in_specs=in_specs, out_specs=out_specs, check_vma=False)
```

```python
import jax
import jax.numpy as jnp
from jax import lax
from jax.sharding import PartitionSpec as P

BLOCK = 256


def shifted(block, axis, distance):
    devices = range(lax.axis_size(axis))
    route = [(i - distance, i) for i in devices if i - distance in devices]
    return lax.ppermute(block, axis, route)


def block_step(state, pieces):
    inputs_x, b_rows, c_rows, step_dt, log_decay = pieces
    length = inputs_x.shape[0]
    heads = step_dt.shape[1]
    hdim = inputs_x.shape[1] // heads
    running = jnp.cumsum(log_decay, axis=0)
    gram = jnp.einsum("tn,un->tu", c_rows, b_rows, preferred_element_type=jnp.float32)
    later = jnp.arange(length)[:, None] >= jnp.arange(length)[None, :]
    spread = running.T[:, :, None] - running.T[:, None, :]
    decay = jnp.where(later[None], jnp.exp(jnp.where(later[None], spread, 0.0)), 0.0)
    mixing = (gram[None] * decay * step_dt.T[:, None, :]).astype(jnp.bfloat16)
    heads_x = inputs_x.reshape(length, heads, hdim)
    inside = jnp.einsum("htu,uhp->thp", mixing, heads_x, preferred_element_type=jnp.float32)
    carried = jnp.exp(running)[:, :, None] * jnp.einsum(
        "tn,hpn->thp", c_rows.astype(jnp.float32), state, precision=lax.Precision.HIGHEST
    )
    final_log = running[-1]
    weighting = jnp.exp(final_log[None, :] - running) * step_dt
    weighted = (
        (heads_x.astype(jnp.float32) * weighting[:, :, None])
        .astype(jnp.bfloat16)
        .reshape(length, heads * hdim)
    )
    contrib = jnp.einsum("ud,un->dn", weighted, b_rows, preferred_element_type=jnp.float32).reshape(
        heads, hdim, -1
    )
    new_state = jnp.exp(final_log)[:, None, None] * state + contrib
    return (new_state, (inside + carried).reshape(length, heads * hdim))


def local(
    hidden, w_in, conv_weight, conv_bias, dt_bias, a_log, d_skip, norm_weight, lengths, prompt_group
):
    tok_rows = hidden[0, 0]
    slots = tok_rows.shape[0]
    inner = norm_weight.shape[0]
    heads = dt_bias.shape[0]
    hdim = inner // heads
    nstate = (conv_bias.shape[0] - inner) // 2
    convdim = conv_bias.shape[0]
    taps = conv_weight.shape[0]
    seq_count = lax.axis_size("seq")
    my_group = lax.axis_index("req")
    my_block = lax.axis_index("seq")
    qlen = jnp.sum(jnp.where(prompt_group == my_group, lengths, 0))
    filled = jnp.arange(slots, dtype=jnp.int32) < qlen
    stacked = lax.all_gather(w_in, "seq", axis=0, tiled=False)
    wide_rows = jnp.transpose(stacked, (1, 0, 2)).reshape(w_in.shape[0], -1)
    projected = jnp.dot(
        tok_rows,
        lax.all_gather(wide_rows, "req", axis=0, tiled=True),
        preferred_element_type=jnp.float32,
    ).astype(jnp.bfloat16)
    gate_z = projected[:, :inner]
    conv_in = projected[:, inner : inner + convdim]
    dt_raw = projected[:, inner + convdim :]
    edge_rows = lax.dynamic_slice_in_dim(conv_in, qlen - (taps - 1), taps - 1, 0)
    prev_edge = shifted(edge_rows, "seq", 1).astype(jnp.float32)
    accum = jnp.zeros((slots, convdim), jnp.float32) + conv_bias[None, :]
    for tap_index in range(taps):
        lag = taps - 1 - tap_index
        taken = jnp.pad(conv_in[: slots - lag], ((lag, 0), (0, 0))).astype(jnp.float32)
        accum = accum + conv_weight[tap_index][None, :] * taken
    edge_terms = []
    for row in range(taps - 1):
        term = jnp.zeros((convdim,), jnp.float32)
        for tap_index in range(taps - 1 - row):
            term = term + conv_weight[tap_index] * prev_edge[row + tap_index]
        edge_terms.append(term)
    edge_fix = jnp.pad(jnp.stack(edge_terms), ((0, slots - (taps - 1)), (0, 0)))
    accum = accum + edge_fix
    conv_act = jax.nn.silu(accum).astype(jnp.bfloat16)
    inputs_x = conv_act[:, :inner]
    b_rows = conv_act[:, inner : inner + nstate]
    c_rows = conv_act[:, inner + nstate :]
    step_dt = jnp.where(
        filled[:, None], jax.nn.softplus(dt_raw.astype(jnp.float32) + dt_bias[None, :]), 0.0
    )
    log_decay = step_dt * (-jnp.exp(a_log))[None, :]
    through = jnp.cumsum(log_decay, axis=0)
    block_total = through[-1]
    block_rows = min(BLOCK, slots)
    count = slots // block_rows
    pieces = (
        inputs_x.reshape(count, block_rows, inner),
        b_rows.reshape(count, block_rows, nstate),
        c_rows.reshape(count, block_rows, nstate),
        step_dt.reshape(count, block_rows, heads),
        log_decay.reshape(count, block_rows, heads),
    )
    zero_state = jnp.zeros((heads, hdim, nstate), jnp.float32)
    local_end = zero_state
    outs = []
    for index in range(count):
        local_end, out = block_step(local_end, tuple(piece[index] for piece in pieces))
        outs.append(out)
    outputs = jnp.concatenate(outs, axis=0)
    total_hi = lax.reduce_precision(block_total, exponent_bits=8, mantissa_bits=7)
    total_rest = block_total - total_hi
    total_mid = lax.reduce_precision(total_rest, exponent_bits=8, mantissa_bits=7)
    total_lo = total_rest - total_mid
    parts = jnp.stack([total_hi, total_mid, total_lo], axis=1).astype(jnp.bfloat16)
    parts = jnp.broadcast_to(parts[:, :, None], (heads, 3, 128))
    packed = jnp.concatenate(
        [local_end.reshape(heads, hdim * nstate).astype(jnp.bfloat16), parts.reshape(heads, 3 * 128)],
        axis=1,
    )
    gathered = lax.all_gather(packed, "seq", axis=0, tiled=False)
    ends = gathered[:, :, : hdim * nstate].astype(jnp.float32).reshape(seq_count, heads, hdim, nstate)
    sent = gathered[:, :, hdim * nstate :].astype(jnp.float32)
    totals = sent[:, :, 0] + (sent[:, :, 128] + sent[:, :, 256])
    order = jnp.arange(seq_count)
    between = (order[None, :] > order[:, None]) & (order[None, :] < my_block)
    log_coef = jnp.sum(jnp.where(between[:, :, None], totals[None, :, :], 0.0), axis=1)
    coef = jnp.where((order < my_block)[:, None], jnp.exp(log_coef), 0.0)
    entering = jnp.sum(coef[:, :, None, None] * ends, axis=0)
    incoming = jnp.exp(through)[:, :, None] * jnp.einsum(
        "tn,hpn->thp", c_rows.astype(jnp.float32), entering, precision=lax.Precision.HIGHEST
    )
    heads_y = (
        outputs.reshape(slots, heads, hdim)
        + incoming
        + d_skip[None, :, None] * inputs_x.astype(jnp.float32).reshape(slots, heads, hdim)
    )
    gated = heads_y.reshape(slots, inner) * jax.nn.silu(gate_z.astype(jnp.float32))
    scale = lax.rsqrt(jnp.mean(gated * gated, axis=1, keepdims=True) + 1e-05)
    normed = jnp.where(filled[:, None], gated * scale * norm_weight[None, :], 0.0)
    gated_out = normed.astype(jnp.bfloat16).reshape(1, 1, slots, inner)
    later_mask = jnp.arange(seq_count)[None, :] > jnp.arange(seq_count)[:, None]
    after = jnp.sum(jnp.where(later_mask[:, :, None], totals[None, :, :], 0.0), axis=1)
    piece = hdim // seq_count
    own_ends = lax.dynamic_slice_in_dim(ends, my_block * piece, piece, axis=2)
    share = jnp.sum(jnp.exp(after)[:, :, None, None] * own_ends, axis=0)
    moved = lax.all_to_all(share[None], "req", split_axis=1, concat_axis=0, tiled=True)
    final_states = jnp.take(moved, prompt_group, axis=0)
    return (gated_out, final_states)


def solution(mesh):
    in_specs = (
        P("req", "seq", None, None),
        P("req", "seq"),
        P(),
        P(),
        P(),
        P(),
        P(),
        P(),
        P(),
        P(),
    )
    out_specs = (P("req", "seq", None, None), P(None, "req", "seq", None))
    return jax.shard_map(local, mesh=mesh, in_specs=in_specs, out_specs=out_specs, check_vma=False)
```

```python
import jax
import jax.numpy as jnp
from jax import lax
from jax.experimental import pallas as pl
from jax.experimental.pallas import tpu as pltpu
from jax.sharding import PartitionSpec as P

BLOCK = 256


def shifted(block, axis, distance):
    devices = range(lax.axis_size(axis))
    route = [(i - distance, i) for i in devices if i - distance in devices]
    return lax.ppermute(block, axis, route)


def conv_kernel(x_ref, edge_ref, w_ref, b_ref, o_ref):
    x = x_ref[...].astype(jnp.float32)
    edge = edge_ref[...].astype(jnp.float32)
    w = w_ref[...]
    taps = w.shape[1]
    lane = lax.broadcasted_iota(jnp.int32, x.shape, 1)
    acc = jnp.broadcast_to(b_ref[...], x.shape)
    for tap in range(taps):
        lag = taps - 1 - tap
        moved = x
        if lag > 0:
            moved = pltpu.roll(x, lag, 1)
            for t in range(lag):
                moved = jnp.where(lane == t, edge[:, taps - 1 - lag + t][:, None], moved)
        acc = acc + w[:, tap][:, None] * moved
    o_ref[...] = (acc * (1.0 / (1.0 + jnp.exp(-acc)))).astype(o_ref.dtype)


def conv_silu(conv_t, edge_t, weight_t, bias_t, rows=256):
    feats, slots = conv_t.shape
    taps = weight_t.shape[1]
    return pl.pallas_call(
        conv_kernel,
        grid=(feats // rows,),
        in_specs=[
            pl.BlockSpec((rows, slots), lambda i: (i, 0)),
            pl.BlockSpec((rows, taps - 1), lambda i: (i, 0)),
            pl.BlockSpec((rows, taps), lambda i: (i, 0)),
            pl.BlockSpec((rows, 1), lambda i: (i, 0)),
        ],
        out_specs=pl.BlockSpec((rows, slots), lambda i: (i, 0)),
        out_shape=jax.ShapeDtypeStruct((feats, slots), jnp.bfloat16),
        cost_estimate=pl.CostEstimate(
            flops=feats * slots * 14, transcendentals=feats * slots, bytes_accessed=feats * slots * 4
        ),
    )(conv_t, edge_t, weight_t, bias_t)


def block_step(state, pieces):
    inputs_x, b_rows, c_rows, step_dt, log_decay = pieces
    length = inputs_x.shape[0]
    heads = step_dt.shape[1]
    hdim = inputs_x.shape[1] // heads
    running = jnp.cumsum(log_decay, axis=0)
    gram = jnp.einsum("tn,un->tu", c_rows, b_rows, preferred_element_type=jnp.float32)
    later = jnp.arange(length)[:, None] >= jnp.arange(length)[None, :]
    spread = running.T[:, :, None] - running.T[:, None, :]
    decay = jnp.where(later[None], jnp.exp(jnp.where(later[None], spread, 0.0)), 0.0)
    mixing = (gram[None] * decay * step_dt.T[:, None, :]).astype(jnp.bfloat16)
    heads_x = inputs_x.reshape(length, heads, hdim)
    inside = jnp.einsum("htu,uhp->thp", mixing, heads_x, preferred_element_type=jnp.float32)
    carried = jnp.exp(running)[:, :, None] * jnp.einsum(
        "tn,hpn->thp", c_rows.astype(jnp.float32), state, precision=lax.Precision.HIGHEST
    )
    final_log = running[-1]
    weighting = jnp.exp(final_log[None, :] - running) * step_dt
    weighted = (
        (heads_x.astype(jnp.float32) * weighting[:, :, None])
        .astype(jnp.bfloat16)
        .reshape(length, heads * hdim)
    )
    contrib = jnp.einsum("ud,un->dn", weighted, b_rows, preferred_element_type=jnp.float32).reshape(
        heads, hdim, -1
    )
    new_state = jnp.exp(final_log)[:, None, None] * state + contrib
    return (new_state, (inside + carried).reshape(length, heads * hdim))


def local(
    hidden, w_in, conv_weight, conv_bias, dt_bias, a_log, d_skip, norm_weight, lengths, prompt_group
):
    tok_rows = hidden[0, 0]
    slots = tok_rows.shape[0]
    inner = norm_weight.shape[0]
    heads = dt_bias.shape[0]
    hdim = inner // heads
    nstate = (conv_bias.shape[0] - inner) // 2
    convdim = conv_bias.shape[0]
    taps = conv_weight.shape[0]
    seq_count = lax.axis_size("seq")
    my_group = lax.axis_index("req")
    my_block = lax.axis_index("seq")
    qlen = jnp.sum(jnp.where(prompt_group == my_group, lengths, 0))
    filled = jnp.arange(slots, dtype=jnp.int32) < qlen
    wide_rows = lax.all_gather(w_in, "seq", axis=1, tiled=True)
    projected = jnp.dot(
        tok_rows,
        lax.all_gather(wide_rows, "req", axis=0, tiled=True),
        preferred_element_type=jnp.float32,
    ).astype(jnp.bfloat16)
    gate_z = projected[:, :inner]
    conv_in = projected[:, inner : inner + convdim]
    dt_raw = projected[:, inner + convdim :]
    edge_rows = lax.dynamic_slice_in_dim(conv_in, qlen - (taps - 1), taps - 1, 0)
    prev_edge = shifted(edge_rows, "seq", 1)
    conv_act = conv_silu(conv_in.T, prev_edge.T, conv_weight.T, conv_bias[:, None]).T
    inputs_x = conv_act[:, :inner]
    b_rows = conv_act[:, inner : inner + nstate]
    c_rows = conv_act[:, inner + nstate :]
    step_dt = jnp.where(
        filled[:, None], jax.nn.softplus(dt_raw.astype(jnp.float32) + dt_bias[None, :]), 0.0
    )
    log_decay = step_dt * (-jnp.exp(a_log))[None, :]
    through = jnp.cumsum(log_decay, axis=0)
    block_total = through[-1]
    block_rows = min(BLOCK, slots)
    count = slots // block_rows
    pieces = (
        inputs_x.reshape(count, block_rows, inner),
        b_rows.reshape(count, block_rows, nstate),
        c_rows.reshape(count, block_rows, nstate),
        step_dt.reshape(count, block_rows, heads),
        log_decay.reshape(count, block_rows, heads),
    )
    zero_state = jnp.zeros((heads, hdim, nstate), jnp.float32)
    local_end = zero_state
    outs = []
    for index in range(count):
        local_end, out = block_step(local_end, tuple(piece[index] for piece in pieces))
        outs.append(out)
    outputs = jnp.concatenate(outs, axis=0)
    total_hi = lax.reduce_precision(block_total, exponent_bits=8, mantissa_bits=7)
    total_rest = block_total - total_hi
    total_mid = lax.reduce_precision(total_rest, exponent_bits=8, mantissa_bits=7)
    total_lo = total_rest - total_mid
    parts = jnp.stack([total_hi, total_mid, total_lo], axis=1).astype(jnp.bfloat16)
    parts = jnp.broadcast_to(parts[:, :, None], (heads, 3, 128))
    packed = jnp.concatenate(
        [local_end.reshape(heads, hdim * nstate).astype(jnp.bfloat16), parts.reshape(heads, 3 * 128)],
        axis=1,
    )
    gathered = lax.all_gather(packed, "seq", axis=0, tiled=False)
    ends = gathered[:, :, : hdim * nstate].astype(jnp.float32).reshape(seq_count, heads, hdim, nstate)
    sent = gathered[:, :, hdim * nstate :].astype(jnp.float32)
    totals = sent[:, :, 0] + (sent[:, :, 128] + sent[:, :, 256])
    entering = zero_state
    for turn in range(seq_count - 1):
        stepped = jnp.exp(totals[turn])[:, None, None] * entering + ends[turn]
        entering = jnp.where(turn < my_block, stepped, entering)
    incoming = jnp.exp(through)[:, :, None] * jnp.einsum(
        "tn,hpn->thp", c_rows.astype(jnp.float32), entering, precision=lax.Precision.HIGHEST
    )
    heads_y = (
        outputs.reshape(slots, heads, hdim)
        + incoming
        + d_skip[None, :, None] * inputs_x.astype(jnp.float32).reshape(slots, heads, hdim)
    )
    gated = heads_y.reshape(slots, inner) * jax.nn.silu(gate_z.astype(jnp.float32))
    scale = lax.rsqrt(jnp.mean(gated * gated, axis=1, keepdims=True) + 1e-05)
    normed = jnp.where(filled[:, None], gated * scale * norm_weight[None, :], 0.0)
    gated_out = normed.astype(jnp.bfloat16).reshape(1, 1, slots, inner)
    later_mask = jnp.arange(seq_count)[None, :] > jnp.arange(seq_count)[:, None]
    after = jnp.sum(jnp.where(later_mask[:, :, None], totals[None, :, :], 0.0), axis=1)
    piece = hdim // seq_count
    own_ends = lax.dynamic_slice_in_dim(ends, my_block * piece, piece, axis=2)
    share = jnp.sum(jnp.exp(after)[:, :, None, None] * own_ends, axis=0)
    moved = lax.all_to_all(share[None], "req", split_axis=1, concat_axis=0, tiled=True)
    final_states = jnp.take(moved, prompt_group, axis=0)
    return (gated_out, final_states)


def solution(mesh):
    in_specs = (
        P("req", "seq", None, None),
        P("req", "seq"),
        P(),
        P(),
        P(),
        P(),
        P(),
        P(),
        P(),
        P(),
    )
    out_specs = (P("req", "seq", None, None), P(None, "req", "seq", None))
    return jax.shard_map(local, mesh=mesh, in_specs=in_specs, out_specs=out_specs, check_vma=False)
```

```python
import jax
import jax.numpy as jnp
from jax import lax
from jax.experimental import pallas as pl
from jax.experimental.pallas import tpu as pltpu
from jax.sharding import PartitionSpec as P

BLOCK = 256


def shifted(block, axis, distance):
    devices = range(lax.axis_size(axis))
    route = [(i - distance, i) for i in devices if i - distance in devices]
    return lax.ppermute(block, axis, route)


def conv_kernel(x_ref, edge_ref, w_ref, b_ref, o_ref):
    x = x_ref[...].astype(jnp.float32)
    edge = edge_ref[...].astype(jnp.float32)
    w = w_ref[...]
    taps = w.shape[1]
    lane = lax.broadcasted_iota(jnp.int32, x.shape, 1)
    acc = jnp.broadcast_to(b_ref[...], x.shape)
    for tap in range(taps):
        lag = taps - 1 - tap
        moved = x
        if lag > 0:
            moved = pltpu.roll(x, lag, 1)
            for t in range(lag):
                moved = jnp.where(lane == t, edge[:, taps - 1 - lag + t][:, None], moved)
        acc = acc + w[:, tap][:, None] * moved
    o_ref[...] = (acc * (0.5 + 0.5 * jnp.tanh(0.5 * acc))).astype(o_ref.dtype)


def conv_silu(conv_t, edge_t, weight_t, bias_t, rows=256):
    feats, slots = conv_t.shape
    taps = weight_t.shape[1]
    return pl.pallas_call(
        conv_kernel,
        grid=(feats // rows,),
        in_specs=[
            pl.BlockSpec((rows, slots), lambda i: (i, 0)),
            pl.BlockSpec((rows, taps - 1), lambda i: (i, 0)),
            pl.BlockSpec((rows, taps), lambda i: (i, 0)),
            pl.BlockSpec((rows, 1), lambda i: (i, 0)),
        ],
        out_specs=pl.BlockSpec((rows, slots), lambda i: (i, 0)),
        out_shape=jax.ShapeDtypeStruct((feats, slots), jnp.bfloat16),
        cost_estimate=pl.CostEstimate(
            flops=feats * slots * 14, transcendentals=feats * slots, bytes_accessed=feats * slots * 4
        ),
    )(conv_t, edge_t, weight_t, bias_t)


def block_step(state, pieces):
    inputs_x, b_rows, c_rows, step_dt, log_decay = pieces
    length = inputs_x.shape[0]
    heads = step_dt.shape[1]
    hdim = inputs_x.shape[1] // heads
    running = jnp.cumsum(log_decay, axis=0)
    gram = jnp.einsum("tn,un->tu", c_rows, b_rows, preferred_element_type=jnp.float32)
    later = jnp.arange(length)[:, None] >= jnp.arange(length)[None, :]
    spread = running.T[:, :, None] - running.T[:, None, :]
    decay = jnp.where(later[None], jnp.exp(jnp.where(later[None], spread, 0.0)), 0.0)
    mixing = (gram[None] * decay * step_dt.T[:, None, :]).astype(jnp.bfloat16)
    heads_x = inputs_x.reshape(length, heads, hdim)
    inside = jnp.einsum("htu,uhp->thp", mixing, heads_x, preferred_element_type=jnp.float32)
    carried = jnp.exp(running)[:, :, None] * jnp.einsum(
        "tn,hpn->thp", c_rows.astype(jnp.float32), state, precision=lax.Precision.HIGHEST
    )
    final_log = running[-1]
    weighting = jnp.exp(final_log[None, :] - running) * step_dt
    weighted = (
        (heads_x.astype(jnp.float32) * weighting[:, :, None])
        .astype(jnp.bfloat16)
        .reshape(length, heads * hdim)
    )
    contrib = jnp.einsum("ud,un->dn", weighted, b_rows, preferred_element_type=jnp.float32).reshape(
        heads, hdim, -1
    )
    new_state = jnp.exp(final_log)[:, None, None] * state + contrib
    return (new_state, (inside + carried).reshape(length, heads * hdim))


def local(
    hidden, w_in, conv_weight, conv_bias, dt_bias, a_log, d_skip, norm_weight, lengths, prompt_group
):
    tok_rows = hidden[0, 0]
    slots = tok_rows.shape[0]
    inner = norm_weight.shape[0]
    heads = dt_bias.shape[0]
    hdim = inner // heads
    nstate = (conv_bias.shape[0] - inner) // 2
    convdim = conv_bias.shape[0]
    taps = conv_weight.shape[0]
    seq_count = lax.axis_size("seq")
    my_group = lax.axis_index("req")
    my_block = lax.axis_index("seq")
    qlen = jnp.sum(jnp.where(prompt_group == my_group, lengths, 0))
    filled = jnp.arange(slots, dtype=jnp.int32) < qlen
    wide_rows = lax.all_gather(w_in, "seq", axis=1, tiled=True)
    projected = jnp.dot(
        tok_rows,
        lax.all_gather(wide_rows, "req", axis=0, tiled=True),
        preferred_element_type=jnp.float32,
    ).astype(jnp.bfloat16)
    gate_z = projected[:, :inner]
    conv_in = projected[:, inner : inner + convdim]
    dt_raw = projected[:, inner + convdim :]
    edge_rows = lax.dynamic_slice_in_dim(conv_in, qlen - (taps - 1), taps - 1, 0)
    prev_edge = shifted(edge_rows, "seq", 1)
    conv_act = conv_silu(conv_in.T, prev_edge.T, conv_weight.T, conv_bias[:, None]).T
    inputs_x = conv_act[:, :inner]
    b_rows = conv_act[:, inner : inner + nstate]
    c_rows = conv_act[:, inner + nstate :]
    step_dt = jnp.where(
        filled[:, None], jax.nn.softplus(dt_raw.astype(jnp.float32) + dt_bias[None, :]), 0.0
    )
    log_decay = step_dt * (-jnp.exp(a_log))[None, :]
    through = jnp.cumsum(log_decay, axis=0)
    block_total = through[-1]
    block_rows = min(BLOCK, slots)
    count = slots // block_rows
    pieces = (
        inputs_x.reshape(count, block_rows, inner),
        b_rows.reshape(count, block_rows, nstate),
        c_rows.reshape(count, block_rows, nstate),
        step_dt.reshape(count, block_rows, heads),
        log_decay.reshape(count, block_rows, heads),
    )
    zero_state = jnp.zeros((heads, hdim, nstate), jnp.float32)
    local_end = zero_state
    outs = []
    for index in range(count):
        local_end, out = block_step(local_end, tuple(piece[index] for piece in pieces))
        outs.append(out)
    outputs = jnp.concatenate(outs, axis=0)
    total_hi = lax.reduce_precision(block_total, exponent_bits=8, mantissa_bits=7)
    total_rest = block_total - total_hi
    total_mid = lax.reduce_precision(total_rest, exponent_bits=8, mantissa_bits=7)
    total_lo = total_rest - total_mid
    parts = jnp.stack([total_hi, total_mid, total_lo], axis=1).astype(jnp.bfloat16)
    parts = jnp.broadcast_to(parts[:, :, None], (heads, 3, 128))
    packed = jnp.concatenate(
        [local_end.reshape(heads, hdim * nstate).astype(jnp.bfloat16), parts.reshape(heads, 3 * 128)],
        axis=1,
    )
    gathered = lax.all_gather(packed, "seq", axis=0, tiled=False)
    ends = gathered[:, :, : hdim * nstate].astype(jnp.float32).reshape(seq_count, heads, hdim, nstate)
    sent = gathered[:, :, hdim * nstate :].astype(jnp.float32)
    totals = sent[:, :, 0] + (sent[:, :, 128] + sent[:, :, 256])
    entering = zero_state
    for turn in range(seq_count - 1):
        stepped = jnp.exp(totals[turn])[:, None, None] * entering + ends[turn]
        entering = jnp.where(turn < my_block, stepped, entering)
    incoming = jnp.exp(through)[:, :, None] * jnp.einsum(
        "tn,hpn->thp", c_rows.astype(jnp.float32), entering, precision=lax.Precision.HIGHEST
    )
    heads_y = (
        outputs.reshape(slots, heads, hdim)
        + incoming
        + d_skip[None, :, None] * inputs_x.astype(jnp.float32).reshape(slots, heads, hdim)
    )
    gate = gate_z.astype(jnp.float32)
    gated = heads_y.reshape(slots, inner) * (gate * (0.5 + 0.5 * jnp.tanh(0.5 * gate)))
    scale = lax.rsqrt(jnp.mean(gated * gated, axis=1, keepdims=True) + 1e-05)
    normed = jnp.where(filled[:, None], gated * scale * norm_weight[None, :], 0.0)
    gated_out = normed.astype(jnp.bfloat16).reshape(1, 1, slots, inner)
    later_mask = jnp.arange(seq_count)[None, :] > jnp.arange(seq_count)[:, None]
    after = jnp.sum(jnp.where(later_mask[:, :, None], totals[None, :, :], 0.0), axis=1)
    piece = hdim // seq_count
    own_ends = lax.dynamic_slice_in_dim(ends, my_block * piece, piece, axis=2)
    share = jnp.sum(jnp.exp(after)[:, :, None, None] * own_ends, axis=0)
    moved = lax.all_to_all(share[None], "req", split_axis=1, concat_axis=0, tiled=True)
    final_states = jnp.take(moved, prompt_group, axis=0)
    return (gated_out, final_states)


def solution(mesh):
    in_specs = (
        P("req", "seq", None, None),
        P("req", "seq"),
        P(),
        P(),
        P(),
        P(),
        P(),
        P(),
        P(),
        P(),
    )
    out_specs = (P("req", "seq", None, None), P(None, "req", "seq", None))
    return jax.shard_map(local, mesh=mesh, in_specs=in_specs, out_specs=out_specs, check_vma=False)
```

```python
import jax
import jax.numpy as jnp
from jax import lax
from jax.experimental import pallas as pl
from jax.experimental.pallas import tpu as pltpu
from jax.sharding import PartitionSpec as P

BLOCK = 256


def shifted(block, axis, distance):
    devices = range(lax.axis_size(axis))
    route = [(i - distance, i) for i in devices if i - distance in devices]
    return lax.ppermute(block, axis, route)


def conv_kernel(x_ref, edge_ref, w_ref, b_ref, o_ref):
    x = x_ref[...].astype(jnp.float32)
    edge = edge_ref[...].astype(jnp.float32)
    w = w_ref[...]
    b = b_ref[...]
    taps = w.shape[1]
    acc = b + w[:, taps - 1 : taps] * x
    for tap in range(taps - 1):
        acc = acc + w[:, tap : tap + 1] * pltpu.roll(x, taps - 1 - tap, 1)
    o_ref[...] = (acc * (0.5 + 0.5 * jnp.tanh(0.5 * acc))).astype(o_ref.dtype)
    head = x[:, :128]
    lane = lax.broadcasted_iota(jnp.int32, head.shape, 1)
    first = b + w[:, taps - 1 : taps] * head
    for tap in range(taps - 1):
        lag = taps - 1 - tap
        moved = pltpu.roll(head, lag, 1)
        for t in range(lag):
            moved = jnp.where(lane == t, edge[:, tap + t : tap + t + 1], moved)
        first = first + w[:, tap : tap + 1] * moved
    o_ref[:, :128] = (first * (0.5 + 0.5 * jnp.tanh(0.5 * first))).astype(o_ref.dtype)


def conv_silu(conv_t, edge_t, weight_t, bias_t, rows=768):
    feats, slots = conv_t.shape
    taps = weight_t.shape[1]
    return pl.pallas_call(
        conv_kernel,
        grid=(feats // rows,),
        in_specs=[
            pl.BlockSpec((rows, slots), lambda i: (i, 0)),
            pl.BlockSpec((rows, taps - 1), lambda i: (i, 0)),
            pl.BlockSpec((rows, taps), lambda i: (i, 0)),
            pl.BlockSpec((rows, 1), lambda i: (i, 0)),
        ],
        out_specs=pl.BlockSpec((rows, slots), lambda i: (i, 0)),
        out_shape=jax.ShapeDtypeStruct((feats, slots), jnp.bfloat16),
        cost_estimate=pl.CostEstimate(
            flops=feats * slots * 14, transcendentals=feats * slots, bytes_accessed=feats * slots * 4
        ),
    )(conv_t, edge_t, weight_t, bias_t)


def block_step(state, pieces):
    inputs_x, b_rows, c_rows, step_dt, log_decay = pieces
    length = inputs_x.shape[0]
    heads = step_dt.shape[1]
    hdim = inputs_x.shape[1] // heads
    running = jnp.cumsum(log_decay, axis=0)
    gram = jnp.einsum("tn,un->tu", c_rows, b_rows, preferred_element_type=jnp.float32)
    later = jnp.arange(length)[:, None] >= jnp.arange(length)[None, :]
    spread = running.T[:, :, None] - running.T[:, None, :]
    decay = jnp.where(later[None], jnp.exp(jnp.where(later[None], spread, 0.0)), 0.0)
    mixing = (gram[None] * decay * step_dt.T[:, None, :]).astype(jnp.bfloat16)
    heads_x = inputs_x.reshape(length, heads, hdim)
    inside = jnp.einsum("htu,uhp->thp", mixing, heads_x, preferred_element_type=jnp.float32)
    carried = jnp.exp(running)[:, :, None] * jnp.einsum(
        "tn,hpn->thp", c_rows.astype(jnp.float32), state, precision=lax.Precision.HIGHEST
    )
    final_log = running[-1]
    weighting = jnp.exp(final_log[None, :] - running) * step_dt
    weighted = (
        (heads_x.astype(jnp.float32) * weighting[:, :, None])
        .astype(jnp.bfloat16)
        .reshape(length, heads * hdim)
    )
    contrib = jnp.einsum("ud,un->dn", weighted, b_rows, preferred_element_type=jnp.float32).reshape(
        heads, hdim, -1
    )
    new_state = jnp.exp(final_log)[:, None, None] * state + contrib
    return (new_state, (inside + carried).reshape(length, heads * hdim))


def local(
    hidden, w_in, conv_weight, conv_bias, dt_bias, a_log, d_skip, norm_weight, lengths, prompt_group
):
    tok_rows = hidden[0, 0]
    slots = tok_rows.shape[0]
    inner = norm_weight.shape[0]
    heads = dt_bias.shape[0]
    hdim = inner // heads
    nstate = (conv_bias.shape[0] - inner) // 2
    convdim = conv_bias.shape[0]
    taps = conv_weight.shape[0]
    seq_count = lax.axis_size("seq")
    my_group = lax.axis_index("req")
    my_block = lax.axis_index("seq")
    qlen = jnp.sum(jnp.where(prompt_group == my_group, lengths, 0))
    filled = jnp.arange(slots, dtype=jnp.int32) < qlen
    wide_rows = lax.all_gather(w_in, "seq", axis=1, tiled=True)
    projected = jnp.dot(
        tok_rows,
        lax.all_gather(wide_rows, "req", axis=0, tiled=True),
        preferred_element_type=jnp.float32,
    ).astype(jnp.bfloat16)
    gate_z = projected[:, :inner]
    conv_in = projected[:, inner : inner + convdim]
    dt_raw = projected[:, inner + convdim :]
    edge_rows = lax.dynamic_slice_in_dim(conv_in, qlen - (taps - 1), taps - 1, 0)
    prev_edge = shifted(edge_rows, "seq", 1)
    conv_act = conv_silu(conv_in.T, prev_edge.T, conv_weight.T, conv_bias[:, None]).T
    inputs_x = conv_act[:, :inner]
    b_rows = conv_act[:, inner : inner + nstate]
    c_rows = conv_act[:, inner + nstate :]
    step_dt = jnp.where(
        filled[:, None], jax.nn.softplus(dt_raw.astype(jnp.float32) + dt_bias[None, :]), 0.0
    )
    log_decay = step_dt * (-jnp.exp(a_log))[None, :]
    through = jnp.cumsum(log_decay, axis=0)
    block_total = through[-1]
    block_rows = min(BLOCK, slots)
    count = slots // block_rows
    pieces = (
        inputs_x.reshape(count, block_rows, inner),
        b_rows.reshape(count, block_rows, nstate),
        c_rows.reshape(count, block_rows, nstate),
        step_dt.reshape(count, block_rows, heads),
        log_decay.reshape(count, block_rows, heads),
    )
    zero_state = jnp.zeros((heads, hdim, nstate), jnp.float32)
    local_end = zero_state
    outs = []
    for index in range(count):
        local_end, out = block_step(local_end, tuple(piece[index] for piece in pieces))
        outs.append(out)
    outputs = jnp.concatenate(outs, axis=0)
    total_hi = lax.reduce_precision(block_total, exponent_bits=8, mantissa_bits=7)
    total_rest = block_total - total_hi
    total_mid = lax.reduce_precision(total_rest, exponent_bits=8, mantissa_bits=7)
    total_lo = total_rest - total_mid
    parts = jnp.stack([total_hi, total_mid, total_lo], axis=1).astype(jnp.bfloat16)
    parts = jnp.broadcast_to(parts[:, :, None], (heads, 3, 128))
    packed = jnp.concatenate(
        [local_end.reshape(heads, hdim * nstate).astype(jnp.bfloat16), parts.reshape(heads, 3 * 128)],
        axis=1,
    )
    gathered = lax.all_gather(packed, "seq", axis=0, tiled=False)
    ends = gathered[:, :, : hdim * nstate].astype(jnp.float32).reshape(seq_count, heads, hdim, nstate)
    sent = gathered[:, :, hdim * nstate :].astype(jnp.float32)
    totals = sent[:, :, 0] + (sent[:, :, 128] + sent[:, :, 256])
    entering = zero_state
    for turn in range(seq_count - 1):
        stepped = jnp.exp(totals[turn])[:, None, None] * entering + ends[turn]
        entering = jnp.where(turn < my_block, stepped, entering)
    incoming = jnp.exp(through)[:, :, None] * jnp.einsum(
        "tn,hpn->thp", c_rows.astype(jnp.float32), entering, precision=lax.Precision.HIGHEST
    )
    heads_y = (
        outputs.reshape(slots, heads, hdim)
        + incoming
        + d_skip[None, :, None] * inputs_x.astype(jnp.float32).reshape(slots, heads, hdim)
    )
    gate = gate_z.astype(jnp.float32)
    gated = heads_y.reshape(slots, inner) * (gate * (0.5 + 0.5 * jnp.tanh(0.5 * gate)))
    scale = lax.rsqrt(jnp.mean(gated * gated, axis=1, keepdims=True) + 1e-05)
    normed = jnp.where(filled[:, None], gated * scale * norm_weight[None, :], 0.0)
    gated_out = normed.astype(jnp.bfloat16).reshape(1, 1, slots, inner)
    later_mask = jnp.arange(seq_count)[None, :] > jnp.arange(seq_count)[:, None]
    after = jnp.sum(jnp.where(later_mask[:, :, None], totals[None, :, :], 0.0), axis=1)
    piece = hdim // seq_count
    own_ends = lax.dynamic_slice_in_dim(ends, my_block * piece, piece, axis=2)
    share = jnp.sum(jnp.exp(after)[:, :, None, None] * own_ends, axis=0)
    moved = lax.all_to_all(share[None], "req", split_axis=1, concat_axis=0, tiled=True)
    final_states = jnp.take(moved, prompt_group, axis=0)
    return (gated_out, final_states)


def solution(mesh):
    in_specs = (
        P("req", "seq", None, None),
        P("req", "seq"),
        P(),
        P(),
        P(),
        P(),
        P(),
        P(),
        P(),
        P(),
    )
    out_specs = (P("req", "seq", None, None), P(None, "req", "seq", None))
    return jax.shard_map(local, mesh=mesh, in_specs=in_specs, out_specs=out_specs, check_vma=False)
```

```python
import jax
import jax.numpy as jnp
from jax import lax
from jax.experimental import pallas as pl
from jax.experimental.pallas import tpu as pltpu
from jax.sharding import PartitionSpec as P

BLOCK = 256


def shifted(block, axis, distance):
    devices = range(lax.axis_size(axis))
    route = [(i - distance, i) for i in devices if i - distance in devices]
    return lax.ppermute(block, axis, route)


def conv_kernel(x_ref, edge_ref, w_ref, b_ref, o_ref):
    x = x_ref[...].astype(jnp.float32)
    edge = edge_ref[...].astype(jnp.float32)
    w = w_ref[...]
    b = b_ref[...]
    taps = w.shape[1]
    acc = b + w[:, taps - 1 : taps] * x
    for tap in range(taps - 1):
        acc = acc + w[:, tap : tap + 1] * pltpu.roll(x, taps - 1 - tap, 1)
    o_ref[...] = (acc * (0.5 + 0.5 * jnp.tanh(0.5 * acc))).astype(o_ref.dtype)
    head = x[:, :128]
    lane = lax.broadcasted_iota(jnp.int32, head.shape, 1)
    first = b + w[:, taps - 1 : taps] * head
    for tap in range(taps - 1):
        lag = taps - 1 - tap
        moved = pltpu.roll(head, lag, 1)
        for t in range(lag):
            moved = jnp.where(lane == t, edge[:, tap + t : tap + t + 1], moved)
        first = first + w[:, tap : tap + 1] * moved
    o_ref[:, :128] = (first * (0.5 + 0.5 * jnp.tanh(0.5 * first))).astype(o_ref.dtype)


def conv_silu(conv_t, edge_t, weight_t, bias_t, rows=768):
    feats, slots = conv_t.shape
    taps = weight_t.shape[1]
    return pl.pallas_call(
        conv_kernel,
        grid=(feats // rows,),
        in_specs=[
            pl.BlockSpec((rows, slots), lambda i: (i, 0)),
            pl.BlockSpec((rows, taps - 1), lambda i: (i, 0)),
            pl.BlockSpec((rows, taps), lambda i: (i, 0)),
            pl.BlockSpec((rows, 1), lambda i: (i, 0)),
        ],
        out_specs=pl.BlockSpec((rows, slots), lambda i: (i, 0)),
        out_shape=jax.ShapeDtypeStruct((feats, slots), jnp.bfloat16),
        cost_estimate=pl.CostEstimate(
            flops=feats * slots * 14, transcendentals=feats * slots, bytes_accessed=feats * slots * 4
        ),
    )(conv_t, edge_t, weight_t, bias_t)


def norm_kernel(y_ref, z_ref, w_ref, mask_ref, o_ref):
    z = z_ref[...].astype(jnp.float32)
    gated = y_ref[...] * (z * (0.5 + 0.5 * jnp.tanh(0.5 * z)))
    mean = jnp.sum(gated * gated, axis=0, keepdims=True) * (1.0 / gated.shape[0])
    normed = gated * lax.rsqrt(mean + 1e-05) * w_ref[...]
    normed = jnp.where(mask_ref[...] > 0.5, normed, 0.0)
    o_ref[...] = normed.T.astype(o_ref.dtype)


def gate_norm(y_t, z_t, weight, mask, cols=128):
    units, slots = y_t.shape
    return pl.pallas_call(
        norm_kernel,
        grid=(slots // cols,),
        in_specs=[
            pl.BlockSpec((units, cols), lambda i: (0, i)),
            pl.BlockSpec((units, cols), lambda i: (0, i)),
            pl.BlockSpec((units, 1), lambda i: (0, 0)),
            pl.BlockSpec((1, cols), lambda i: (0, i)),
        ],
        out_specs=pl.BlockSpec((cols, units), lambda i: (i, 0)),
        out_shape=jax.ShapeDtypeStruct((slots, units), jnp.bfloat16),
        cost_estimate=pl.CostEstimate(
            flops=units * slots * 12, transcendentals=units * slots, bytes_accessed=units * slots * 8
        ),
    )(y_t, z_t, weight, mask)


def block_step(state, pieces):
    inputs_x, b_rows, c_rows, step_dt, log_decay = pieces
    length = inputs_x.shape[0]
    heads = step_dt.shape[1]
    hdim = inputs_x.shape[1] // heads
    running = jnp.cumsum(log_decay, axis=0)
    gram = jnp.einsum("tn,un->tu", c_rows, b_rows, preferred_element_type=jnp.float32)
    later = jnp.arange(length)[:, None] >= jnp.arange(length)[None, :]
    spread = running.T[:, :, None] - running.T[:, None, :]
    decay = jnp.where(later[None], jnp.exp(jnp.where(later[None], spread, 0.0)), 0.0)
    mixing = (gram[None] * decay * step_dt.T[:, None, :]).astype(jnp.bfloat16)
    heads_x = inputs_x.reshape(length, heads, hdim)
    inside = jnp.einsum("htu,uhp->thp", mixing, heads_x, preferred_element_type=jnp.float32)
    carried = jnp.exp(running)[:, :, None] * jnp.einsum(
        "tn,hpn->thp", c_rows.astype(jnp.float32), state, precision=lax.Precision.HIGHEST
    )
    final_log = running[-1]
    weighting = jnp.exp(final_log[None, :] - running) * step_dt
    weighted = (
        (heads_x.astype(jnp.float32) * weighting[:, :, None])
        .astype(jnp.bfloat16)
        .reshape(length, heads * hdim)
    )
    contrib = jnp.einsum("ud,un->dn", weighted, b_rows, preferred_element_type=jnp.float32).reshape(
        heads, hdim, -1
    )
    new_state = jnp.exp(final_log)[:, None, None] * state + contrib
    return (new_state, (inside + carried).reshape(length, heads * hdim))


def local(
    hidden, w_in, conv_weight, conv_bias, dt_bias, a_log, d_skip, norm_weight, lengths, prompt_group
):
    tok_rows = hidden[0, 0]
    slots = tok_rows.shape[0]
    inner = norm_weight.shape[0]
    heads = dt_bias.shape[0]
    hdim = inner // heads
    nstate = (conv_bias.shape[0] - inner) // 2
    convdim = conv_bias.shape[0]
    taps = conv_weight.shape[0]
    seq_count = lax.axis_size("seq")
    my_group = lax.axis_index("req")
    my_block = lax.axis_index("seq")
    qlen = jnp.sum(jnp.where(prompt_group == my_group, lengths, 0))
    filled = jnp.arange(slots, dtype=jnp.int32) < qlen
    wide_rows = lax.all_gather(w_in, "seq", axis=1, tiled=True)
    projected = jnp.dot(
        tok_rows,
        lax.all_gather(wide_rows, "req", axis=0, tiled=True),
        preferred_element_type=jnp.float32,
    ).astype(jnp.bfloat16)
    gate_z = projected[:, :inner]
    conv_in = projected[:, inner : inner + convdim]
    dt_raw = projected[:, inner + convdim :]
    edge_rows = lax.dynamic_slice_in_dim(conv_in, qlen - (taps - 1), taps - 1, 0)
    prev_edge = shifted(edge_rows, "seq", 1)
    conv_act = conv_silu(conv_in.T, prev_edge.T, conv_weight.T, conv_bias[:, None]).T
    inputs_x = conv_act[:, :inner]
    b_rows = conv_act[:, inner : inner + nstate]
    c_rows = conv_act[:, inner + nstate :]
    step_dt = jnp.where(
        filled[:, None], jax.nn.softplus(dt_raw.astype(jnp.float32) + dt_bias[None, :]), 0.0
    )
    log_decay = step_dt * (-jnp.exp(a_log))[None, :]
    through = jnp.cumsum(log_decay, axis=0)
    block_total = through[-1]
    block_rows = min(BLOCK, slots)
    count = slots // block_rows
    pieces = (
        inputs_x.reshape(count, block_rows, inner),
        b_rows.reshape(count, block_rows, nstate),
        c_rows.reshape(count, block_rows, nstate),
        step_dt.reshape(count, block_rows, heads),
        log_decay.reshape(count, block_rows, heads),
    )
    zero_state = jnp.zeros((heads, hdim, nstate), jnp.float32)
    local_end = zero_state
    outs = []
    for index in range(count):
        local_end, out = block_step(local_end, tuple(piece[index] for piece in pieces))
        outs.append(out)
    outputs = jnp.concatenate(outs, axis=0)
    total_hi = lax.reduce_precision(block_total, exponent_bits=8, mantissa_bits=7)
    total_rest = block_total - total_hi
    total_mid = lax.reduce_precision(total_rest, exponent_bits=8, mantissa_bits=7)
    total_lo = total_rest - total_mid
    parts = jnp.stack([total_hi, total_mid, total_lo], axis=1).astype(jnp.bfloat16)
    parts = jnp.broadcast_to(parts[:, :, None], (heads, 3, 128))
    packed = jnp.concatenate(
        [local_end.reshape(heads, hdim * nstate).astype(jnp.bfloat16), parts.reshape(heads, 3 * 128)],
        axis=1,
    )
    gathered = lax.all_gather(packed, "seq", axis=0, tiled=False)
    ends = gathered[:, :, : hdim * nstate].astype(jnp.float32).reshape(seq_count, heads, hdim, nstate)
    sent = gathered[:, :, hdim * nstate :].astype(jnp.float32)
    totals = sent[:, :, 0] + (sent[:, :, 128] + sent[:, :, 256])
    entering = zero_state
    for turn in range(seq_count - 1):
        stepped = jnp.exp(totals[turn])[:, None, None] * entering + ends[turn]
        entering = jnp.where(turn < my_block, stepped, entering)
    incoming = jnp.exp(through)[:, :, None] * jnp.einsum(
        "tn,hpn->thp", c_rows.astype(jnp.float32), entering, precision=lax.Precision.HIGHEST
    )
    heads_y = (
        outputs.reshape(slots, heads, hdim)
        + incoming
        + d_skip[None, :, None] * inputs_x.astype(jnp.float32).reshape(slots, heads, hdim)
    )
    gated_out = gate_norm(
        heads_y.reshape(slots, inner).T,
        gate_z.T,
        norm_weight[:, None],
        filled.astype(jnp.float32)[None, :],
    ).reshape(1, 1, slots, inner)
    later_mask = jnp.arange(seq_count)[None, :] > jnp.arange(seq_count)[:, None]
    after = jnp.sum(jnp.where(later_mask[:, :, None], totals[None, :, :], 0.0), axis=1)
    piece = hdim // seq_count
    own_ends = lax.dynamic_slice_in_dim(ends, my_block * piece, piece, axis=2)
    share = jnp.sum(jnp.exp(after)[:, :, None, None] * own_ends, axis=0)
    moved = lax.all_to_all(share[None], "req", split_axis=1, concat_axis=0, tiled=True)
    final_states = jnp.take(moved, prompt_group, axis=0)
    return (gated_out, final_states)


def solution(mesh):
    in_specs = (
        P("req", "seq", None, None),
        P("req", "seq"),
        P(),
        P(),
        P(),
        P(),
        P(),
        P(),
        P(),
        P(),
    )
    out_specs = (P("req", "seq", None, None), P(None, "req", "seq", None))
    return jax.shard_map(local, mesh=mesh, in_specs=in_specs, out_specs=out_specs, check_vma=False)
```

```python
import jax
import jax.numpy as jnp
from jax import lax
from jax.experimental import pallas as pl
from jax.experimental.pallas import tpu as pltpu
from jax.sharding import PartitionSpec as P

BLOCK = 256


def shifted(block, axis, distance):
    devices = range(lax.axis_size(axis))
    route = [(i - distance, i) for i in devices if i - distance in devices]
    return lax.ppermute(block, axis, route)


def conv_kernel(x_ref, edge_ref, w_ref, b_ref, o_ref):
    x = x_ref[...].astype(jnp.float32)
    edge = edge_ref[...].astype(jnp.float32)
    w = w_ref[...]
    b = b_ref[...]
    taps = w.shape[1]
    acc = b + w[:, taps - 1 : taps] * x
    for tap in range(taps - 1):
        acc = acc + w[:, tap : tap + 1] * pltpu.roll(x, taps - 1 - tap, 1)
    o_ref[...] = (acc * (0.5 + 0.5 * jnp.tanh(0.5 * acc))).astype(o_ref.dtype)
    head = x[:, :128]
    lane = lax.broadcasted_iota(jnp.int32, head.shape, 1)
    first = b + w[:, taps - 1 : taps] * head
    for tap in range(taps - 1):
        lag = taps - 1 - tap
        moved = pltpu.roll(head, lag, 1)
        for t in range(lag):
            moved = jnp.where(lane == t, edge[:, tap + t : tap + t + 1], moved)
        first = first + w[:, tap : tap + 1] * moved
    o_ref[:, :128] = (first * (0.5 + 0.5 * jnp.tanh(0.5 * first))).astype(o_ref.dtype)


def conv_silu(conv_t, edge_t, weight_t, bias_t, rows=768):
    feats, slots = conv_t.shape
    taps = weight_t.shape[1]
    return pl.pallas_call(
        conv_kernel,
        grid=(feats // rows,),
        in_specs=[
            pl.BlockSpec((rows, slots), lambda i: (i, 0)),
            pl.BlockSpec((rows, taps - 1), lambda i: (i, 0)),
            pl.BlockSpec((rows, taps), lambda i: (i, 0)),
            pl.BlockSpec((rows, 1), lambda i: (i, 0)),
        ],
        out_specs=pl.BlockSpec((rows, slots), lambda i: (i, 0)),
        out_shape=jax.ShapeDtypeStruct((feats, slots), jnp.bfloat16),
        cost_estimate=pl.CostEstimate(
            flops=feats * slots * 14, transcendentals=feats * slots, bytes_accessed=feats * slots * 4
        ),
    )(conv_t, edge_t, weight_t, bias_t)


def norm_kernel(y_ref, z_ref, w_ref, mask_ref, o_ref):
    z = z_ref[...].astype(jnp.float32)
    gated = y_ref[...] * (z * (0.5 + 0.5 * jnp.tanh(0.5 * z)))
    mean = jnp.sum(gated * gated, axis=0, keepdims=True) * (1.0 / gated.shape[0])
    normed = gated * lax.rsqrt(mean + 1e-05) * w_ref[...]
    normed = jnp.where(mask_ref[...] > 0.5, normed, 0.0)
    o_ref[...] = normed.T.astype(o_ref.dtype)


def gate_norm(y_t, z_t, weight, mask, cols=128):
    units, slots = y_t.shape
    return pl.pallas_call(
        norm_kernel,
        grid=(slots // cols,),
        in_specs=[
            pl.BlockSpec((units, cols), lambda i: (0, i)),
            pl.BlockSpec((units, cols), lambda i: (0, i)),
            pl.BlockSpec((units, 1), lambda i: (0, 0)),
            pl.BlockSpec((1, cols), lambda i: (0, i)),
        ],
        out_specs=pl.BlockSpec((cols, units), lambda i: (i, 0)),
        out_shape=jax.ShapeDtypeStruct((slots, units), jnp.bfloat16),
        cost_estimate=pl.CostEstimate(
            flops=units * slots * 12, transcendentals=units * slots, bytes_accessed=units * slots * 8
        ),
    )(y_t, z_t, weight, mask)


def block_step(state, pieces):
    inputs_x, b_rows, c_rows, step_dt, log_decay = pieces
    length = inputs_x.shape[0]
    heads = step_dt.shape[1]
    hdim = inputs_x.shape[1] // heads
    running = jnp.cumsum(log_decay, axis=0)
    gram = jnp.einsum("tn,un->tu", c_rows, b_rows, preferred_element_type=jnp.float32)
    later = jnp.arange(length)[:, None] >= jnp.arange(length)[None, :]
    spread = running.T[:, :, None] - running.T[:, None, :]
    decay = jnp.where(later[None], jnp.exp(jnp.where(later[None], spread, 0.0)), 0.0)
    mixing = (gram[None] * decay * step_dt.T[:, None, :]).astype(jnp.bfloat16)
    heads_x = inputs_x.reshape(length, heads, hdim)
    inside = jnp.einsum("htu,uhp->thp", mixing, heads_x, preferred_element_type=jnp.float32)
    carried = jnp.exp(running)[:, :, None] * jnp.einsum(
        "tn,hpn->thp", c_rows.astype(jnp.float32), state, precision=lax.Precision.HIGHEST
    )
    final_log = running[-1]
    weighting = jnp.exp(final_log[None, :] - running) * step_dt
    weighted = (
        (heads_x.astype(jnp.float32) * weighting[:, :, None])
        .astype(jnp.bfloat16)
        .reshape(length, heads * hdim)
    )
    contrib = jnp.einsum("ud,un->dn", weighted, b_rows, preferred_element_type=jnp.float32).reshape(
        heads, hdim, -1
    )
    new_state = jnp.exp(final_log)[:, None, None] * state + contrib
    return (new_state, (inside + carried).reshape(length, heads * hdim))


def local(
    hidden, w_in, conv_weight, conv_bias, dt_bias, a_log, d_skip, norm_weight, lengths, prompt_group
):
    tok_rows = hidden[0, 0]
    slots = tok_rows.shape[0]
    inner = norm_weight.shape[0]
    heads = dt_bias.shape[0]
    hdim = inner // heads
    nstate = (conv_bias.shape[0] - inner) // 2
    convdim = conv_bias.shape[0]
    taps = conv_weight.shape[0]
    seq_count = lax.axis_size("seq")
    my_group = lax.axis_index("req")
    my_block = lax.axis_index("seq")
    qlen = jnp.sum(jnp.where(prompt_group == my_group, lengths, 0))
    filled = jnp.arange(slots, dtype=jnp.int32) < qlen
    column_blocks = [w_in]
    for distance in range(1, seq_count):
        cycle = [(i, (i + distance) % seq_count) for i in range(seq_count)]
        column_blocks.append(lax.ppermute(w_in, "seq", cycle))
    by_distance = jnp.stack(column_blocks)
    from_block = (my_block - jnp.arange(seq_count)) % seq_count
    in_order = jnp.take(by_distance, from_block, axis=0)
    wide_rows = jnp.transpose(in_order, (1, 0, 2)).reshape(w_in.shape[0], -1)
    projected = jnp.dot(
        tok_rows,
        lax.all_gather(wide_rows, "req", axis=0, tiled=True),
        preferred_element_type=jnp.float32,
    ).astype(jnp.bfloat16)
    gate_z = projected[:, :inner]
    conv_in = projected[:, inner : inner + convdim]
    dt_raw = projected[:, inner + convdim :]
    edge_rows = lax.dynamic_slice_in_dim(conv_in, qlen - (taps - 1), taps - 1, 0)
    prev_edge = shifted(edge_rows, "seq", 1)
    conv_act = conv_silu(conv_in.T, prev_edge.T, conv_weight.T, conv_bias[:, None]).T
    inputs_x = conv_act[:, :inner]
    b_rows = conv_act[:, inner : inner + nstate]
    c_rows = conv_act[:, inner + nstate :]
    step_dt = jnp.where(
        filled[:, None], jax.nn.softplus(dt_raw.astype(jnp.float32) + dt_bias[None, :]), 0.0
    )
    log_decay = step_dt * (-jnp.exp(a_log))[None, :]
    through = jnp.cumsum(log_decay, axis=0)
    block_total = through[-1]
    block_rows = min(BLOCK, slots)
    count = slots // block_rows
    pieces = (
        inputs_x.reshape(count, block_rows, inner),
        b_rows.reshape(count, block_rows, nstate),
        c_rows.reshape(count, block_rows, nstate),
        step_dt.reshape(count, block_rows, heads),
        log_decay.reshape(count, block_rows, heads),
    )
    zero_state = jnp.zeros((heads, hdim, nstate), jnp.float32)
    local_end = zero_state
    outs = []
    for index in range(count):
        local_end, out = block_step(local_end, tuple(piece[index] for piece in pieces))
        outs.append(out)
    outputs = jnp.concatenate(outs, axis=0)
    total_hi = lax.reduce_precision(block_total, exponent_bits=8, mantissa_bits=7)
    total_rest = block_total - total_hi
    total_mid = lax.reduce_precision(total_rest, exponent_bits=8, mantissa_bits=7)
    total_lo = total_rest - total_mid
    parts = jnp.stack([total_hi, total_mid, total_lo], axis=1).astype(jnp.bfloat16)
    parts = jnp.broadcast_to(parts[:, :, None], (heads, 3, 128))
    packed = jnp.concatenate(
        [local_end.reshape(heads, hdim * nstate).astype(jnp.bfloat16), parts.reshape(heads, 3 * 128)],
        axis=1,
    )
    gathered = lax.all_gather(packed, "seq", axis=0, tiled=False)
    ends = gathered[:, :, : hdim * nstate].astype(jnp.float32).reshape(seq_count, heads, hdim, nstate)
    sent = gathered[:, :, hdim * nstate :].astype(jnp.float32)
    totals = sent[:, :, 0] + (sent[:, :, 128] + sent[:, :, 256])
    entering = zero_state
    for turn in range(seq_count - 1):
        stepped = jnp.exp(totals[turn])[:, None, None] * entering + ends[turn]
        entering = jnp.where(turn < my_block, stepped, entering)
    incoming = jnp.exp(through)[:, :, None] * jnp.einsum(
        "tn,hpn->thp", c_rows.astype(jnp.float32), entering, precision=lax.Precision.HIGHEST
    )
    heads_y = (
        outputs.reshape(slots, heads, hdim)
        + incoming
        + d_skip[None, :, None] * inputs_x.astype(jnp.float32).reshape(slots, heads, hdim)
    )
    gated_out = gate_norm(
        heads_y.reshape(slots, inner).T,
        gate_z.T,
        norm_weight[:, None],
        filled.astype(jnp.float32)[None, :],
    ).reshape(1, 1, slots, inner)
    later_mask = jnp.arange(seq_count)[None, :] > jnp.arange(seq_count)[:, None]
    after = jnp.sum(jnp.where(later_mask[:, :, None], totals[None, :, :], 0.0), axis=1)
    piece = hdim // seq_count
    own_ends = lax.dynamic_slice_in_dim(ends, my_block * piece, piece, axis=2)
    share = jnp.sum(jnp.exp(after)[:, :, None, None] * own_ends, axis=0)
    moved = lax.all_to_all(share[None], "req", split_axis=1, concat_axis=0, tiled=True)
    final_states = jnp.take(moved, prompt_group, axis=0)
    return (gated_out, final_states)


def solution(mesh):
    in_specs = (
        P("req", "seq", None, None),
        P("req", "seq"),
        P(),
        P(),
        P(),
        P(),
        P(),
        P(),
        P(),
        P(),
    )
    out_specs = (P("req", "seq", None, None), P(None, "req", "seq", None))
    return jax.shard_map(local, mesh=mesh, in_specs=in_specs, out_specs=out_specs, check_vma=False)
```

```python
import jax
import jax.numpy as jnp
from jax import lax
from jax.experimental import pallas as pl
from jax.experimental.pallas import tpu as pltpu
from jax.sharding import PartitionSpec as P

BLOCK = 256


def shifted(block, axis, distance):
    devices = range(lax.axis_size(axis))
    route = [(i - distance, i) for i in devices if i - distance in devices]
    return lax.ppermute(block, axis, route)


def conv_kernel(x_ref, edge_ref, w_ref, b_ref, o_ref):
    x = x_ref[...].astype(jnp.float32)
    edge = edge_ref[...].astype(jnp.float32)
    w = w_ref[...]
    b = b_ref[...]
    taps = w.shape[1]
    acc = b + w[:, taps - 1 : taps] * x
    for tap in range(taps - 1):
        acc = acc + w[:, tap : tap + 1] * pltpu.roll(x, taps - 1 - tap, 1)
    o_ref[...] = (acc * (0.5 + 0.5 * jnp.tanh(0.5 * acc))).astype(o_ref.dtype)
    head = x[:, :128]
    lane = lax.broadcasted_iota(jnp.int32, head.shape, 1)
    first = b + w[:, taps - 1 : taps] * head
    for tap in range(taps - 1):
        lag = taps - 1 - tap
        moved = pltpu.roll(head, lag, 1)
        for t in range(lag):
            moved = jnp.where(lane == t, edge[:, tap + t : tap + t + 1], moved)
        first = first + w[:, tap : tap + 1] * moved
    o_ref[:, :128] = (first * (0.5 + 0.5 * jnp.tanh(0.5 * first))).astype(o_ref.dtype)


def conv_silu(conv_t, edge_t, weight_t, bias_t, rows=768):
    feats, slots = conv_t.shape
    taps = weight_t.shape[1]
    return pl.pallas_call(
        conv_kernel,
        grid=(feats // rows,),
        in_specs=[
            pl.BlockSpec((rows, slots), lambda i: (i, 0)),
            pl.BlockSpec((rows, taps - 1), lambda i: (i, 0)),
            pl.BlockSpec((rows, taps), lambda i: (i, 0)),
            pl.BlockSpec((rows, 1), lambda i: (i, 0)),
        ],
        out_specs=pl.BlockSpec((rows, slots), lambda i: (i, 0)),
        out_shape=jax.ShapeDtypeStruct((feats, slots), jnp.bfloat16),
        cost_estimate=pl.CostEstimate(
            flops=feats * slots * 14, transcendentals=feats * slots, bytes_accessed=feats * slots * 4
        ),
    )(conv_t, edge_t, weight_t, bias_t)


def norm_kernel(y_ref, z_ref, w_ref, mask_ref, o_ref):
    z = z_ref[...].astype(jnp.float32)
    gated = y_ref[...] * (z * (0.5 + 0.5 * jnp.tanh(0.5 * z)))
    mean = jnp.sum(gated * gated, axis=0, keepdims=True) * (1.0 / gated.shape[0])
    normed = gated * lax.rsqrt(mean + 1e-05) * w_ref[...]
    normed = jnp.where(mask_ref[...] > 0.5, normed, 0.0)
    o_ref[...] = normed.T.astype(o_ref.dtype)


def gate_norm(y_t, z_t, weight, mask, cols=128):
    units, slots = y_t.shape
    return pl.pallas_call(
        norm_kernel,
        grid=(slots // cols,),
        in_specs=[
            pl.BlockSpec((units, cols), lambda i: (0, i)),
            pl.BlockSpec((units, cols), lambda i: (0, i)),
            pl.BlockSpec((units, 1), lambda i: (0, 0)),
            pl.BlockSpec((1, cols), lambda i: (0, i)),
        ],
        out_specs=pl.BlockSpec((cols, units), lambda i: (i, 0)),
        out_shape=jax.ShapeDtypeStruct((slots, units), jnp.bfloat16),
        cost_estimate=pl.CostEstimate(
            flops=units * slots * 12, transcendentals=units * slots, bytes_accessed=units * slots * 8
        ),
    )(y_t, z_t, weight, mask)


def block_step(state, pieces):
    inputs_x, b_rows, c_rows, step_dt, log_decay = pieces
    length = inputs_x.shape[0]
    heads = step_dt.shape[1]
    hdim = inputs_x.shape[1] // heads
    running = jnp.cumsum(log_decay, axis=0)
    gram = jnp.einsum("tn,un->tu", c_rows, b_rows, preferred_element_type=jnp.float32)
    later = jnp.arange(length)[:, None] >= jnp.arange(length)[None, :]
    spread = running.T[:, :, None] - running.T[:, None, :]
    decay = jnp.where(later[None], jnp.exp(jnp.where(later[None], spread, 0.0)), 0.0)
    mixing = (gram[None] * decay * step_dt.T[:, None, :]).astype(jnp.bfloat16)
    heads_x = inputs_x.reshape(length, heads, hdim)
    inside = jnp.einsum("htu,uhp->thp", mixing, heads_x, preferred_element_type=jnp.float32)
    carried = jnp.exp(running)[:, :, None] * jnp.einsum(
        "tn,hpn->thp", c_rows.astype(jnp.float32), state, precision=lax.Precision.HIGHEST
    )
    final_log = running[-1]
    weighting = jnp.exp(final_log[None, :] - running) * step_dt
    weighted = (
        (heads_x.astype(jnp.float32) * weighting[:, :, None])
        .astype(jnp.bfloat16)
        .reshape(length, heads * hdim)
    )
    contrib = jnp.einsum("ud,un->dn", weighted, b_rows, preferred_element_type=jnp.float32).reshape(
        heads, hdim, -1
    )
    new_state = jnp.exp(final_log)[:, None, None] * state + contrib
    return (new_state, (inside + carried).reshape(length, heads * hdim))


def local(
    hidden, w_in, conv_weight, conv_bias, dt_bias, a_log, d_skip, norm_weight, lengths, prompt_group
):
    tok_rows = hidden[0, 0]
    slots = tok_rows.shape[0]
    inner = norm_weight.shape[0]
    heads = dt_bias.shape[0]
    hdim = inner // heads
    nstate = (conv_bias.shape[0] - inner) // 2
    convdim = conv_bias.shape[0]
    taps = conv_weight.shape[0]
    seq_count = lax.axis_size("seq")
    my_group = lax.axis_index("req")
    my_block = lax.axis_index("seq")
    qlen = jnp.sum(jnp.where(prompt_group == my_group, lengths, 0))
    filled = jnp.arange(slots, dtype=jnp.int32) < qlen
    column_blocks = [w_in]
    for distance in range(1, seq_count):
        cycle = [(i, (i + distance) % seq_count) for i in range(seq_count)]
        column_blocks.append(lax.ppermute(w_in, "seq", cycle))
    ordered = []
    for block in range(seq_count):
        distance_of = (my_block - block) % seq_count
        chosen = column_blocks[0]
        for distance in range(1, seq_count):
            chosen = jnp.where(distance_of == distance, column_blocks[distance], chosen)
        ordered.append(chosen)
    wide_rows = jnp.concatenate(ordered, axis=1)
    projected = jnp.dot(
        tok_rows,
        lax.all_gather(wide_rows, "req", axis=0, tiled=True),
        preferred_element_type=jnp.float32,
    ).astype(jnp.bfloat16)
    gate_z = projected[:, :inner]
    conv_in = projected[:, inner : inner + convdim]
    dt_raw = projected[:, inner + convdim :]
    edge_rows = lax.dynamic_slice_in_dim(conv_in, qlen - (taps - 1), taps - 1, 0)
    prev_edge = shifted(edge_rows, "seq", 1)
    conv_act = conv_silu(conv_in.T, prev_edge.T, conv_weight.T, conv_bias[:, None]).T
    inputs_x = conv_act[:, :inner]
    b_rows = conv_act[:, inner : inner + nstate]
    c_rows = conv_act[:, inner + nstate :]
    step_dt = jnp.where(
        filled[:, None], jax.nn.softplus(dt_raw.astype(jnp.float32) + dt_bias[None, :]), 0.0
    )
    log_decay = step_dt * (-jnp.exp(a_log))[None, :]
    through = jnp.cumsum(log_decay, axis=0)
    block_total = through[-1]
    block_rows = min(BLOCK, slots)
    count = slots // block_rows
    pieces = (
        inputs_x.reshape(count, block_rows, inner),
        b_rows.reshape(count, block_rows, nstate),
        c_rows.reshape(count, block_rows, nstate),
        step_dt.reshape(count, block_rows, heads),
        log_decay.reshape(count, block_rows, heads),
    )
    zero_state = jnp.zeros((heads, hdim, nstate), jnp.float32)
    local_end = zero_state
    outs = []
    for index in range(count):
        local_end, out = block_step(local_end, tuple(piece[index] for piece in pieces))
        outs.append(out)
    outputs = jnp.concatenate(outs, axis=0)
    total_hi = lax.reduce_precision(block_total, exponent_bits=8, mantissa_bits=7)
    total_rest = block_total - total_hi
    total_mid = lax.reduce_precision(total_rest, exponent_bits=8, mantissa_bits=7)
    total_lo = total_rest - total_mid
    parts = jnp.stack([total_hi, total_mid, total_lo], axis=1).astype(jnp.bfloat16)
    parts = jnp.broadcast_to(parts[:, :, None], (heads, 3, 128))
    packed = jnp.concatenate(
        [local_end.reshape(heads, hdim * nstate).astype(jnp.bfloat16), parts.reshape(heads, 3 * 128)],
        axis=1,
    )
    gathered = lax.all_gather(packed, "seq", axis=0, tiled=False)
    ends = gathered[:, :, : hdim * nstate].astype(jnp.float32).reshape(seq_count, heads, hdim, nstate)
    sent = gathered[:, :, hdim * nstate :].astype(jnp.float32)
    totals = sent[:, :, 0] + (sent[:, :, 128] + sent[:, :, 256])
    entering = zero_state
    for turn in range(seq_count - 1):
        stepped = jnp.exp(totals[turn])[:, None, None] * entering + ends[turn]
        entering = jnp.where(turn < my_block, stepped, entering)
    incoming = jnp.exp(through)[:, :, None] * jnp.einsum(
        "tn,hpn->thp", c_rows.astype(jnp.float32), entering, precision=lax.Precision.HIGHEST
    )
    heads_y = (
        outputs.reshape(slots, heads, hdim)
        + incoming
        + d_skip[None, :, None] * inputs_x.astype(jnp.float32).reshape(slots, heads, hdim)
    )
    gated_out = gate_norm(
        heads_y.reshape(slots, inner).T,
        gate_z.T,
        norm_weight[:, None],
        filled.astype(jnp.float32)[None, :],
    ).reshape(1, 1, slots, inner)
    later_mask = jnp.arange(seq_count)[None, :] > jnp.arange(seq_count)[:, None]
    after = jnp.sum(jnp.where(later_mask[:, :, None], totals[None, :, :], 0.0), axis=1)
    piece = hdim // seq_count
    own_ends = lax.dynamic_slice_in_dim(ends, my_block * piece, piece, axis=2)
    share = jnp.sum(jnp.exp(after)[:, :, None, None] * own_ends, axis=0)
    moved = lax.all_to_all(share[None], "req", split_axis=1, concat_axis=0, tiled=True)
    final_states = jnp.take(moved, prompt_group, axis=0)
    return (gated_out, final_states)


def solution(mesh):
    in_specs = (
        P("req", "seq", None, None),
        P("req", "seq"),
        P(),
        P(),
        P(),
        P(),
        P(),
        P(),
        P(),
        P(),
    )
    out_specs = (P("req", "seq", None, None), P(None, "req", "seq", None))
    return jax.shard_map(local, mesh=mesh, in_specs=in_specs, out_specs=out_specs, check_vma=False)
```

```python
import jax
import jax.numpy as jnp
from jax import lax
from jax.experimental import pallas as pl
from jax.experimental.pallas import tpu as pltpu
from jax.sharding import PartitionSpec as P

BLOCK = 256


def shifted(block, axis, distance):
    devices = range(lax.axis_size(axis))
    route = [(i - distance, i) for i in devices if i - distance in devices]
    return lax.ppermute(block, axis, route)


def conv_kernel(x_ref, edge_ref, w_ref, b_ref, o_ref):
    x = x_ref[...].astype(jnp.float32)
    edge = edge_ref[...].astype(jnp.float32)
    w = w_ref[...]
    b = b_ref[...]
    taps = w.shape[1]
    acc = b + w[:, taps - 1 : taps] * x
    for tap in range(taps - 1):
        acc = acc + w[:, tap : tap + 1] * pltpu.roll(x, taps - 1 - tap, 1)
    o_ref[...] = (acc * (0.5 + 0.5 * jnp.tanh(0.5 * acc))).astype(o_ref.dtype)
    head = x[:, :128]
    lane = lax.broadcasted_iota(jnp.int32, head.shape, 1)
    first = b + w[:, taps - 1 : taps] * head
    for tap in range(taps - 1):
        lag = taps - 1 - tap
        moved = pltpu.roll(head, lag, 1)
        for t in range(lag):
            moved = jnp.where(lane == t, edge[:, tap + t : tap + t + 1], moved)
        first = first + w[:, tap : tap + 1] * moved
    o_ref[:, :128] = (first * (0.5 + 0.5 * jnp.tanh(0.5 * first))).astype(o_ref.dtype)


def conv_silu(conv_t, edge_t, weight_t, bias_t, rows=768):
    feats, slots = conv_t.shape
    taps = weight_t.shape[1]
    return pl.pallas_call(
        conv_kernel,
        grid=(feats // rows,),
        in_specs=[
            pl.BlockSpec((rows, slots), lambda i: (i, 0)),
            pl.BlockSpec((rows, taps - 1), lambda i: (i, 0)),
            pl.BlockSpec((rows, taps), lambda i: (i, 0)),
            pl.BlockSpec((rows, 1), lambda i: (i, 0)),
        ],
        out_specs=pl.BlockSpec((rows, slots), lambda i: (i, 0)),
        out_shape=jax.ShapeDtypeStruct((feats, slots), jnp.bfloat16),
        cost_estimate=pl.CostEstimate(
            flops=feats * slots * 14, transcendentals=feats * slots, bytes_accessed=feats * slots * 4
        ),
    )(conv_t, edge_t, weight_t, bias_t)


def norm_kernel(y_ref, z_ref, w_ref, mask_ref, o_ref):
    z = z_ref[...].astype(jnp.float32)
    gated = y_ref[...] * (z * (0.5 + 0.5 * jnp.tanh(0.5 * z)))
    mean = jnp.sum(gated * gated, axis=0, keepdims=True) * (1.0 / gated.shape[0])
    normed = gated * lax.rsqrt(mean + 1e-05) * w_ref[...]
    normed = jnp.where(mask_ref[...] > 0.5, normed, 0.0)
    o_ref[...] = normed.T.astype(o_ref.dtype)


def gate_norm(y_t, z_t, weight, mask, cols=128):
    units, slots = y_t.shape
    return pl.pallas_call(
        norm_kernel,
        grid=(slots // cols,),
        in_specs=[
            pl.BlockSpec((units, cols), lambda i: (0, i)),
            pl.BlockSpec((units, cols), lambda i: (0, i)),
            pl.BlockSpec((units, 1), lambda i: (0, 0)),
            pl.BlockSpec((1, cols), lambda i: (0, i)),
        ],
        out_specs=pl.BlockSpec((cols, units), lambda i: (i, 0)),
        out_shape=jax.ShapeDtypeStruct((slots, units), jnp.bfloat16),
        cost_estimate=pl.CostEstimate(
            flops=units * slots * 12, transcendentals=units * slots, bytes_accessed=units * slots * 8
        ),
    )(y_t, z_t, weight, mask)


def block_step(state, pieces):
    inputs_x, b_rows, c_rows, step_dt, log_decay = pieces
    length = inputs_x.shape[0]
    heads = step_dt.shape[1]
    hdim = inputs_x.shape[1] // heads
    running = jnp.cumsum(log_decay, axis=0)
    gram = jnp.einsum("tn,un->tu", c_rows, b_rows, preferred_element_type=jnp.float32)
    later = jnp.arange(length)[:, None] >= jnp.arange(length)[None, :]
    spread = running.T[:, :, None] - running.T[:, None, :]
    decay = jnp.where(later[None], jnp.exp(jnp.where(later[None], spread, 0.0)), 0.0)
    mixing = (gram[None] * decay * step_dt.T[:, None, :]).astype(jnp.bfloat16)
    heads_x = inputs_x.reshape(length, heads, hdim)
    inside = jnp.einsum("htu,uhp->thp", mixing, heads_x, preferred_element_type=jnp.float32)
    carried = jnp.exp(running)[:, :, None] * jnp.einsum(
        "tn,hpn->thp", c_rows.astype(jnp.float32), state, precision=lax.Precision.HIGHEST
    )
    final_log = running[-1]
    weighting = jnp.exp(final_log[None, :] - running) * step_dt
    weighted = (
        (heads_x.astype(jnp.float32) * weighting[:, :, None])
        .astype(jnp.bfloat16)
        .reshape(length, heads * hdim)
    )
    contrib = jnp.einsum("ud,un->dn", weighted, b_rows, preferred_element_type=jnp.float32).reshape(
        heads, hdim, -1
    )
    new_state = jnp.exp(final_log)[:, None, None] * state + contrib
    return (new_state, (inside + carried).reshape(length, heads * hdim))


def local(
    hidden, w_in, conv_weight, conv_bias, dt_bias, a_log, d_skip, norm_weight, lengths, prompt_group
):
    tok_rows = hidden[0, 0]
    slots = tok_rows.shape[0]
    inner = norm_weight.shape[0]
    heads = dt_bias.shape[0]
    hdim = inner // heads
    nstate = (conv_bias.shape[0] - inner) // 2
    convdim = conv_bias.shape[0]
    taps = conv_weight.shape[0]
    seq_count = lax.axis_size("seq")
    my_group = lax.axis_index("req")
    my_block = lax.axis_index("seq")
    qlen = jnp.sum(jnp.where(prompt_group == my_group, lengths, 0))
    filled = jnp.arange(slots, dtype=jnp.int32) < qlen
    column_blocks = [w_in]
    for distance in range(1, seq_count):
        cycle = [(i, (i + distance) % seq_count) for i in range(seq_count)]
        column_blocks.append(lax.ppermute(w_in, "seq", cycle))
    by_distance = jnp.stack(column_blocks)
    from_block = (my_block - jnp.arange(seq_count)) % seq_count
    in_order = jnp.take(by_distance, from_block, axis=0)
    wide_rows = jnp.transpose(in_order, (1, 0, 2)).reshape(w_in.shape[0], -1)
    projected = jnp.dot(
        tok_rows,
        lax.all_gather(wide_rows, "req", axis=0, tiled=True),
        preferred_element_type=jnp.float32,
    ).astype(jnp.bfloat16)
    gate_z = projected[:, :inner]
    conv_in = projected[:, inner : inner + convdim]
    dt_raw = projected[:, inner + convdim :]
    edge_rows = lax.dynamic_slice_in_dim(conv_in, qlen - (taps - 1), taps - 1, 0)
    prev_edge = shifted(edge_rows, "seq", 1)
    conv_act = conv_silu(conv_in.T, prev_edge.T, conv_weight.T, conv_bias[:, None]).T
    inputs_x = conv_act[:, :inner]
    b_rows = conv_act[:, inner : inner + nstate]
    c_rows = conv_act[:, inner + nstate :]
    step_dt = jnp.where(
        filled[:, None], jax.nn.softplus(dt_raw.astype(jnp.float32) + dt_bias[None, :]), 0.0
    )
    log_decay = step_dt * (-jnp.exp(a_log))[None, :]
    through = jnp.cumsum(log_decay, axis=0)
    block_total = through[-1]
    block_rows = min(BLOCK, slots)
    count = slots // block_rows
    pieces = (
        inputs_x.reshape(count, block_rows, inner),
        b_rows.reshape(count, block_rows, nstate),
        c_rows.reshape(count, block_rows, nstate),
        step_dt.reshape(count, block_rows, heads),
        log_decay.reshape(count, block_rows, heads),
    )
    zero_state = jnp.zeros((heads, hdim, nstate), jnp.float32)
    local_end = zero_state
    outs = []
    for index in range(count):
        local_end, out = block_step(local_end, tuple(piece[index] for piece in pieces))
        outs.append(out)
    outputs = jnp.concatenate(outs, axis=0)
    total_hi = lax.reduce_precision(block_total, exponent_bits=8, mantissa_bits=7)
    total_rest = block_total - total_hi
    total_mid = lax.reduce_precision(total_rest, exponent_bits=8, mantissa_bits=7)
    total_lo = total_rest - total_mid
    parts = jnp.stack([total_hi, total_mid, total_lo], axis=1).astype(jnp.bfloat16)
    parts = jnp.broadcast_to(parts[:, :, None], (heads, 3, 128))
    packed = jnp.concatenate(
        [local_end.reshape(heads, hdim * nstate).astype(jnp.bfloat16), parts.reshape(heads, 3 * 128)],
        axis=1,
    )
    gathered = lax.all_gather(packed, "seq", axis=0, tiled=False)
    ends = gathered[:, :, : hdim * nstate].astype(jnp.float32).reshape(seq_count, heads, hdim, nstate)
    sent = gathered[:, :, hdim * nstate :].astype(jnp.float32)
    totals = sent[:, :, 0] + (sent[:, :, 128] + sent[:, :, 256])
    entering = zero_state
    for turn in range(seq_count - 1):
        stepped = jnp.exp(totals[turn])[:, None, None] * entering + ends[turn]
        entering = jnp.where(turn < my_block, stepped, entering)
    incoming = jnp.exp(through)[:, :, None] * jnp.einsum(
        "tn,hpn->thp", c_rows.astype(jnp.float32), entering, precision=lax.Precision.HIGHEST
    )
    heads_y = (
        outputs.reshape(slots, heads, hdim)
        + incoming
        + d_skip[None, :, None] * inputs_x.astype(jnp.float32).reshape(slots, heads, hdim)
    )
    gated_out = gate_norm(
        heads_y.reshape(slots, inner).T,
        gate_z.T,
        norm_weight[:, None],
        filled.astype(jnp.float32)[None, :],
    ).reshape(1, 1, slots, inner)
    later_mask = jnp.arange(seq_count)[None, :] > jnp.arange(seq_count)[:, None]
    after = jnp.sum(jnp.where(later_mask[:, :, None], totals[None, :, :], 0.0), axis=1)
    piece = hdim // seq_count
    own_ends = lax.dynamic_slice_in_dim(ends, my_block * piece, piece, axis=2)
    share = jnp.sum(jnp.exp(after)[:, :, None, None] * own_ends, axis=0)
    moved = lax.all_to_all(share[None], "req", split_axis=1, concat_axis=0, tiled=True)
    pick = (prompt_group[:, None] == jnp.arange(moved.shape[0])[None, :]).astype(jnp.float32)
    final_states = jnp.einsum(
        "pg,gabc->pabc", pick, moved, precision=lax.Precision.HIGHEST
    )
    return (gated_out, final_states)


def solution(mesh):
    in_specs = (
        P("req", "seq", None, None),
        P("req", "seq"),
        P(),
        P(),
        P(),
        P(),
        P(),
        P(),
        P(),
        P(),
    )
    out_specs = (P("req", "seq", None, None), P(None, "req", "seq", None))
    return jax.shard_map(local, mesh=mesh, in_specs=in_specs, out_specs=out_specs, check_vma=False)
```

```python
import jax
import jax.numpy as jnp
from jax import lax
from jax.experimental import pallas as pl
from jax.experimental.pallas import tpu as pltpu
from jax.sharding import PartitionSpec as P

BLOCK = 256


def shifted(block, axis, distance):
    devices = range(lax.axis_size(axis))
    route = [(i - distance, i) for i in devices if i - distance in devices]
    return lax.ppermute(block, axis, route)


def conv_kernel(x_ref, edge_ref, w_ref, b_ref, o_ref):
    x = x_ref[...].astype(jnp.float32)
    edge = edge_ref[...].astype(jnp.float32)
    w = w_ref[...]
    b = b_ref[...]
    taps = w.shape[1]
    acc = b + w[:, taps - 1 : taps] * x
    for tap in range(taps - 1):
        acc = acc + w[:, tap : tap + 1] * pltpu.roll(x, taps - 1 - tap, 1)
    o_ref[...] = (acc * (0.5 + 0.5 * jnp.tanh(0.5 * acc))).astype(o_ref.dtype)
    head = x[:, :128]
    lane = lax.broadcasted_iota(jnp.int32, head.shape, 1)
    first = b + w[:, taps - 1 : taps] * head
    for tap in range(taps - 1):
        lag = taps - 1 - tap
        moved = pltpu.roll(head, lag, 1)
        for t in range(lag):
            moved = jnp.where(lane == t, edge[:, tap + t : tap + t + 1], moved)
        first = first + w[:, tap : tap + 1] * moved
    o_ref[:, :128] = (first * (0.5 + 0.5 * jnp.tanh(0.5 * first))).astype(o_ref.dtype)


def conv_silu(conv_t, edge_t, weight_t, bias_t, rows=768):
    feats, slots = conv_t.shape
    taps = weight_t.shape[1]
    return pl.pallas_call(
        conv_kernel,
        grid=(feats // rows,),
        in_specs=[
            pl.BlockSpec((rows, slots), lambda i: (i, 0)),
            pl.BlockSpec((rows, taps - 1), lambda i: (i, 0)),
            pl.BlockSpec((rows, taps), lambda i: (i, 0)),
            pl.BlockSpec((rows, 1), lambda i: (i, 0)),
        ],
        out_specs=pl.BlockSpec((rows, slots), lambda i: (i, 0)),
        out_shape=jax.ShapeDtypeStruct((feats, slots), jnp.bfloat16),
        cost_estimate=pl.CostEstimate(
            flops=feats * slots * 14, transcendentals=feats * slots, bytes_accessed=feats * slots * 4
        ),
    )(conv_t, edge_t, weight_t, bias_t)


def norm_kernel(y_ref, z_ref, w_ref, mask_ref, o_ref):
    z = z_ref[...].astype(jnp.float32)
    gated = y_ref[...] * (z * (0.5 + 0.5 * jnp.tanh(0.5 * z)))
    mean = jnp.sum(gated * gated, axis=0, keepdims=True) * (1.0 / gated.shape[0])
    normed = gated * lax.rsqrt(mean + 1e-05) * w_ref[...]
    normed = jnp.where(mask_ref[...] > 0.5, normed, 0.0)
    o_ref[...] = normed.T.astype(o_ref.dtype)


def gate_norm(y_t, z_t, weight, mask, cols=128):
    units, slots = y_t.shape
    return pl.pallas_call(
        norm_kernel,
        grid=(slots // cols,),
        in_specs=[
            pl.BlockSpec((units, cols), lambda i: (0, i)),
            pl.BlockSpec((units, cols), lambda i: (0, i)),
            pl.BlockSpec((units, 1), lambda i: (0, 0)),
            pl.BlockSpec((1, cols), lambda i: (0, i)),
        ],
        out_specs=pl.BlockSpec((cols, units), lambda i: (i, 0)),
        out_shape=jax.ShapeDtypeStruct((slots, units), jnp.bfloat16),
        cost_estimate=pl.CostEstimate(
            flops=units * slots * 12, transcendentals=units * slots, bytes_accessed=units * slots * 8
        ),
    )(y_t, z_t, weight, mask)


def block_step(state, pieces):
    inputs_x, b_rows, c_rows, step_dt, log_decay = pieces
    length = inputs_x.shape[0]
    heads = step_dt.shape[1]
    hdim = inputs_x.shape[1] // heads
    running = jnp.cumsum(log_decay, axis=0)
    gram = jnp.einsum("tn,un->tu", c_rows, b_rows, preferred_element_type=jnp.float32)
    later = jnp.arange(length)[:, None] >= jnp.arange(length)[None, :]
    spread = running.T[:, :, None] - running.T[:, None, :]
    decay = jnp.where(later[None], jnp.exp(jnp.where(later[None], spread, 0.0)), 0.0)
    mixing = (gram[None] * decay * step_dt.T[:, None, :]).astype(jnp.bfloat16)
    heads_x = inputs_x.reshape(length, heads, hdim)
    inside = jnp.einsum("htu,uhp->thp", mixing, heads_x, preferred_element_type=jnp.float32)
    carried = jnp.exp(running)[:, :, None] * jnp.einsum(
        "tn,hpn->thp", c_rows.astype(jnp.float32), state, precision=lax.Precision.HIGHEST
    )
    final_log = running[-1]
    weighting = jnp.exp(final_log[None, :] - running) * step_dt
    weighted = (
        (heads_x.astype(jnp.float32) * weighting[:, :, None])
        .astype(jnp.bfloat16)
        .reshape(length, heads * hdim)
    )
    contrib = jnp.einsum("ud,un->dn", weighted, b_rows, preferred_element_type=jnp.float32).reshape(
        heads, hdim, -1
    )
    new_state = jnp.exp(final_log)[:, None, None] * state + contrib
    return (new_state, (inside + carried).reshape(length, heads * hdim))


def local(
    hidden, w_in, conv_weight, conv_bias, dt_bias, a_log, d_skip, norm_weight, lengths, prompt_group
):
    tok_rows = hidden[0, 0]
    slots = tok_rows.shape[0]
    inner = norm_weight.shape[0]
    heads = dt_bias.shape[0]
    hdim = inner // heads
    nstate = (conv_bias.shape[0] - inner) // 2
    convdim = conv_bias.shape[0]
    taps = conv_weight.shape[0]
    seq_count = lax.axis_size("seq")
    my_group = lax.axis_index("req")
    my_block = lax.axis_index("seq")
    qlen = jnp.sum(jnp.where(prompt_group == my_group, lengths, 0))
    filled = jnp.arange(slots, dtype=jnp.int32) < qlen
    column_blocks = [w_in]
    for distance in range(1, seq_count):
        cycle = [(i, (i + distance) % seq_count) for i in range(seq_count)]
        column_blocks.append(lax.ppermute(w_in, "seq", cycle))
    by_distance = jnp.stack(column_blocks)
    from_block = (my_block - jnp.arange(seq_count)) % seq_count
    in_order = jnp.take(by_distance, from_block, axis=0)
    wide_rows = jnp.transpose(in_order, (1, 0, 2)).reshape(w_in.shape[0], -1)
    projected = jnp.dot(
        tok_rows,
        lax.all_gather(wide_rows, "req", axis=0, tiled=True),
        preferred_element_type=jnp.float32,
    ).astype(jnp.bfloat16)
    gate_z = projected[:, :inner]
    conv_in = projected[:, inner : inner + convdim]
    dt_raw = projected[:, inner + convdim :]
    edge_rows = lax.dynamic_slice_in_dim(conv_in, qlen - (taps - 1), taps - 1, 0)
    prev_edge = shifted(edge_rows, "seq", 1)
    conv_act = conv_silu(conv_in.T, prev_edge.T, conv_weight.T, conv_bias[:, None]).T
    inputs_x = conv_act[:, :inner]
    b_rows = conv_act[:, inner : inner + nstate]
    c_rows = conv_act[:, inner + nstate :]
    step_dt = jnp.where(
        filled[:, None], jax.nn.softplus(dt_raw.astype(jnp.float32) + dt_bias[None, :]), 0.0
    )
    log_decay = step_dt * (-jnp.exp(a_log))[None, :]
    through = jnp.cumsum(log_decay, axis=0)
    block_total = through[-1]
    block_rows = min(BLOCK, slots)
    count = slots // block_rows
    pieces = (
        inputs_x.reshape(count, block_rows, inner),
        b_rows.reshape(count, block_rows, nstate),
        c_rows.reshape(count, block_rows, nstate),
        step_dt.reshape(count, block_rows, heads),
        log_decay.reshape(count, block_rows, heads),
    )
    zero_state = jnp.zeros((heads, hdim, nstate), jnp.float32)
    local_end = zero_state
    outs = []
    for index in range(count):
        local_end, out = block_step(local_end, tuple(piece[index] for piece in pieces))
        outs.append(out)
    outputs = jnp.concatenate(outs, axis=0)
    total_hi = lax.reduce_precision(block_total, exponent_bits=8, mantissa_bits=7)
    total_rest = block_total - total_hi
    total_mid = lax.reduce_precision(total_rest, exponent_bits=8, mantissa_bits=7)
    total_lo = total_rest - total_mid
    parts = jnp.stack([total_hi, total_mid, total_lo], axis=1).astype(jnp.bfloat16)
    parts = jnp.broadcast_to(parts[:, :, None], (heads, 3, 128))
    packed = jnp.concatenate(
        [local_end.reshape(heads, hdim * nstate).astype(jnp.bfloat16), parts.reshape(heads, 3 * 128)],
        axis=1,
    )
    piece = hdim // seq_count
    slices = local_end.reshape(heads, seq_count, piece, nstate)
    own_total = jnp.broadcast_to(block_total[:, None, None, None], (heads, seq_count, 1, nstate))
    payload = jnp.concatenate([slices, own_total], axis=2).reshape(heads * seq_count, piece + 1, nstate)
    received = lax.all_to_all(payload, ("req", "seq"), split_axis=0, concat_axis=0, tiled=True)
    received = received.reshape(-1, seq_count, piece + 1, nstate)
    group_totals = received[:, :, piece, 0]
    later_mask = jnp.arange(seq_count)[None, :] > jnp.arange(seq_count)[:, None]
    group_after = jnp.sum(
        jnp.where(later_mask[None, :, :], group_totals[:, None, :], 0.0), axis=2
    )
    group_final = jnp.sum(jnp.exp(group_after)[:, :, None, None] * received[:, :, :piece, :], axis=1)
    gathered = lax.all_gather(packed, "seq", axis=0, tiled=False)
    ends = gathered[:, :, : hdim * nstate].astype(jnp.float32).reshape(seq_count, heads, hdim, nstate)
    sent = gathered[:, :, hdim * nstate :].astype(jnp.float32)
    totals = sent[:, :, 0] + (sent[:, :, 128] + sent[:, :, 256])
    entering = zero_state
    for turn in range(seq_count - 1):
        stepped = jnp.exp(totals[turn])[:, None, None] * entering + ends[turn]
        entering = jnp.where(turn < my_block, stepped, entering)
    incoming = jnp.exp(through)[:, :, None] * jnp.einsum(
        "tn,hpn->thp", c_rows.astype(jnp.float32), entering, precision=lax.Precision.HIGHEST
    )
    heads_y = (
        outputs.reshape(slots, heads, hdim)
        + incoming
        + d_skip[None, :, None] * inputs_x.astype(jnp.float32).reshape(slots, heads, hdim)
    )
    gated_out = gate_norm(
        heads_y.reshape(slots, inner).T,
        gate_z.T,
        norm_weight[:, None],
        filled.astype(jnp.float32)[None, :],
    ).reshape(1, 1, slots, inner)
    pick = (prompt_group[:, None] == jnp.arange(group_final.shape[0])[None, :]).astype(jnp.float32)
    final_states = jnp.einsum(
        "pg,gbc->pbc", pick, group_final, precision=lax.Precision.HIGHEST
    )[:, None]
    return (gated_out, final_states)


def solution(mesh):
    in_specs = (
        P("req", "seq", None, None),
        P("req", "seq"),
        P(),
        P(),
        P(),
        P(),
        P(),
        P(),
        P(),
        P(),
    )
    out_specs = (P("req", "seq", None, None), P(None, "req", "seq", None))
    return jax.shard_map(local, mesh=mesh, in_specs=in_specs, out_specs=out_specs, check_vma=False)
```

```python
import jax
import jax.numpy as jnp
from jax import lax
from jax.experimental import pallas as pl
from jax.experimental.pallas import tpu as pltpu
from jax.sharding import PartitionSpec as P

BLOCK = 256


def shifted(block, axis, distance):
    devices = range(lax.axis_size(axis))
    route = [(i - distance, i) for i in devices if i - distance in devices]
    return lax.ppermute(block, axis, route)


def conv_kernel(x_ref, edge_ref, w_ref, b_ref, o_ref):
    x = x_ref[...].astype(jnp.float32)
    edge = edge_ref[...].astype(jnp.float32)
    w = w_ref[...]
    b = b_ref[...]
    taps = w.shape[1]
    acc = b + w[:, taps - 1 : taps] * x
    for tap in range(taps - 1):
        acc = acc + w[:, tap : tap + 1] * pltpu.roll(x, taps - 1 - tap, 1)
    o_ref[...] = (acc * (0.5 + 0.5 * jnp.tanh(0.5 * acc))).astype(o_ref.dtype)
    head = x[:, :128]
    lane = lax.broadcasted_iota(jnp.int32, head.shape, 1)
    first = b + w[:, taps - 1 : taps] * head
    for tap in range(taps - 1):
        lag = taps - 1 - tap
        moved = pltpu.roll(head, lag, 1)
        for t in range(lag):
            moved = jnp.where(lane == t, edge[:, tap + t : tap + t + 1], moved)
        first = first + w[:, tap : tap + 1] * moved
    o_ref[:, :128] = (first * (0.5 + 0.5 * jnp.tanh(0.5 * first))).astype(o_ref.dtype)


def conv_silu(conv_t, edge_t, weight_t, bias_t, rows=768):
    feats, slots = conv_t.shape
    taps = weight_t.shape[1]
    return pl.pallas_call(
        conv_kernel,
        grid=(feats // rows,),
        in_specs=[
            pl.BlockSpec((rows, slots), lambda i: (i, 0)),
            pl.BlockSpec((rows, taps - 1), lambda i: (i, 0)),
            pl.BlockSpec((rows, taps), lambda i: (i, 0)),
            pl.BlockSpec((rows, 1), lambda i: (i, 0)),
        ],
        out_specs=pl.BlockSpec((rows, slots), lambda i: (i, 0)),
        out_shape=jax.ShapeDtypeStruct((feats, slots), jnp.bfloat16),
        cost_estimate=pl.CostEstimate(
            flops=feats * slots * 14, transcendentals=feats * slots, bytes_accessed=feats * slots * 4
        ),
    )(conv_t, edge_t, weight_t, bias_t)


def norm_kernel(y_ref, z_ref, w_ref, mask_ref, o_ref):
    z = z_ref[...].astype(jnp.float32)
    gated = y_ref[...] * (z * (0.5 + 0.5 * jnp.tanh(0.5 * z)))
    mean = jnp.sum(gated * gated, axis=0, keepdims=True) * (1.0 / gated.shape[0])
    normed = gated * lax.rsqrt(mean + 1e-05) * w_ref[...]
    normed = jnp.where(mask_ref[...] > 0.5, normed, 0.0)
    o_ref[...] = normed.T.astype(o_ref.dtype)


def gate_norm(y_t, z_t, weight, mask, cols=128):
    units, slots = y_t.shape
    return pl.pallas_call(
        norm_kernel,
        grid=(slots // cols,),
        in_specs=[
            pl.BlockSpec((units, cols), lambda i: (0, i)),
            pl.BlockSpec((units, cols), lambda i: (0, i)),
            pl.BlockSpec((units, 1), lambda i: (0, 0)),
            pl.BlockSpec((1, cols), lambda i: (0, i)),
        ],
        out_specs=pl.BlockSpec((cols, units), lambda i: (i, 0)),
        out_shape=jax.ShapeDtypeStruct((slots, units), jnp.bfloat16),
        cost_estimate=pl.CostEstimate(
            flops=units * slots * 12, transcendentals=units * slots, bytes_accessed=units * slots * 8
        ),
    )(y_t, z_t, weight, mask)


def block_step(state, pieces):
    inputs_x, b_rows, c_rows, step_dt, log_decay = pieces
    length = inputs_x.shape[0]
    heads = step_dt.shape[1]
    hdim = inputs_x.shape[1] // heads
    running = jnp.cumsum(log_decay, axis=0)
    gram = jnp.einsum("tn,un->tu", c_rows, b_rows, preferred_element_type=jnp.float32)
    later = jnp.arange(length)[:, None] >= jnp.arange(length)[None, :]
    spread = running.T[:, :, None] - running.T[:, None, :]
    decay = jnp.where(later[None], jnp.exp(jnp.where(later[None], spread, 0.0)), 0.0)
    mixing = (gram[None] * decay * step_dt.T[:, None, :]).astype(jnp.bfloat16)
    heads_x = inputs_x.reshape(length, heads, hdim)
    inside = jnp.einsum("htu,uhp->thp", mixing, heads_x, preferred_element_type=jnp.float32)
    carried = jnp.exp(running)[:, :, None] * jnp.einsum(
        "tn,hpn->thp", c_rows.astype(jnp.float32), state, precision=lax.Precision.HIGHEST
    )
    final_log = running[-1]
    weighting = jnp.exp(final_log[None, :] - running) * step_dt
    weighted = (
        (heads_x.astype(jnp.float32) * weighting[:, :, None])
        .astype(jnp.bfloat16)
        .reshape(length, heads * hdim)
    )
    contrib = jnp.einsum("ud,un->dn", weighted, b_rows, preferred_element_type=jnp.float32).reshape(
        heads, hdim, -1
    )
    new_state = jnp.exp(final_log)[:, None, None] * state + contrib
    return (new_state, (inside + carried).reshape(length, heads * hdim))


def local(
    hidden, w_in, conv_weight, conv_bias, dt_bias, a_log, d_skip, norm_weight, lengths, prompt_group
):
    tok_rows = hidden[0, 0]
    slots = tok_rows.shape[0]
    inner = norm_weight.shape[0]
    heads = dt_bias.shape[0]
    hdim = inner // heads
    nstate = (conv_bias.shape[0] - inner) // 2
    convdim = conv_bias.shape[0]
    taps = conv_weight.shape[0]
    seq_count = lax.axis_size("seq")
    my_group = lax.axis_index("req")
    my_block = lax.axis_index("seq")
    qlen = jnp.sum(jnp.where(prompt_group == my_group, lengths, 0))
    filled = jnp.arange(slots, dtype=jnp.int32) < qlen
    column_blocks = [w_in]
    for distance in range(1, seq_count):
        cycle = [(i, (i + distance) % seq_count) for i in range(seq_count)]
        column_blocks.append(lax.ppermute(w_in, "seq", cycle))
    by_distance = jnp.stack(column_blocks)
    from_block = (my_block - jnp.arange(seq_count)) % seq_count
    in_order = jnp.take(by_distance, from_block, axis=0)
    wide_rows = jnp.transpose(in_order, (1, 0, 2)).reshape(w_in.shape[0], -1)
    projected = jnp.dot(
        tok_rows,
        lax.all_gather(wide_rows, "req", axis=0, tiled=True),
        preferred_element_type=jnp.float32,
    ).astype(jnp.bfloat16)
    gate_z = projected[:, :inner]
    conv_in = projected[:, inner : inner + convdim]
    dt_raw = projected[:, inner + convdim :]
    edge_rows = lax.dynamic_slice_in_dim(conv_in, qlen - (taps - 1), taps - 1, 0)
    prev_edge = shifted(edge_rows, "seq", 1)
    conv_act = conv_silu(conv_in.T, prev_edge.T, conv_weight.T, conv_bias[:, None]).T
    inputs_x = conv_act[:, :inner]
    b_rows = conv_act[:, inner : inner + nstate]
    c_rows = conv_act[:, inner + nstate :]
    step_dt = jnp.where(
        filled[:, None], jax.nn.softplus(dt_raw.astype(jnp.float32) + dt_bias[None, :]), 0.0
    )
    log_decay = step_dt * (-jnp.exp(a_log))[None, :]
    through = jnp.cumsum(log_decay, axis=0)
    block_total = through[-1]
    block_rows = min(BLOCK, slots)
    count = slots // block_rows
    pieces = (
        inputs_x.reshape(count, block_rows, inner),
        b_rows.reshape(count, block_rows, nstate),
        c_rows.reshape(count, block_rows, nstate),
        step_dt.reshape(count, block_rows, heads),
        log_decay.reshape(count, block_rows, heads),
    )
    zero_state = jnp.zeros((heads, hdim, nstate), jnp.float32)
    local_end = zero_state
    outs = []
    for index in range(count):
        local_end, out = block_step(local_end, tuple(piece[index] for piece in pieces))
        outs.append(out)
    outputs = jnp.concatenate(outs, axis=0)
    total_hi = lax.reduce_precision(block_total, exponent_bits=8, mantissa_bits=7)
    total_rest = block_total - total_hi
    total_mid = lax.reduce_precision(total_rest, exponent_bits=8, mantissa_bits=7)
    total_lo = total_rest - total_mid
    parts = jnp.stack([total_hi, total_mid, total_lo], axis=1).astype(jnp.bfloat16)
    parts = jnp.broadcast_to(parts[:, :, None], (heads, 3, 128))
    packed = jnp.concatenate(
        [local_end.reshape(heads, hdim * nstate).astype(jnp.bfloat16), parts.reshape(heads, 3 * 128)],
        axis=1,
    )
    gathered = lax.all_gather(packed, "seq", axis=0, tiled=False)
    ends = gathered[:, :, : hdim * nstate].astype(jnp.float32).reshape(seq_count, heads, hdim, nstate)
    sent = gathered[:, :, hdim * nstate :].astype(jnp.float32)
    totals = sent[:, :, 0] + (sent[:, :, 128] + sent[:, :, 256])
    entering = zero_state
    for turn in range(seq_count - 1):
        stepped = jnp.exp(totals[turn])[:, None, None] * entering + ends[turn]
        entering = jnp.where(turn < my_block, stepped, entering)
    incoming = jnp.exp(through)[:, :, None] * jnp.einsum(
        "tn,hpn->thp", c_rows.astype(jnp.float32), entering, precision=lax.Precision.HIGHEST
    )
    heads_y = (
        outputs.reshape(slots, heads, hdim)
        + incoming
        + d_skip[None, :, None] * inputs_x.astype(jnp.float32).reshape(slots, heads, hdim)
    )
    gated_out = gate_norm(
        heads_y.reshape(slots, inner).T,
        gate_z.T,
        norm_weight[:, None],
        filled.astype(jnp.float32)[None, :],
    ).reshape(1, 1, slots, inner)
    later_mask = jnp.arange(seq_count)[None, :] > jnp.arange(seq_count)[:, None]
    after = jnp.sum(jnp.where(later_mask[:, :, None], totals[None, :, :], 0.0), axis=1)
    piece = hdim // seq_count
    own_ends = lax.dynamic_slice_in_dim(ends, my_block * piece, piece, axis=2)
    share = jnp.sum(jnp.exp(after)[:, :, None, None] * own_ends, axis=0)
    moved = lax.all_to_all(
        share[None].astype(jnp.bfloat16), "req", split_axis=1, concat_axis=0, tiled=True
    ).astype(jnp.float32)
    pick = (prompt_group[:, None] == jnp.arange(moved.shape[0])[None, :]).astype(jnp.float32)
    final_states = jnp.einsum(
        "pg,gabc->pabc", pick, moved, precision=lax.Precision.HIGHEST
    )
    return (gated_out, final_states)


def solution(mesh):
    in_specs = (
        P("req", "seq", None, None),
        P("req", "seq"),
        P(),
        P(),
        P(),
        P(),
        P(),
        P(),
        P(),
        P(),
    )
    out_specs = (P("req", "seq", None, None), P(None, "req", "seq", None))
    return jax.shard_map(local, mesh=mesh, in_specs=in_specs, out_specs=out_specs, check_vma=False)
```

```python
import jax
import jax.numpy as jnp
from jax import lax
from jax.experimental import pallas as pl
from jax.experimental.pallas import tpu as pltpu
from jax.sharding import PartitionSpec as P

BLOCK = 256


def shifted(block, axis, distance):
    devices = range(lax.axis_size(axis))
    route = [(i - distance, i) for i in devices if i - distance in devices]
    return lax.ppermute(block, axis, route)


def conv_kernel(x_ref, edge_ref, w_ref, b_ref, o_ref):
    x = x_ref[...].astype(jnp.float32)
    edge = edge_ref[...].astype(jnp.float32)
    w = w_ref[...]
    b = b_ref[...]
    taps = w.shape[1]
    acc = b + w[:, taps - 1 : taps] * x
    for tap in range(taps - 1):
        acc = acc + w[:, tap : tap + 1] * pltpu.roll(x, taps - 1 - tap, 1)
    o_ref[...] = (acc * (0.5 + 0.5 * jnp.tanh(0.5 * acc))).astype(o_ref.dtype)
    head = x[:, :128]
    lane = lax.broadcasted_iota(jnp.int32, head.shape, 1)
    first = b + w[:, taps - 1 : taps] * head
    for tap in range(taps - 1):
        lag = taps - 1 - tap
        moved = pltpu.roll(head, lag, 1)
        for t in range(lag):
            moved = jnp.where(lane == t, edge[:, tap + t : tap + t + 1], moved)
        first = first + w[:, tap : tap + 1] * moved
    o_ref[:, :128] = (first * (0.5 + 0.5 * jnp.tanh(0.5 * first))).astype(o_ref.dtype)


def conv_silu(conv_t, edge_t, weight_t, bias_t, rows=768):
    feats, slots = conv_t.shape
    taps = weight_t.shape[1]
    return pl.pallas_call(
        conv_kernel,
        grid=(feats // rows,),
        in_specs=[
            pl.BlockSpec((rows, slots), lambda i: (i, 0)),
            pl.BlockSpec((rows, taps - 1), lambda i: (i, 0)),
            pl.BlockSpec((rows, taps), lambda i: (i, 0)),
            pl.BlockSpec((rows, 1), lambda i: (i, 0)),
        ],
        out_specs=pl.BlockSpec((rows, slots), lambda i: (i, 0)),
        out_shape=jax.ShapeDtypeStruct((feats, slots), jnp.bfloat16),
        cost_estimate=pl.CostEstimate(
            flops=feats * slots * 14, transcendentals=feats * slots, bytes_accessed=feats * slots * 4
        ),
    )(conv_t, edge_t, weight_t, bias_t)


def norm_kernel(out_ref, inc_ref, x_ref, skip_ref, z_ref, w_ref, mask_ref, o_ref):
    z = z_ref[...].astype(jnp.float32)
    y = out_ref[...] + inc_ref[...] + skip_ref[...] * x_ref[...].astype(jnp.float32)
    gated = y * (z * (0.5 + 0.5 * jnp.tanh(0.5 * z)))
    mean = jnp.sum(gated * gated, axis=0, keepdims=True) * (1.0 / gated.shape[0])
    normed = gated * lax.rsqrt(mean + 1e-05) * w_ref[...]
    normed = jnp.where(mask_ref[...] > 0.5, normed, 0.0)
    o_ref[...] = normed.T.astype(o_ref.dtype)


def gate_norm(out_t, inc_t, x_t, skip, z_t, weight, mask, cols=128):
    units, slots = out_t.shape
    return pl.pallas_call(
        norm_kernel,
        grid=(slots // cols,),
        in_specs=[
            pl.BlockSpec((units, cols), lambda i: (0, i)),
            pl.BlockSpec((units, cols), lambda i: (0, i)),
            pl.BlockSpec((units, cols), lambda i: (0, i)),
            pl.BlockSpec((units, 1), lambda i: (0, 0)),
            pl.BlockSpec((units, cols), lambda i: (0, i)),
            pl.BlockSpec((units, 1), lambda i: (0, 0)),
            pl.BlockSpec((1, cols), lambda i: (0, i)),
        ],
        out_specs=pl.BlockSpec((cols, units), lambda i: (i, 0)),
        out_shape=jax.ShapeDtypeStruct((slots, units), jnp.bfloat16),
        cost_estimate=pl.CostEstimate(
            flops=units * slots * 12, transcendentals=units * slots, bytes_accessed=units * slots * 8
        ),
    )(out_t, inc_t, x_t, skip, z_t, weight, mask)


def block_step(state, pieces):
    inputs_x, b_rows, c_rows, step_dt, log_decay = pieces
    length = inputs_x.shape[0]
    heads = step_dt.shape[1]
    hdim = inputs_x.shape[1] // heads
    running = jnp.cumsum(log_decay, axis=0)
    gram = jnp.einsum("tn,un->tu", c_rows, b_rows, preferred_element_type=jnp.float32)
    later = jnp.arange(length)[:, None] >= jnp.arange(length)[None, :]
    spread = running.T[:, :, None] - running.T[:, None, :]
    decay = jnp.where(later[None], jnp.exp(jnp.where(later[None], spread, 0.0)), 0.0)
    mixing = (gram[None] * decay * step_dt.T[:, None, :]).astype(jnp.bfloat16)
    heads_x = inputs_x.reshape(length, heads, hdim)
    inside = jnp.einsum("htu,uhp->thp", mixing, heads_x, preferred_element_type=jnp.float32)
    carried = jnp.exp(running)[:, :, None] * jnp.einsum(
        "tn,hpn->thp", c_rows.astype(jnp.float32), state, precision=lax.Precision.HIGHEST
    )
    final_log = running[-1]
    weighting = jnp.exp(final_log[None, :] - running) * step_dt
    weighted = (
        (heads_x.astype(jnp.float32) * weighting[:, :, None])
        .astype(jnp.bfloat16)
        .reshape(length, heads * hdim)
    )
    contrib = jnp.einsum("ud,un->dn", weighted, b_rows, preferred_element_type=jnp.float32).reshape(
        heads, hdim, -1
    )
    new_state = jnp.exp(final_log)[:, None, None] * state + contrib
    return (new_state, (inside + carried).reshape(length, heads * hdim))


def local(
    hidden, w_in, conv_weight, conv_bias, dt_bias, a_log, d_skip, norm_weight, lengths, prompt_group
):
    tok_rows = hidden[0, 0]
    slots = tok_rows.shape[0]
    inner = norm_weight.shape[0]
    heads = dt_bias.shape[0]
    hdim = inner // heads
    nstate = (conv_bias.shape[0] - inner) // 2
    convdim = conv_bias.shape[0]
    taps = conv_weight.shape[0]
    seq_count = lax.axis_size("seq")
    my_group = lax.axis_index("req")
    my_block = lax.axis_index("seq")
    qlen = jnp.sum(jnp.where(prompt_group == my_group, lengths, 0))
    filled = jnp.arange(slots, dtype=jnp.int32) < qlen
    column_blocks = [w_in]
    for distance in range(1, seq_count):
        cycle = [(i, (i + distance) % seq_count) for i in range(seq_count)]
        column_blocks.append(lax.ppermute(w_in, "seq", cycle))
    by_distance = jnp.stack(column_blocks)
    from_block = (my_block - jnp.arange(seq_count)) % seq_count
    in_order = jnp.take(by_distance, from_block, axis=0)
    wide_rows = jnp.transpose(in_order, (1, 0, 2)).reshape(w_in.shape[0], -1)
    projected = jnp.dot(
        tok_rows,
        lax.all_gather(wide_rows, "req", axis=0, tiled=True),
        preferred_element_type=jnp.float32,
    ).astype(jnp.bfloat16)
    gate_z = projected[:, :inner]
    conv_in = projected[:, inner : inner + convdim]
    dt_raw = projected[:, inner + convdim :]
    edge_rows = lax.dynamic_slice_in_dim(conv_in, qlen - (taps - 1), taps - 1, 0)
    prev_edge = shifted(edge_rows, "seq", 1)
    conv_act = conv_silu(conv_in.T, prev_edge.T, conv_weight.T, conv_bias[:, None]).T
    inputs_x = conv_act[:, :inner]
    b_rows = conv_act[:, inner : inner + nstate]
    c_rows = conv_act[:, inner + nstate :]
    step_dt = jnp.where(
        filled[:, None], jax.nn.softplus(dt_raw.astype(jnp.float32) + dt_bias[None, :]), 0.0
    )
    log_decay = step_dt * (-jnp.exp(a_log))[None, :]
    through = jnp.cumsum(log_decay, axis=0)
    block_total = through[-1]
    block_rows = min(BLOCK, slots)
    count = slots // block_rows
    pieces = (
        inputs_x.reshape(count, block_rows, inner),
        b_rows.reshape(count, block_rows, nstate),
        c_rows.reshape(count, block_rows, nstate),
        step_dt.reshape(count, block_rows, heads),
        log_decay.reshape(count, block_rows, heads),
    )
    zero_state = jnp.zeros((heads, hdim, nstate), jnp.float32)
    local_end = zero_state
    outs = []
    for index in range(count):
        local_end, out = block_step(local_end, tuple(piece[index] for piece in pieces))
        outs.append(out)
    outputs = jnp.concatenate(outs, axis=0)
    total_hi = lax.reduce_precision(block_total, exponent_bits=8, mantissa_bits=7)
    total_rest = block_total - total_hi
    total_mid = lax.reduce_precision(total_rest, exponent_bits=8, mantissa_bits=7)
    total_lo = total_rest - total_mid
    parts = jnp.stack([total_hi, total_mid, total_lo], axis=1).astype(jnp.bfloat16)
    parts = jnp.broadcast_to(parts[:, :, None], (heads, 3, 128))
    packed = jnp.concatenate(
        [local_end.reshape(heads, hdim * nstate).astype(jnp.bfloat16), parts.reshape(heads, 3 * 128)],
        axis=1,
    )
    gathered = lax.all_gather(packed, "seq", axis=0, tiled=False)
    ends = gathered[:, :, : hdim * nstate].astype(jnp.float32).reshape(seq_count, heads, hdim, nstate)
    sent = gathered[:, :, hdim * nstate :].astype(jnp.float32)
    totals = sent[:, :, 0] + (sent[:, :, 128] + sent[:, :, 256])
    entering = zero_state
    for turn in range(seq_count - 1):
        stepped = jnp.exp(totals[turn])[:, None, None] * entering + ends[turn]
        entering = jnp.where(turn < my_block, stepped, entering)
    incoming = jnp.exp(through)[:, :, None] * jnp.einsum(
        "tn,hpn->thp", c_rows.astype(jnp.float32), entering, precision=lax.Precision.HIGHEST
    )
    gated_out = gate_norm(
        outputs.reshape(slots, inner).T,
        incoming.reshape(slots, inner).T,
        inputs_x.T,
        jnp.repeat(d_skip, hdim)[:, None],
        gate_z.T,
        norm_weight[:, None],
        filled.astype(jnp.float32)[None, :],
    ).reshape(1, 1, slots, inner)
    later_mask = jnp.arange(seq_count)[None, :] > jnp.arange(seq_count)[:, None]
    after = jnp.sum(jnp.where(later_mask[:, :, None], totals[None, :, :], 0.0), axis=1)
    piece = hdim // seq_count
    own_ends = lax.dynamic_slice_in_dim(ends, my_block * piece, piece, axis=2)
    share = jnp.sum(jnp.exp(after)[:, :, None, None] * own_ends, axis=0)
    moved = lax.all_to_all(share[None], "req", split_axis=1, concat_axis=0, tiled=True)
    pick = (prompt_group[:, None] == jnp.arange(moved.shape[0])[None, :]).astype(jnp.float32)
    final_states = jnp.einsum(
        "pg,gabc->pabc", pick, moved, precision=lax.Precision.HIGHEST
    )
    return (gated_out, final_states)


def solution(mesh):
    in_specs = (
        P("req", "seq", None, None),
        P("req", "seq"),
        P(),
        P(),
        P(),
        P(),
        P(),
        P(),
        P(),
        P(),
    )
    out_specs = (P("req", "seq", None, None), P(None, "req", "seq", None))
    return jax.shard_map(local, mesh=mesh, in_specs=in_specs, out_specs=out_specs, check_vma=False)
```

```python
import jax
import jax.numpy as jnp
from jax import lax
from jax.experimental import pallas as pl
from jax.experimental.pallas import tpu as pltpu
from jax.sharding import PartitionSpec as P

BLOCK = 256


def shifted(block, axis, distance):
    devices = range(lax.axis_size(axis))
    route = [(i - distance, i) for i in devices if i - distance in devices]
    return lax.ppermute(block, axis, route)


def conv_kernel(x_ref, edge_ref, w_ref, b_ref, o_ref):
    x = x_ref[...].astype(jnp.float32)
    edge = edge_ref[...].astype(jnp.float32)
    w = w_ref[...]
    b = b_ref[...]
    taps = w.shape[1]
    acc = b + w[:, taps - 1 : taps] * x
    for tap in range(taps - 1):
        acc = acc + w[:, tap : tap + 1] * pltpu.roll(x, taps - 1 - tap, 1)
    o_ref[...] = (acc * (0.5 + 0.5 * jnp.tanh(0.5 * acc))).astype(o_ref.dtype)
    head = x[:, :128]
    lane = lax.broadcasted_iota(jnp.int32, head.shape, 1)
    first = b + w[:, taps - 1 : taps] * head
    for tap in range(taps - 1):
        lag = taps - 1 - tap
        moved = pltpu.roll(head, lag, 1)
        for t in range(lag):
            moved = jnp.where(lane == t, edge[:, tap + t : tap + t + 1], moved)
        first = first + w[:, tap : tap + 1] * moved
    o_ref[:, :128] = (first * (0.5 + 0.5 * jnp.tanh(0.5 * first))).astype(o_ref.dtype)


def conv_silu(conv_t, edge_t, weight_t, bias_t, rows=768):
    feats, slots = conv_t.shape
    taps = weight_t.shape[1]
    return pl.pallas_call(
        conv_kernel,
        grid=(feats // rows,),
        in_specs=[
            pl.BlockSpec((rows, slots), lambda i: (i, 0)),
            pl.BlockSpec((rows, taps - 1), lambda i: (i, 0)),
            pl.BlockSpec((rows, taps), lambda i: (i, 0)),
            pl.BlockSpec((rows, 1), lambda i: (i, 0)),
        ],
        out_specs=pl.BlockSpec((rows, slots), lambda i: (i, 0)),
        out_shape=jax.ShapeDtypeStruct((feats, slots), jnp.bfloat16),
        cost_estimate=pl.CostEstimate(
            flops=feats * slots * 14, transcendentals=feats * slots, bytes_accessed=feats * slots * 4
        ),
    )(conv_t, edge_t, weight_t, bias_t)


def norm_kernel(y_ref, z_ref, w_ref, mask_ref, o_ref):
    z = z_ref[...].astype(jnp.float32)
    gated = y_ref[...] * (z * (0.5 + 0.5 * jnp.tanh(0.5 * z)))
    mean = jnp.sum(gated * gated, axis=0, keepdims=True) * (1.0 / gated.shape[0])
    normed = gated * lax.rsqrt(mean + 1e-05) * w_ref[...]
    normed = jnp.where(mask_ref[...] > 0.5, normed, 0.0)
    o_ref[...] = normed.T.astype(o_ref.dtype)


def gate_norm(y_t, z_t, weight, mask, cols=256):
    units, slots = y_t.shape
    return pl.pallas_call(
        norm_kernel,
        grid=(slots // cols,),
        in_specs=[
            pl.BlockSpec((units, cols), lambda i: (0, i)),
            pl.BlockSpec((units, cols), lambda i: (0, i)),
            pl.BlockSpec((units, 1), lambda i: (0, 0)),
            pl.BlockSpec((1, cols), lambda i: (0, i)),
        ],
        out_specs=pl.BlockSpec((cols, units), lambda i: (i, 0)),
        out_shape=jax.ShapeDtypeStruct((slots, units), jnp.bfloat16),
        cost_estimate=pl.CostEstimate(
            flops=units * slots * 12, transcendentals=units * slots, bytes_accessed=units * slots * 8
        ),
    )(y_t, z_t, weight, mask)


def block_step(state, pieces):
    inputs_x, b_rows, c_rows, step_dt, log_decay = pieces
    length = inputs_x.shape[0]
    heads = step_dt.shape[1]
    hdim = inputs_x.shape[1] // heads
    running = jnp.cumsum(log_decay, axis=0)
    gram = jnp.einsum("tn,un->tu", c_rows, b_rows, preferred_element_type=jnp.float32)
    later = jnp.arange(length)[:, None] >= jnp.arange(length)[None, :]
    spread = running.T[:, :, None] - running.T[:, None, :]
    decay = jnp.where(later[None], jnp.exp(jnp.where(later[None], spread, 0.0)), 0.0)
    mixing = (gram[None] * decay * step_dt.T[:, None, :]).astype(jnp.bfloat16)
    heads_x = inputs_x.reshape(length, heads, hdim)
    inside = jnp.einsum("htu,uhp->thp", mixing, heads_x, preferred_element_type=jnp.float32)
    carried = jnp.exp(running)[:, :, None] * jnp.einsum(
        "tn,hpn->thp", c_rows.astype(jnp.float32), state, precision=lax.Precision.HIGHEST
    )
    final_log = running[-1]
    weighting = jnp.exp(final_log[None, :] - running) * step_dt
    weighted = (
        (heads_x.astype(jnp.float32) * weighting[:, :, None])
        .astype(jnp.bfloat16)
        .reshape(length, heads * hdim)
    )
    contrib = jnp.einsum("ud,un->dn", weighted, b_rows, preferred_element_type=jnp.float32).reshape(
        heads, hdim, -1
    )
    new_state = jnp.exp(final_log)[:, None, None] * state + contrib
    return (new_state, (inside + carried).reshape(length, heads * hdim))


def local(
    hidden, w_in, conv_weight, conv_bias, dt_bias, a_log, d_skip, norm_weight, lengths, prompt_group
):
    tok_rows = hidden[0, 0]
    slots = tok_rows.shape[0]
    inner = norm_weight.shape[0]
    heads = dt_bias.shape[0]
    hdim = inner // heads
    nstate = (conv_bias.shape[0] - inner) // 2
    convdim = conv_bias.shape[0]
    taps = conv_weight.shape[0]
    seq_count = lax.axis_size("seq")
    my_group = lax.axis_index("req")
    my_block = lax.axis_index("seq")
    qlen = jnp.sum(jnp.where(prompt_group == my_group, lengths, 0))
    filled = jnp.arange(slots, dtype=jnp.int32) < qlen
    column_blocks = [w_in]
    for distance in range(1, seq_count):
        cycle = [(i, (i + distance) % seq_count) for i in range(seq_count)]
        column_blocks.append(lax.ppermute(w_in, "seq", cycle))
    by_distance = jnp.stack(column_blocks)
    from_block = (my_block - jnp.arange(seq_count)) % seq_count
    in_order = jnp.take(by_distance, from_block, axis=0)
    wide_rows = jnp.transpose(in_order, (1, 0, 2)).reshape(w_in.shape[0], -1)
    projected = jnp.dot(
        tok_rows,
        lax.all_gather(wide_rows, "req", axis=0, tiled=True),
        preferred_element_type=jnp.float32,
    ).astype(jnp.bfloat16)
    gate_z = projected[:, :inner]
    conv_in = projected[:, inner : inner + convdim]
    dt_raw = projected[:, inner + convdim :]
    edge_rows = lax.dynamic_slice_in_dim(conv_in, qlen - (taps - 1), taps - 1, 0)
    prev_edge = shifted(edge_rows, "seq", 1)
    conv_act = conv_silu(conv_in.T, prev_edge.T, conv_weight.T, conv_bias[:, None]).T
    inputs_x = conv_act[:, :inner]
    b_rows = conv_act[:, inner : inner + nstate]
    c_rows = conv_act[:, inner + nstate :]
    step_dt = jnp.where(
        filled[:, None], jax.nn.softplus(dt_raw.astype(jnp.float32) + dt_bias[None, :]), 0.0
    )
    log_decay = step_dt * (-jnp.exp(a_log))[None, :]
    through = jnp.cumsum(log_decay, axis=0)
    block_total = through[-1]
    block_rows = min(BLOCK, slots)
    count = slots // block_rows
    pieces = (
        inputs_x.reshape(count, block_rows, inner),
        b_rows.reshape(count, block_rows, nstate),
        c_rows.reshape(count, block_rows, nstate),
        step_dt.reshape(count, block_rows, heads),
        log_decay.reshape(count, block_rows, heads),
    )
    zero_state = jnp.zeros((heads, hdim, nstate), jnp.float32)
    local_end = zero_state
    outs = []
    for index in range(count):
        local_end, out = block_step(local_end, tuple(piece[index] for piece in pieces))
        outs.append(out)
    outputs = jnp.concatenate(outs, axis=0)
    total_hi = lax.reduce_precision(block_total, exponent_bits=8, mantissa_bits=7)
    total_rest = block_total - total_hi
    total_mid = lax.reduce_precision(total_rest, exponent_bits=8, mantissa_bits=7)
    total_lo = total_rest - total_mid
    parts = jnp.stack([total_hi, total_mid, total_lo], axis=1).astype(jnp.bfloat16)
    parts = jnp.broadcast_to(parts[:, :, None], (heads, 3, 128))
    packed = jnp.concatenate(
        [local_end.reshape(heads, hdim * nstate).astype(jnp.bfloat16), parts.reshape(heads, 3 * 128)],
        axis=1,
    )
    gathered = lax.all_gather(packed, "seq", axis=0, tiled=False)
    ends = gathered[:, :, : hdim * nstate].astype(jnp.float32).reshape(seq_count, heads, hdim, nstate)
    sent = gathered[:, :, hdim * nstate :].astype(jnp.float32)
    totals = sent[:, :, 0] + (sent[:, :, 128] + sent[:, :, 256])
    entering = zero_state
    for turn in range(seq_count - 1):
        stepped = jnp.exp(totals[turn])[:, None, None] * entering + ends[turn]
        entering = jnp.where(turn < my_block, stepped, entering)
    incoming = jnp.exp(through)[:, :, None] * jnp.einsum(
        "tn,hpn->thp", c_rows.astype(jnp.float32), entering, precision=lax.Precision.HIGHEST
    )
    heads_y = (
        outputs.reshape(slots, heads, hdim)
        + incoming
        + d_skip[None, :, None] * inputs_x.astype(jnp.float32).reshape(slots, heads, hdim)
    )
    gated_out = gate_norm(
        heads_y.reshape(slots, inner).T,
        gate_z.T,
        norm_weight[:, None],
        filled.astype(jnp.float32)[None, :],
    ).reshape(1, 1, slots, inner)
    later_mask = jnp.arange(seq_count)[None, :] > jnp.arange(seq_count)[:, None]
    after = jnp.sum(jnp.where(later_mask[:, :, None], totals[None, :, :], 0.0), axis=1)
    piece = hdim // seq_count
    own_ends = lax.dynamic_slice_in_dim(ends, my_block * piece, piece, axis=2)
    share = jnp.sum(jnp.exp(after)[:, :, None, None] * own_ends, axis=0)
    moved = lax.all_to_all(share[None], "req", split_axis=1, concat_axis=0, tiled=True)
    pick = (prompt_group[:, None] == jnp.arange(moved.shape[0])[None, :]).astype(jnp.float32)
    final_states = jnp.einsum(
        "pg,gabc->pabc", pick, moved, precision=lax.Precision.HIGHEST
    )
    return (gated_out, final_states)


def solution(mesh):
    in_specs = (
        P("req", "seq", None, None),
        P("req", "seq"),
        P(),
        P(),
        P(),
        P(),
        P(),
        P(),
        P(),
        P(),
    )
    out_specs = (P("req", "seq", None, None), P(None, "req", "seq", None))
    return jax.shard_map(local, mesh=mesh, in_specs=in_specs, out_specs=out_specs, check_vma=False)
```

```python
import jax
import jax.numpy as jnp
from jax import lax
from jax.experimental import pallas as pl
from jax.experimental.pallas import tpu as pltpu
from jax.sharding import PartitionSpec as P

BLOCK = 256


def shifted(block, axis, distance):
    devices = range(lax.axis_size(axis))
    route = [(i - distance, i) for i in devices if i - distance in devices]
    return lax.ppermute(block, axis, route)


def conv_kernel(x_ref, edge_ref, w_ref, b_ref, o_ref):
    x = x_ref[...].astype(jnp.float32)
    edge = edge_ref[...].astype(jnp.float32)
    w = w_ref[...]
    b = b_ref[...]
    taps = w.shape[1]
    acc = b + w[:, taps - 1 : taps] * x
    for tap in range(taps - 1):
        acc = acc + w[:, tap : tap + 1] * pltpu.roll(x, taps - 1 - tap, 1)
    o_ref[...] = (acc * (0.5 + 0.5 * jnp.tanh(0.5 * acc))).astype(o_ref.dtype)
    head = x[:, :128]
    lane = lax.broadcasted_iota(jnp.int32, head.shape, 1)
    first = b + w[:, taps - 1 : taps] * head
    for tap in range(taps - 1):
        lag = taps - 1 - tap
        moved = pltpu.roll(head, lag, 1)
        for t in range(lag):
            moved = jnp.where(lane == t, edge[:, tap + t : tap + t + 1], moved)
        first = first + w[:, tap : tap + 1] * moved
    o_ref[:, :128] = (first * (0.5 + 0.5 * jnp.tanh(0.5 * first))).astype(o_ref.dtype)


def conv_silu(conv_t, edge_t, weight_t, bias_t, rows=1152):
    feats, slots = conv_t.shape
    taps = weight_t.shape[1]
    return pl.pallas_call(
        conv_kernel,
        grid=(feats // rows,),
        in_specs=[
            pl.BlockSpec((rows, slots), lambda i: (i, 0)),
            pl.BlockSpec((rows, taps - 1), lambda i: (i, 0)),
            pl.BlockSpec((rows, taps), lambda i: (i, 0)),
            pl.BlockSpec((rows, 1), lambda i: (i, 0)),
        ],
        out_specs=pl.BlockSpec((rows, slots), lambda i: (i, 0)),
        out_shape=jax.ShapeDtypeStruct((feats, slots), jnp.bfloat16),
        cost_estimate=pl.CostEstimate(
            flops=feats * slots * 14, transcendentals=feats * slots, bytes_accessed=feats * slots * 4
        ),
    )(conv_t, edge_t, weight_t, bias_t)


def norm_kernel(y_ref, z_ref, w_ref, mask_ref, o_ref):
    z = z_ref[...].astype(jnp.float32)
    gated = y_ref[...] * (z * (0.5 + 0.5 * jnp.tanh(0.5 * z)))
    mean = jnp.sum(gated * gated, axis=0, keepdims=True) * (1.0 / gated.shape[0])
    normed = gated * lax.rsqrt(mean + 1e-05) * w_ref[...]
    normed = jnp.where(mask_ref[...] > 0.5, normed, 0.0)
    o_ref[...] = normed.T.astype(o_ref.dtype)


def gate_norm(y_t, z_t, weight, mask, cols=128):
    units, slots = y_t.shape
    return pl.pallas_call(
        norm_kernel,
        grid=(slots // cols,),
        in_specs=[
            pl.BlockSpec((units, cols), lambda i: (0, i)),
            pl.BlockSpec((units, cols), lambda i: (0, i)),
            pl.BlockSpec((units, 1), lambda i: (0, 0)),
            pl.BlockSpec((1, cols), lambda i: (0, i)),
        ],
        out_specs=pl.BlockSpec((cols, units), lambda i: (i, 0)),
        out_shape=jax.ShapeDtypeStruct((slots, units), jnp.bfloat16),
        cost_estimate=pl.CostEstimate(
            flops=units * slots * 12, transcendentals=units * slots, bytes_accessed=units * slots * 8
        ),
    )(y_t, z_t, weight, mask)


def block_step(state, pieces):
    inputs_x, b_rows, c_rows, step_dt, log_decay = pieces
    length = inputs_x.shape[0]
    heads = step_dt.shape[1]
    hdim = inputs_x.shape[1] // heads
    running = jnp.cumsum(log_decay, axis=0)
    gram = jnp.einsum("tn,un->tu", c_rows, b_rows, preferred_element_type=jnp.float32)
    later = jnp.arange(length)[:, None] >= jnp.arange(length)[None, :]
    spread = running.T[:, :, None] - running.T[:, None, :]
    decay = jnp.where(later[None], jnp.exp(jnp.where(later[None], spread, 0.0)), 0.0)
    mixing = (gram[None] * decay * step_dt.T[:, None, :]).astype(jnp.bfloat16)
    heads_x = inputs_x.reshape(length, heads, hdim)
    inside = jnp.einsum("htu,uhp->thp", mixing, heads_x, preferred_element_type=jnp.float32)
    carried = jnp.exp(running)[:, :, None] * jnp.einsum(
        "tn,hpn->thp", c_rows.astype(jnp.float32), state, precision=lax.Precision.HIGHEST
    )
    final_log = running[-1]
    weighting = jnp.exp(final_log[None, :] - running) * step_dt
    weighted = (
        (heads_x.astype(jnp.float32) * weighting[:, :, None])
        .astype(jnp.bfloat16)
        .reshape(length, heads * hdim)
    )
    contrib = jnp.einsum("ud,un->dn", weighted, b_rows, preferred_element_type=jnp.float32).reshape(
        heads, hdim, -1
    )
    new_state = jnp.exp(final_log)[:, None, None] * state + contrib
    return (new_state, (inside + carried).reshape(length, heads * hdim))


def local(
    hidden, w_in, conv_weight, conv_bias, dt_bias, a_log, d_skip, norm_weight, lengths, prompt_group
):
    tok_rows = hidden[0, 0]
    slots = tok_rows.shape[0]
    inner = norm_weight.shape[0]
    heads = dt_bias.shape[0]
    hdim = inner // heads
    nstate = (conv_bias.shape[0] - inner) // 2
    convdim = conv_bias.shape[0]
    taps = conv_weight.shape[0]
    seq_count = lax.axis_size("seq")
    my_group = lax.axis_index("req")
    my_block = lax.axis_index("seq")
    qlen = jnp.sum(jnp.where(prompt_group == my_group, lengths, 0))
    filled = jnp.arange(slots, dtype=jnp.int32) < qlen
    column_blocks = [w_in]
    for distance in range(1, seq_count):
        cycle = [(i, (i + distance) % seq_count) for i in range(seq_count)]
        column_blocks.append(lax.ppermute(w_in, "seq", cycle))
    by_distance = jnp.stack(column_blocks)
    from_block = (my_block - jnp.arange(seq_count)) % seq_count
    in_order = jnp.take(by_distance, from_block, axis=0)
    wide_rows = jnp.transpose(in_order, (1, 0, 2)).reshape(w_in.shape[0], -1)
    projected = jnp.dot(
        tok_rows,
        lax.all_gather(wide_rows, "req", axis=0, tiled=True),
        preferred_element_type=jnp.float32,
    ).astype(jnp.bfloat16)
    gate_z = projected[:, :inner]
    conv_in = projected[:, inner : inner + convdim]
    dt_raw = projected[:, inner + convdim :]
    edge_rows = lax.dynamic_slice_in_dim(conv_in, qlen - (taps - 1), taps - 1, 0)
    prev_edge = shifted(edge_rows, "seq", 1)
    conv_act = conv_silu(conv_in.T, prev_edge.T, conv_weight.T, conv_bias[:, None]).T
    inputs_x = conv_act[:, :inner]
    b_rows = conv_act[:, inner : inner + nstate]
    c_rows = conv_act[:, inner + nstate :]
    step_dt = jnp.where(
        filled[:, None], jax.nn.softplus(dt_raw.astype(jnp.float32) + dt_bias[None, :]), 0.0
    )
    log_decay = step_dt * (-jnp.exp(a_log))[None, :]
    through = jnp.cumsum(log_decay, axis=0)
    block_total = through[-1]
    block_rows = min(BLOCK, slots)
    count = slots // block_rows
    pieces = (
        inputs_x.reshape(count, block_rows, inner),
        b_rows.reshape(count, block_rows, nstate),
        c_rows.reshape(count, block_rows, nstate),
        step_dt.reshape(count, block_rows, heads),
        log_decay.reshape(count, block_rows, heads),
    )
    zero_state = jnp.zeros((heads, hdim, nstate), jnp.float32)
    local_end = zero_state
    outs = []
    for index in range(count):
        local_end, out = block_step(local_end, tuple(piece[index] for piece in pieces))
        outs.append(out)
    outputs = jnp.concatenate(outs, axis=0)
    total_hi = lax.reduce_precision(block_total, exponent_bits=8, mantissa_bits=7)
    total_rest = block_total - total_hi
    total_mid = lax.reduce_precision(total_rest, exponent_bits=8, mantissa_bits=7)
    total_lo = total_rest - total_mid
    parts = jnp.stack([total_hi, total_mid, total_lo], axis=1).astype(jnp.bfloat16)
    parts = jnp.broadcast_to(parts[:, :, None], (heads, 3, 128))
    packed = jnp.concatenate(
        [local_end.reshape(heads, hdim * nstate).astype(jnp.bfloat16), parts.reshape(heads, 3 * 128)],
        axis=1,
    )
    gathered = lax.all_gather(packed, "seq", axis=0, tiled=False)
    ends = gathered[:, :, : hdim * nstate].astype(jnp.float32).reshape(seq_count, heads, hdim, nstate)
    sent = gathered[:, :, hdim * nstate :].astype(jnp.float32)
    totals = sent[:, :, 0] + (sent[:, :, 128] + sent[:, :, 256])
    entering = zero_state
    for turn in range(seq_count - 1):
        stepped = jnp.exp(totals[turn])[:, None, None] * entering + ends[turn]
        entering = jnp.where(turn < my_block, stepped, entering)
    incoming = jnp.exp(through)[:, :, None] * jnp.einsum(
        "tn,hpn->thp", c_rows.astype(jnp.float32), entering, precision=lax.Precision.HIGHEST
    )
    heads_y = (
        outputs.reshape(slots, heads, hdim)
        + incoming
        + d_skip[None, :, None] * inputs_x.astype(jnp.float32).reshape(slots, heads, hdim)
    )
    gated_out = gate_norm(
        heads_y.reshape(slots, inner).T,
        gate_z.T,
        norm_weight[:, None],
        filled.astype(jnp.float32)[None, :],
    ).reshape(1, 1, slots, inner)
    later_mask = jnp.arange(seq_count)[None, :] > jnp.arange(seq_count)[:, None]
    after = jnp.sum(jnp.where(later_mask[:, :, None], totals[None, :, :], 0.0), axis=1)
    piece = hdim // seq_count
    own_ends = lax.dynamic_slice_in_dim(ends, my_block * piece, piece, axis=2)
    share = jnp.sum(jnp.exp(after)[:, :, None, None] * own_ends, axis=0)
    moved = lax.all_to_all(share[None], "req", split_axis=1, concat_axis=0, tiled=True)
    pick = (prompt_group[:, None] == jnp.arange(moved.shape[0])[None, :]).astype(jnp.float32)
    final_states = jnp.einsum(
        "pg,gabc->pabc", pick, moved, precision=lax.Precision.HIGHEST
    )
    return (gated_out, final_states)


def solution(mesh):
    in_specs = (
        P("req", "seq", None, None),
        P("req", "seq"),
        P(),
        P(),
        P(),
        P(),
        P(),
        P(),
        P(),
        P(),
    )
    out_specs = (P("req", "seq", None, None), P(None, "req", "seq", None))
    return jax.shard_map(local, mesh=mesh, in_specs=in_specs, out_specs=out_specs, check_vma=False)
```

```python
import jax
import jax.numpy as jnp
from jax import lax
from jax.experimental import pallas as pl
from jax.experimental.pallas import tpu as pltpu
from jax.sharding import PartitionSpec as P

BLOCK = 256


def shifted(block, axis, distance):
    devices = range(lax.axis_size(axis))
    route = [(i - distance, i) for i in devices if i - distance in devices]
    return lax.ppermute(block, axis, route)


def conv_kernel(x_ref, edge_ref, w_ref, b_ref, o_ref):
    x = x_ref[...].astype(jnp.float32)
    edge = edge_ref[...].astype(jnp.float32)
    w = w_ref[...]
    b = b_ref[...]
    taps = w.shape[1]
    acc = b + w[:, taps - 1 : taps] * x
    for tap in range(taps - 1):
        acc = acc + w[:, tap : tap + 1] * pltpu.roll(x, taps - 1 - tap, 1)
    o_ref[...] = (acc * (0.5 + 0.5 * jnp.tanh(0.5 * acc))).astype(o_ref.dtype)
    head = x[:, :128]
    lane = lax.broadcasted_iota(jnp.int32, head.shape, 1)
    first = b + w[:, taps - 1 : taps] * head
    for tap in range(taps - 1):
        lag = taps - 1 - tap
        moved = pltpu.roll(head, lag, 1)
        for t in range(lag):
            moved = jnp.where(lane == t, edge[:, tap + t : tap + t + 1], moved)
        first = first + w[:, tap : tap + 1] * moved
    o_ref[:, :128] = (first * (0.5 + 0.5 * jnp.tanh(0.5 * first))).astype(o_ref.dtype)


def conv_silu(conv_t, edge_t, weight_t, bias_t, rows=768):
    feats, slots = conv_t.shape
    taps = weight_t.shape[1]
    return pl.pallas_call(
        conv_kernel,
        grid=(feats // rows,),
        in_specs=[
            pl.BlockSpec((rows, slots), lambda i: (i, 0)),
            pl.BlockSpec((rows, taps - 1), lambda i: (i, 0)),
            pl.BlockSpec((rows, taps), lambda i: (i, 0)),
            pl.BlockSpec((rows, 1), lambda i: (i, 0)),
        ],
        out_specs=pl.BlockSpec((rows, slots), lambda i: (i, 0)),
        out_shape=jax.ShapeDtypeStruct((feats, slots), jnp.bfloat16),
        cost_estimate=pl.CostEstimate(
            flops=feats * slots * 14, transcendentals=feats * slots, bytes_accessed=feats * slots * 4
        ),
    )(conv_t, edge_t, weight_t, bias_t)


def norm_kernel(y_ref, z_ref, w_ref, mask_ref, o_ref):
    z = z_ref[...].astype(jnp.float32)
    gated = y_ref[...] * (z * (0.5 + 0.5 * jnp.tanh(0.5 * z)))
    mean = jnp.sum(gated * gated, axis=0, keepdims=True) * (1.0 / gated.shape[0])
    normed = gated * lax.rsqrt(mean + 1e-05) * w_ref[...]
    normed = jnp.where(mask_ref[...] > 0.5, normed, 0.0)
    o_ref[...] = normed.T.astype(o_ref.dtype)


def gate_norm(y_t, z_t, weight, mask, cols=128):
    units, slots = y_t.shape
    return pl.pallas_call(
        norm_kernel,
        grid=(slots // cols,),
        in_specs=[
            pl.BlockSpec((units, cols), lambda i: (0, i)),
            pl.BlockSpec((units, cols), lambda i: (0, i)),
            pl.BlockSpec((units, 1), lambda i: (0, 0)),
            pl.BlockSpec((1, cols), lambda i: (0, i)),
        ],
        out_specs=pl.BlockSpec((cols, units), lambda i: (i, 0)),
        out_shape=jax.ShapeDtypeStruct((slots, units), jnp.bfloat16),
        cost_estimate=pl.CostEstimate(
            flops=units * slots * 12, transcendentals=units * slots, bytes_accessed=units * slots * 8
        ),
    )(y_t, z_t, weight, mask)


def block_step(state, pieces):
    inputs_x, b_rows, c_rows, step_dt, log_decay = pieces
    length = inputs_x.shape[0]
    heads = step_dt.shape[1]
    hdim = inputs_x.shape[1] // heads
    running = jnp.cumsum(log_decay, axis=0)
    gram = jnp.einsum("tn,un->tu", c_rows, b_rows, preferred_element_type=jnp.float32)
    later = jnp.arange(length)[:, None] >= jnp.arange(length)[None, :]
    spread = running.T[:, :, None] - running.T[:, None, :]
    decay = jnp.where(later[None], jnp.exp(jnp.where(later[None], spread, 0.0)), 0.0)
    mixing = (gram[None] * decay * step_dt.T[:, None, :]).astype(jnp.bfloat16)
    heads_x = inputs_x.reshape(length, heads, hdim)
    inside = jnp.einsum("htu,uhp->thp", mixing, heads_x, preferred_element_type=jnp.float32)
    carried = jnp.exp(running)[:, :, None] * jnp.einsum(
        "tn,hpn->thp", c_rows.astype(jnp.float32), state, precision=lax.Precision.HIGHEST
    )
    final_log = running[-1]
    weighting = jnp.exp(final_log[None, :] - running) * step_dt
    weighted = (
        (heads_x.astype(jnp.float32) * weighting[:, :, None])
        .astype(jnp.bfloat16)
        .reshape(length, heads * hdim)
    )
    contrib = jnp.einsum("ud,un->dn", weighted, b_rows, preferred_element_type=jnp.float32).reshape(
        heads, hdim, -1
    )
    new_state = jnp.exp(final_log)[:, None, None] * state + contrib
    return (new_state, (inside + carried).reshape(length, heads * hdim))


def local(
    hidden, w_in, conv_weight, conv_bias, dt_bias, a_log, d_skip, norm_weight, lengths, prompt_group
):
    tok_rows = hidden[0, 0]
    slots = tok_rows.shape[0]
    inner = norm_weight.shape[0]
    heads = dt_bias.shape[0]
    hdim = inner // heads
    nstate = (conv_bias.shape[0] - inner) // 2
    convdim = conv_bias.shape[0]
    taps = conv_weight.shape[0]
    seq_count = lax.axis_size("seq")
    my_group = lax.axis_index("req")
    my_block = lax.axis_index("seq")
    qlen = jnp.sum(jnp.where(prompt_group == my_group, lengths, 0))
    filled = jnp.arange(slots, dtype=jnp.int32) < qlen
    column_blocks = [w_in]
    for distance in range(1, seq_count):
        cycle = [(i, (i + distance) % seq_count) for i in range(seq_count)]
        column_blocks.append(lax.ppermute(w_in, "seq", cycle))
    by_distance = jnp.stack(column_blocks)
    from_block = (my_block - jnp.arange(seq_count)) % seq_count
    in_order = jnp.take(by_distance, from_block, axis=0)
    wide_rows = jnp.transpose(in_order, (1, 0, 2)).reshape(w_in.shape[0], -1)
    projected = jnp.dot(
        tok_rows,
        lax.all_gather(wide_rows, "req", axis=0, tiled=True),
        preferred_element_type=jnp.float32,
    ).astype(jnp.bfloat16)
    gate_z = projected[:, :inner]
    conv_in = projected[:, inner : inner + convdim]
    dt_raw = projected[:, inner + convdim :]
    edge_rows = lax.dynamic_slice_in_dim(conv_in, qlen - (taps - 1), taps - 1, 0)
    prev_edge = shifted(edge_rows, "seq", 1)
    conv_act = conv_silu(conv_in.T, prev_edge.T, conv_weight.T, conv_bias[:, None]).T
    inputs_x = conv_act[:, :inner]
    b_rows = conv_act[:, inner : inner + nstate]
    c_rows = conv_act[:, inner + nstate :]
    step_dt = jnp.where(
        filled[:, None], jax.nn.softplus(dt_raw.astype(jnp.float32) + dt_bias[None, :]), 0.0
    )
    log_decay = step_dt * (-jnp.exp(a_log))[None, :]
    through = jnp.cumsum(log_decay, axis=0)
    block_total = through[-1]
    block_rows = min(BLOCK, slots)
    count = slots // block_rows
    pieces = (
        inputs_x.reshape(count, block_rows, inner),
        b_rows.reshape(count, block_rows, nstate),
        c_rows.reshape(count, block_rows, nstate),
        step_dt.reshape(count, block_rows, heads),
        log_decay.reshape(count, block_rows, heads),
    )
    zero_state = jnp.zeros((heads, hdim, nstate), jnp.float32)
    local_end = zero_state
    outs = []
    for index in range(count):
        local_end, out = block_step(local_end, tuple(piece[index] for piece in pieces))
        outs.append(out)
    outputs = jnp.concatenate(outs, axis=0)
    total_hi = lax.reduce_precision(block_total, exponent_bits=8, mantissa_bits=7)
    total_rest = block_total - total_hi
    total_mid = lax.reduce_precision(total_rest, exponent_bits=8, mantissa_bits=7)
    total_lo = total_rest - total_mid
    parts = jnp.stack([total_hi, total_mid, total_lo], axis=1).astype(jnp.bfloat16)
    parts = jnp.pad(parts, ((0, 0), (0, 128 - 3)))
    packed = jnp.concatenate(
        [local_end.reshape(heads, hdim * nstate).astype(jnp.bfloat16), parts],
        axis=1,
    )
    gathered = lax.all_gather(packed, "seq", axis=0, tiled=False)
    ends = gathered[:, :, : hdim * nstate].astype(jnp.float32).reshape(seq_count, heads, hdim, nstate)
    sent = gathered[:, :, hdim * nstate :].astype(jnp.float32)
    totals = sent[:, :, 0] + (sent[:, :, 1] + sent[:, :, 2])
    entering = zero_state
    for turn in range(seq_count - 1):
        stepped = jnp.exp(totals[turn])[:, None, None] * entering + ends[turn]
        entering = jnp.where(turn < my_block, stepped, entering)
    incoming = jnp.exp(through)[:, :, None] * jnp.einsum(
        "tn,hpn->thp", c_rows.astype(jnp.float32), entering, precision=lax.Precision.HIGHEST
    )
    heads_y = (
        outputs.reshape(slots, heads, hdim)
        + incoming
        + d_skip[None, :, None] * inputs_x.astype(jnp.float32).reshape(slots, heads, hdim)
    )
    gated_out = gate_norm(
        heads_y.reshape(slots, inner).T,
        gate_z.T,
        norm_weight[:, None],
        filled.astype(jnp.float32)[None, :],
    ).reshape(1, 1, slots, inner)
    later_mask = jnp.arange(seq_count)[None, :] > jnp.arange(seq_count)[:, None]
    after = jnp.sum(jnp.where(later_mask[:, :, None], totals[None, :, :], 0.0), axis=1)
    piece = hdim // seq_count
    own_ends = lax.dynamic_slice_in_dim(ends, my_block * piece, piece, axis=2)
    share = jnp.sum(jnp.exp(after)[:, :, None, None] * own_ends, axis=0)
    moved = lax.all_to_all(share[None], "req", split_axis=1, concat_axis=0, tiled=True)
    pick = (prompt_group[:, None] == jnp.arange(moved.shape[0])[None, :]).astype(jnp.float32)
    final_states = jnp.einsum(
        "pg,gabc->pabc", pick, moved, precision=lax.Precision.HIGHEST
    )
    return (gated_out, final_states)


def solution(mesh):
    in_specs = (
        P("req", "seq", None, None),
        P("req", "seq"),
        P(),
        P(),
        P(),
        P(),
        P(),
        P(),
        P(),
        P(),
    )
    out_specs = (P("req", "seq", None, None), P(None, "req", "seq", None))
    return jax.shard_map(local, mesh=mesh, in_specs=in_specs, out_specs=out_specs, check_vma=False)
```
